128 devices in a mesh: group: 16 (over x, z), mp: 8 (over y, core).
Axes of the slice: x: 4, y: 4, z: 4, core: 2. Of those that a mesh axis runs over, the one named last changes fastest.
Arguments:
- stream: bfloat16 [8192, 3584], P('group', 'mp'), may hold values from -6 to 6
- prenorm_gain: float32 [3584], replicated, may hold values from 0.25 to 12
- query_weight: bfloat16 [3584, 4096], P(None, 'mp'), may hold values from -0.09375 to 0.09375
- key_weight: bfloat16 [3584, 2048], P(None, 'mp'), may hold values from -0.09375 to 0.09375
- value_weight: bfloat16 [3584, 2048], P(None, 'mp'), may hold values from -0.09375 to 0.09375
- output_weight: bfloat16 [4096, 3584], P('mp'), may hold values from -0.09375 to 0.09375
- adapter_down_rows: bfloat16 [64, 16, 3584], P('group', None, 'mp'), may hold values from -0.09375 to 0.09375
- adapter_up_query: bfloat16 [64, 16, 4096], P('group', None, 'mp'), may hold values from -1.5 to 1.5
- request_adapter: int32 [16, 4], replicated, may hold values from 0 to 63
- adapter_row_index: int32 [64], replicated, may hold values from 0 to 63, each once
- request_token_length: int32 [16, 4], replicated, may hold values from 1 to 256, 512 in all within a row
- continues_previous: int32 [16], replicated, may hold values from 0 to 1, as said below
- request_cache_block: int32 [16, 4], replicated, may hold values from 0 to 31, as said below
- cached_length: int32 [16, 4], replicated, may hold values from 1 to 256
- cached_rotated_keys: bfloat16 [32, 256, 2048], P('group', None, 'mp'), may hold values from -6 to 6
- cached_value_rows: bfloat16 [32, 256, 2048], P('group', None, 'mp'), may hold values from -6 to 6
Outputs:
- attn_out: bfloat16 [8192, 3584], P('group', 'mp')
The draws below stay inside these ranges and needn't reach their ends.
Inputs may be any that keep to these rules, and one draw needn't show every extreme that they name: `continues_previous`: the first group has 0; some group has 1. `request_cache_block`: the owner of block b is group b // 2; blocks may be shared by requests.
All inputs are finite; a program needn't handle non-finite values.
Results may differ from the reference program's by a relative error of at most 0.017.
The reference program's roundings to bfloat16 on the way count: a program that leaves them out, or rounds other values in their place, can miss the bound.
Values may be sent and summed in bfloat16 or wider, within the bound.
No kernel may reach another device: no remote copies, remote signals or barrier semaphores. Data moves between devices by JAX's collectives and lax.ppermute only.
A program may use at most 128 MiB of HBM per device.

```python
import math
import jax
import jax.numpy as jnp
import numpy as np
from jax import lax

MODEL_WIDTH = 3584
QUERY_HEADS = 16
KEY_VALUE_HEADS = 8
HEAD_WIDTH = 256
ADAPTER_RANK = 16
REQS = 4
BLOCK_POSITIONS = 256
TOK_DEV = 512
MOSTLEN = 256
NGROUPS = 16
ADAPTER_TOTAL = 64
CACHE_BLOCK_TOTAL = 32
TOKENS = 8192


def draw_prenorm_gain(key, part):
    gain = jnp.exp(jax.random.uniform(key, (MODEL_WIDTH,), jnp.float32, jnp.log(0.25), jnp.log(4.0)))
    return gain


def draw_continues_previous(key, part):
    flags = jax.random.randint(key, (NGROUPS,), 0, 2).astype(jnp.int32)
    return flags.at[0].set(0).at[1].set(1)


def draw_request_cache_block(key, part):
    blocks = jax.random.randint(key, (NGROUPS, REQS), 0, CACHE_BLOCK_TOTAL).astype(jnp.int32)
    return blocks.at[0, 0].set(0).at[NGROUPS - 1, REQS - 1].set(CACHE_BLOCK_TOTAL - 1)


def draw_cached_length(key, part):
    spans = jax.random.randint(key, (NGROUPS, REQS), 1, BLOCK_POSITIONS + 1).astype(jnp.int32)
    return spans.at[0, REQS - 1].set(BLOCK_POSITIONS)


def plant(values, key, least, largest):
    dims = values.shape
    spot = [jax.random.randint(jax.random.fold_in(key, axis), (), 0, dims[axis]) for axis in range(len(dims))]
    values = values.at[tuple(spot)].set(least)
    longest = dims.index(max(dims))
    spot[longest] = (spot[longest] + 1) % dims[longest]
    return values.at[tuple(spot)].set(largest)


def block_scale(own_key, extent, pieces, low, high):
    loudness, own = 1.0, jax.random.fold_in(own_key, 6)
    for dim, blocks in pieces:
        steps = jnp.exp(jax.random.uniform(jax.random.fold_in(own, dim), (blocks,), jnp.float32, low / len(pieces), high / len(pieces)))
        loudness = loudness * jnp.repeat(steps, extent[dim] // blocks).reshape([-1 if axis == dim else 1 for axis in range(len(extent))])
    return loudness


def profile(count, total, most, lean):
    loads = [(1 << 20) // math.isqrt(standing ** lean) + 1 for standing in range(2, count + 1)]
    spare, holding = total - most - (count - 1), [1] * (count - 1)
    while spare > 0:
        candidates = [i for i in range(count - 1) if holding[i] < most]
        pool, left = sum([loads[i] for i in candidates]), spare
        for i in candidates:
            more = min(most - holding[i], max(1, left * loads[i] // pool), spare)
            holding[i] = holding[i] + more
            spare = spare - more
    return np.array([most] + holding)


def ragged_sizes(key, amount, total, bound, slope):
    if amount == 2:
        one = jax.random.randint(key, (), max(1, total - bound), min(bound, total - 1) + 1)
        return jnp.stack([one, total - one])
    sizes = jnp.asarray(profile(amount, total, bound, slope), jnp.int32)
    couples = (amount - 1) // 2
    giver, taker = sizes[1:1 + 2 * couples:2], sizes[2:2 + 2 * couples:2]
    room = jnp.minimum(giver - 1, bound - taker)
    moved = jax.random.randint(jax.random.fold_in(key, 1), (couples,), 0, 1 << 20) % (room + 1)
    sizes = sizes.at[1:1 + 2 * couples:2].set(giver - moved).at[2:2 + 2 * couples:2].set(taker + moved)
    return sizes[jax.random.permutation(jax.random.fold_in(key, 2), amount)]


def scatter_about(stream_key, shape, scale, most, cuts=(), kind=jnp.bfloat16):
    values = jax.random.normal(stream_key, shape, jnp.float32) * scale
    if len(cuts) > 0:
        values = block_scale(stream_key, shape, cuts, -0.22, 0.18) * values
    return jnp.clip(values, min=-most, max=most).astype(kind)


def setup_inputs(seed: int = 0) -> dict:
    seeds = jax.random.split(jax.random.key(seed), 17)
    stream = scatter_about(seeds[0], (TOKENS, MODEL_WIDTH), 1.0, 6.0, ((0, 16), (1, 8)))
    prenorm_gain = draw_prenorm_gain(jax.random.fold_in(seeds[16], 71), 0)
    query_weight = scatter_about(seeds[2], (MODEL_WIDTH, QUERY_HEADS * HEAD_WIDTH), MODEL_WIDTH ** -0.5, 0.09375, ((1, 8),))
    key_weight = scatter_about(seeds[3], (MODEL_WIDTH, KEY_VALUE_HEADS * HEAD_WIDTH), MODEL_WIDTH ** -0.5, 0.09375, ((1, 8),))
    value_weight = scatter_about(seeds[4], (MODEL_WIDTH, KEY_VALUE_HEADS * HEAD_WIDTH), MODEL_WIDTH ** -0.5, 0.09375, ((1, 8),))
    output_weight = scatter_about(seeds[5], (QUERY_HEADS * HEAD_WIDTH, MODEL_WIDTH), (QUERY_HEADS * HEAD_WIDTH) ** -0.5, 0.09375, ((0, 8),))
    adapter_down_rows = scatter_about(seeds[6], (ADAPTER_TOTAL, ADAPTER_RANK, MODEL_WIDTH), MODEL_WIDTH ** -0.5, 0.09375, ((0, 16), (2, 8)))
    adapter_up_query = scatter_about(seeds[7], (ADAPTER_TOTAL, ADAPTER_RANK, QUERY_HEADS * HEAD_WIDTH), ADAPTER_RANK ** -0.5, 1.5, ((0, 16), (2, 8)))
    request_adapter = plant(jax.random.randint(seeds[8], (NGROUPS, REQS), 0, ADAPTER_TOTAL), jax.random.fold_in(seeds[8], 1), 0, ADAPTER_TOTAL - 1).astype(jnp.int32)
    adapter_row_index = jax.random.permutation(seeds[9], ADAPTER_TOTAL).astype(jnp.int32)
    request_token_length = jax.vmap(lambda own: ragged_sizes(own, REQS, TOK_DEV, MOSTLEN, 2))(jax.random.split(seeds[10], NGROUPS)).reshape((NGROUPS, REQS)).astype(jnp.int32)
    continues_previous = draw_continues_previous(jax.random.fold_in(seeds[16], 71), 0)
    request_cache_block = draw_request_cache_block(jax.random.fold_in(seeds[16], 71), 0)
    cached_length = draw_cached_length(jax.random.fold_in(seeds[16], 71), 0)
    cached_rotated_keys = scatter_about(seeds[14], (CACHE_BLOCK_TOTAL, BLOCK_POSITIONS, KEY_VALUE_HEADS * HEAD_WIDTH), 1.0, 6.0, ((0, 16), (2, 8)))
    cached_value_rows = scatter_about(seeds[15], (CACHE_BLOCK_TOTAL, BLOCK_POSITIONS, KEY_VALUE_HEADS * HEAD_WIDTH), 1.0, 6.0, ((0, 16), (2, 8)))
    return {"stream": stream, "prenorm_gain": prenorm_gain, "query_weight": query_weight, "key_weight": key_weight, "value_weight": value_weight, "output_weight": output_weight, "adapter_down_rows": adapter_down_rows, "adapter_up_query": adapter_up_query, "request_adapter": request_adapter, "adapter_row_index": adapter_row_index, "request_token_length": request_token_length, "continues_previous": continues_previous, "request_cache_block": request_cache_block, "cached_length": cached_length, "cached_rotated_keys": cached_rotated_keys, "cached_value_rows": cached_value_rows}


adapter_scale = 2.0

def rotate(values, position, head_size):
    count = values.shape[0]
    shaped = values.reshape(count, -1, head_size)
    half = head_size // 2
    freq = 10000.0 ** (-jnp.arange(half, dtype=jnp.float32) / half)
    angle = position[:, None, None] * freq[None, None, :]
    cosine = jnp.cos(angle)
    sine = jnp.sin(angle)
    first = shaped[..., :half]
    second = shaped[..., half:]
    turned = jnp.concatenate([first * cosine - second * sine, second * cosine + first * sine], axis=-1)
    return turned.reshape(count, -1)

def layout(lengths, cached, split_flag, prev_len, count):
    ends = jnp.cumsum(lengths).astype(jnp.int32)
    starts = (ends - lengths).astype(jnp.int32)
    place = jnp.arange(count, dtype=jnp.int32)
    member = ((place[:, None] >= starts[None, :]) & (place[:, None] < ends[None, :])).astype(jnp.int32)
    request = lax.optimization_barrier(jnp.sum(member * jnp.arange(lengths.shape[0], dtype=jnp.int32)[None, :], axis=1)).astype(jnp.int32)
    offset = place - lax.optimization_barrier(jnp.sum(member * starts[None, :], axis=1)).astype(jnp.int32)
    extra = jnp.where(request == 0, split_flag * prev_len, 0).astype(jnp.int32)
    position = lax.optimization_barrier(jnp.sum(member * cached[None, :], axis=1)).astype(jnp.int32) + extra + offset
    return (member, request, position.astype(jnp.float32))

def attend(query_vectors, keys, values, prev_keys, prev_values, cache_keys, cache_values, request, cached, split_flag, prev_len, head_size):
    count = query_vectors.shape[0]
    kv_heads = keys.shape[1] // head_size
    ratio = query_vectors.shape[1] // keys.shape[1]
    block = cache_keys.shape[1]
    slots = cache_keys.shape[0] * block
    every_key = jnp.concatenate([cache_keys.reshape(slots, -1), prev_keys, keys], 0).reshape(-1, kv_heads, head_size)
    every_value = jnp.concatenate([cache_values.reshape(slots, -1), prev_values, values], 0).reshape(-1, kv_heads, head_size)
    slot_req = (jnp.arange(slots, dtype=jnp.int32) // block).astype(jnp.int32)
    slot_col = (jnp.arange(slots, dtype=jnp.int32) % block).astype(jnp.int32)
    cache_ok = (request[:, None] == slot_req[None, :]) & (slot_col[None, :] < cached[slot_req][None, :])
    place = jnp.arange(count, dtype=jnp.int32)
    prev_ok = (split_flag == 1) & (request[:, None] == 0) & (place[None, :] >= count - prev_len)
    own_ok = (request[:, None] == request[None, :]) & (place[None, :] <= place[:, None])
    allowed = jnp.concatenate([cache_ok, prev_ok, own_ok], 1)
    grouped = query_vectors.reshape(count, kv_heads, ratio, head_size)
    scores = jnp.einsum('tkrd,skd->krts', grouped.astype(jnp.float32), every_key.astype(jnp.float32)) * head_size ** (-0.5)
    scores = jnp.where(allowed[None, None], scores, jnp.float32(-1e+30))
    top = lax.optimization_barrier(jnp.max(scores, axis=-1, keepdims=True))
    weights = jnp.exp(scores - top)
    total = lax.optimization_barrier(jnp.sum(weights, axis=-1))
    rounded = weights.astype(jnp.bfloat16).astype(jnp.float32)
    numer = jnp.einsum('krts,skd->tkrd', rounded, every_value.astype(jnp.float32))
    result = numer / jnp.transpose(total, (2, 0, 1))[..., None]
    return result.reshape(count, -1).astype(jnp.bfloat16)

def reference(stream, prenorm_gain, query_weight, key_weight, value_weight, output_weight, adapter_down_rows, adapter_up_query, request_adapter, adapter_row_index, request_token_length, continues_previous, request_cache_block, cached_length, cached_rotated_keys, cached_value_rows):
    wide = stream.astype(jnp.float32)
    normalized_input = (wide * lax.rsqrt(lax.optimization_barrier(jnp.mean(wide * wide, axis=1, keepdims=True)) + 1e-06) * prenorm_gain.astype(jnp.float32)).astype(jnp.bfloat16)
    prev_lens = jnp.concatenate([jnp.zeros((1,), jnp.int32), request_token_length[:-1, -1].astype(jnp.int32)])
    members, requests, positions = jax.vmap(lambda lengths, cached, flag, before: layout(lengths, cached, flag, before, TOK_DEV))(request_token_length, cached_length, continues_previous, prev_lens)
    position = positions.reshape(-1)
    ids_tok = jnp.take_along_axis(request_adapter, requests, axis=1).reshape(-1)
    rows = adapter_row_index[ids_tok]
    select = (rows[:, None] == jnp.arange(ADAPTER_TOTAL, dtype=jnp.int32)[None, :]).astype(jnp.float32)
    all_low_rank = jnp.einsum('vx,nhx->vnh', normalized_input.astype(jnp.float32), adapter_down_rows.astype(jnp.float32))
    low = lax.optimization_barrier(jnp.sum(select[:, :, None] * all_low_rank, axis=1)).astype(jnp.bfloat16)
    token_spread = select[:, :, None] * low.astype(jnp.float32)[:, None, :]
    query_update = jnp.einsum('jqz,qzs->js', token_spread, adapter_up_query.astype(jnp.float32))
    query_vectors = jnp.dot(normalized_input, query_weight, preferred_element_type=jnp.float32) + adapter_scale * query_update
    query_vectors = rotate(query_vectors, position, HEAD_WIDTH).astype(jnp.bfloat16)
    keys = rotate(jnp.dot(normalized_input, key_weight, preferred_element_type=jnp.float32), position, HEAD_WIDTH).astype(jnp.bfloat16)
    values = jnp.dot(normalized_input, value_weight, preferred_element_type=jnp.float32).astype(jnp.bfloat16)

    def one_group(index):
        before = jnp.maximum(index - 1, 0)
        start = (index * TOK_DEV).astype(jnp.int32)
        start_prev = (before * TOK_DEV).astype(jnp.int32)
        q_rows = lax.dynamic_slice_in_dim(query_vectors, start, TOK_DEV, 0)
        k_rows = lax.dynamic_slice_in_dim(keys, start, TOK_DEV, 0)
        v_rows = lax.dynamic_slice_in_dim(values, start, TOK_DEV, 0)
        k_prev = lax.dynamic_slice_in_dim(keys, start_prev, TOK_DEV, 0)
        v_prev = lax.dynamic_slice_in_dim(values, start_prev, TOK_DEV, 0)
        blocks = request_cache_block[index]
        return attend(q_rows, k_rows, v_rows, k_prev, v_prev, cached_rotated_keys[blocks], cached_value_rows[blocks], requests[index], cached_length[index], continues_previous[index], prev_lens[index], HEAD_WIDTH)
    attended = lax.map(one_group, jnp.arange(NGROUPS, dtype=jnp.int32)).reshape(TOKENS, -1)
    return jnp.dot(attended, output_weight, preferred_element_type=jnp.float32).astype(jnp.bfloat16)
```

```python
import jax
import jax.numpy as jnp
from jax import lax
from jax.sharding import Mesh, PartitionSpec as P

HEAD_WIDTH = 256
REQS = 4


adapter_scale = 2.0


def shifted(value, axis, steps):
    count = lax.axis_size(axis)
    first, last = (max(0, -steps), min(count, count - steps))
    return lax.ppermute(value, axis, [(source, source + steps) for source in range(first, last)])


def rotate(values, position, head_size):
    count = values.shape[0]
    shaped = values.reshape(count, -1, head_size)
    half = head_size // 2
    freq = 10000.0 ** (-jnp.arange(half, dtype=jnp.float32) / half)
    angle = position[:, None, None] * freq[None, None, :]
    cosine = jnp.cos(angle)
    sine = jnp.sin(angle)
    first = shaped[..., :half]
    second = shaped[..., half:]
    turned = jnp.concatenate(
        [first * cosine - second * sine, second * cosine + first * sine], axis=-1
    )
    return turned.reshape(count, -1)


def layout(lengths, cached, split_flag, prev_len, count):
    ends = jnp.cumsum(lengths)
    starts = ends - lengths
    place = jnp.arange(count, dtype=jnp.int32)
    member = ((place[:, None] >= starts[None, :]) & (place[:, None] < ends[None, :])).astype(
        jnp.int32
    )
    request = jnp.sum(member * jnp.arange(lengths.shape[0], dtype=jnp.int32)[None, :], axis=1)
    offset = place - jnp.sum(member * starts[None, :], axis=1)
    extra = jnp.where(request == 0, split_flag * prev_len, 0)
    position = jnp.sum(member * cached[None, :], axis=1) + extra + offset
    return (member, request, position.astype(jnp.float32))


def attend(
    query_vectors,
    keys,
    values,
    prev_keys,
    prev_values,
    cache_keys,
    cache_values,
    request,
    cached,
    split_flag,
    prev_len,
    head_size,
):
    count = query_vectors.shape[0]
    kv_heads = keys.shape[1] // head_size
    ratio = query_vectors.shape[1] // keys.shape[1]
    block = cache_keys.shape[1]
    slots = cache_keys.shape[0] * block
    every_key = jnp.concatenate([cache_keys.reshape(slots, -1), prev_keys, keys], 0).reshape(
        -1, kv_heads, head_size
    )
    every_value = jnp.concatenate(
        [cache_values.reshape(slots, -1), prev_values, values], 0
    ).reshape(-1, kv_heads, head_size)
    slot_req = jnp.arange(slots, dtype=jnp.int32) // block
    slot_col = jnp.arange(slots, dtype=jnp.int32) % block
    cache_ok = (request[:, None] == slot_req[None, :]) & (
        slot_col[None, :] < cached[slot_req][None, :]
    )
    place = jnp.arange(count, dtype=jnp.int32)
    prev_ok = (split_flag == 1) & (request[:, None] == 0) & (place[None, :] >= count - prev_len)
    own_ok = (request[:, None] == request[None, :]) & (place[None, :] <= place[:, None])
    allowed = jnp.concatenate([cache_ok, prev_ok, own_ok], 1)
    grouped = query_vectors.reshape(count, kv_heads, ratio, head_size)
    scores = jnp.einsum(
        "tkrd,skd->krts", grouped, every_key, preferred_element_type=jnp.float32
    ) * head_size ** (-0.5)
    scores = jnp.where(allowed[None, None], scores, jnp.float32(-1e30))
    top = jnp.max(scores, axis=-1, keepdims=True)
    weights = jnp.exp(scores - top)
    total = jnp.sum(weights, axis=-1)
    numer = jnp.einsum(
        "krts,skd->tkrd",
        weights.astype(jnp.bfloat16),
        every_value,
        preferred_element_type=jnp.float32,
    )
    result = numer / jnp.transpose(total, (2, 0, 1))[..., None]
    return result.reshape(count, -1).astype(jnp.bfloat16)


SIDE = 4


def ring_gather(value, axis):
    held = [value]
    for step in range(1, SIDE):
        held.append(lax.ppermute(value, axis, [(i, (i + step) % SIDE) for i in range(SIDE)]))
    return jnp.stack(held)


def group_of(first, a_coord, b_coord):
    return b_coord * SIDE + a_coord if first == "gz" else a_coord * SIDE + b_coord


def route(local, wanted, first, second):
    per_owner = local.shape[0]
    coords = {"gx": lax.axis_index("gx"), "gz": lax.axis_index("gz")}
    own_a, own_b = coords[first], coords[second]
    owner = wanted // per_owner
    owner_coords = {"gx": owner // SIDE, "gz": owner % SIDE}
    owner_a, owner_b = owner_coords[first], owner_coords[second]
    part = wanted % per_owner
    held = ring_gather(local, first).reshape(SIDE * per_owner, *local.shape[1:])

    def pick(requester_b):
        asker = group_of(first, own_a, requester_b)
        shift = (own_a - owner_a[asker]) % SIDE
        return held[shift * per_owner + part[asker]]

    received = [pick(own_b)]
    for step in range(1, SIDE):
        payload = pick((own_b + step) % SIDE)
        received.append(
            lax.ppermute(payload, second, [(i, (i + step) % SIDE) for i in range(SIDE)])
        )
    stacked = jnp.stack(received)
    me = group_of(first, own_a, own_b)
    came_from = (own_b - owner_b[me]) % SIDE
    return stacked[came_from, jnp.arange(wanted.shape[1])]


def gather_model(value, axis):
    count = 8
    model_at = lax.axis_index(("my", "mc"))
    held = [value]
    for step in range(1, count):
        held.append(
            lax.ppermute(value, ("my", "mc"), [(i, (i + step) % count) for i in range(count)])
        )
    held = jnp.stack(held)
    ordered = held[(model_at - jnp.arange(count)) % count]
    moved = jnp.moveaxis(ordered, 0, axis)
    shape = list(value.shape)
    shape[axis] = shape[axis] * count
    return moved.reshape(shape)


def on_device(
    stream,
    prenorm_gain,
    query_weight,
    key_weight,
    value_weight,
    output_weight,
    adapter_down_rows,
    adapter_up_query,
    request_adapter,
    adapter_row_index,
    request_token_length,
    continues_previous,
    request_cache_block,
    cached_length,
    cached_rotated_keys,
    cached_value_rows,
):
    count = stream.shape[0]
    group_at = lax.axis_index(("gx", "gz"))
    wanted = adapter_row_index[request_adapter]
    down_width = adapter_down_rows.shape[2]
    adapters = jnp.concatenate([adapter_down_rows, adapter_up_query], axis=2)
    chosen = route(adapters, wanted, "gz", "gx")
    chosen_down = chosen[:, :, :down_width]
    chosen_up = chosen[:, :, down_width:]
    cache_keys = route(cached_rotated_keys, request_cache_block, "gz", "gx")
    cache_values = route(cached_value_rows, request_cache_block, "gx", "gz")
    full_down = gather_model(chosen_down, 2)

    whole = lax.all_gather(stream, ("my", "mc"), axis=1, tiled=True)
    wide = whole.astype(jnp.float32)
    normalized_input = (
        wide * lax.rsqrt(jnp.mean(wide * wide, axis=1, keepdims=True) + 1e-06) * prenorm_gain
    ).astype(jnp.bfloat16)
    before = jnp.maximum(group_at - 1, 0)
    lengths = request_token_length[group_at]
    cached = cached_length[group_at]
    split_flag = continues_previous[group_at]
    prev_len = request_token_length[before, REQS - 1]
    member, request, position = layout(lengths, cached, split_flag, prev_len, count)
    rank_index = adapter_down_rows.shape[1]
    low = jnp.einsum(
        "td,rkd->trk", normalized_input, full_down, preferred_element_type=jnp.float32
    ).reshape(count, REQS * rank_index).astype(jnp.bfloat16)
    own_columns = jnp.repeat(member, rank_index, axis=1).astype(jnp.bfloat16)
    query_update = jnp.dot(
        low * own_columns,
        chosen_up.reshape(REQS * rank_index, -1),
        preferred_element_type=jnp.float32,
    )
    query_vectors = (
        jnp.dot(normalized_input, query_weight, preferred_element_type=jnp.float32)
        + adapter_scale * query_update
    )
    query_vectors = rotate(query_vectors, position, HEAD_WIDTH).astype(jnp.bfloat16)
    keys = rotate(
        jnp.dot(normalized_input, key_weight, preferred_element_type=jnp.float32),
        position,
        HEAD_WIDTH,
    ).astype(jnp.bfloat16)
    values = jnp.dot(normalized_input, value_weight, preferred_element_type=jnp.float32).astype(
        jnp.bfloat16
    )
    prev_keys, prev_values = shifted((keys, values), ("gx", "gz"), 1)
    attended = attend(
        query_vectors,
        keys,
        values,
        prev_keys,
        prev_values,
        cache_keys,
        cache_values,
        request,
        cached,
        split_flag,
        prev_len,
        HEAD_WIDTH,
    )
    partial_out = jnp.dot(attended, output_weight, preferred_element_type=jnp.float32)
    return lax.psum_scatter(
        partial_out.astype(jnp.bfloat16), ("my", "mc"), scatter_dimension=1, tiled=True
    )


def solution(mesh):
    split = Mesh(mesh.devices.reshape(SIDE, SIDE, 4, 2), ("gx", "gz", "my", "mc"))
    groups = ("gx", "gz")
    model = ("my", "mc")
    placed = (
        P(groups, model),
        P(),
        P(None, model),
        P(None, model),
        P(None, model),
        P(model, None),
        P(groups, None, model),
        P(groups, None, model),
        P(),
        P(),
        P(),
        P(),
        P(),
        P(),
        P(groups, None, model),
        P(groups, None, model),
    )
    return jax.shard_map(
        on_device, mesh=split, in_specs=placed, out_specs=P(groups, model), check_vma=False
    )
```

```python
import jax
import jax.numpy as jnp
from jax import lax
from jax.sharding import Mesh, PartitionSpec as P

HEAD_WIDTH = 256
REQS = 4


adapter_scale = 2.0


def shifted(value, axis, steps):
    count = lax.axis_size(axis)
    first, last = (max(0, -steps), min(count, count - steps))
    return lax.ppermute(value, axis, [(source, source + steps) for source in range(first, last)])


def rotate(values, position, head_size):
    count = values.shape[0]
    shaped = values.reshape(count, -1, head_size)
    half = head_size // 2
    freq = 10000.0 ** (-jnp.arange(half, dtype=jnp.float32) / half)
    angle = position[:, None, None] * freq[None, None, :]
    cosine = jnp.cos(angle)
    sine = jnp.sin(angle)
    first = shaped[..., :half]
    second = shaped[..., half:]
    turned = jnp.concatenate(
        [first * cosine - second * sine, second * cosine + first * sine], axis=-1
    )
    return turned.reshape(count, -1)


def layout(lengths, cached, split_flag, prev_len, count):
    ends = jnp.cumsum(lengths)
    starts = ends - lengths
    place = jnp.arange(count, dtype=jnp.int32)
    member = ((place[:, None] >= starts[None, :]) & (place[:, None] < ends[None, :])).astype(
        jnp.int32
    )
    request = jnp.sum(member * jnp.arange(lengths.shape[0], dtype=jnp.int32)[None, :], axis=1)
    offset = place - jnp.sum(member * starts[None, :], axis=1)
    extra = jnp.where(request == 0, split_flag * prev_len, 0)
    position = jnp.sum(member * cached[None, :], axis=1) + extra + offset
    return (member, request, position.astype(jnp.float32))


def attend(
    query_vectors,
    keys,
    values,
    prev_keys,
    prev_values,
    cache_keys,
    cache_values,
    request,
    cached,
    split_flag,
    prev_len,
    head_size,
):
    count = query_vectors.shape[0]
    kv_heads = keys.shape[1] // head_size
    ratio = query_vectors.shape[1] // keys.shape[1]
    block = cache_keys.shape[1]
    slots = cache_keys.shape[0] * block
    every_key = jnp.concatenate([cache_keys.reshape(slots, -1), prev_keys, keys], 0).reshape(
        -1, kv_heads, head_size
    )
    every_value = jnp.concatenate(
        [cache_values.reshape(slots, -1), prev_values, values], 0
    ).reshape(-1, kv_heads, head_size)
    slot_req = jnp.arange(slots, dtype=jnp.int32) // block
    slot_col = jnp.arange(slots, dtype=jnp.int32) % block
    cache_ok = (request[:, None] == slot_req[None, :]) & (
        slot_col[None, :] < cached[slot_req][None, :]
    )
    place = jnp.arange(count, dtype=jnp.int32)
    prev_ok = (split_flag == 1) & (request[:, None] == 0) & (place[None, :] >= count - prev_len)
    own_ok = (request[:, None] == request[None, :]) & (place[None, :] <= place[:, None])
    allowed = jnp.concatenate([cache_ok, prev_ok, own_ok], 1)
    grouped = query_vectors.reshape(count, kv_heads, ratio, head_size)
    scores = jnp.einsum(
        "tkrd,skd->krts", grouped, every_key, preferred_element_type=jnp.float32
    ) * head_size ** (-0.5)
    scores = jnp.where(allowed[None, None], scores, jnp.float32(-1e30))
    top = jnp.max(scores, axis=-1, keepdims=True)
    weights = jnp.exp(scores - top)
    total = jnp.sum(weights, axis=-1)
    numer = jnp.einsum(
        "krts,skd->tkrd",
        weights.astype(jnp.bfloat16),
        every_value,
        preferred_element_type=jnp.float32,
    )
    result = numer / jnp.transpose(total, (2, 0, 1))[..., None]
    return result.reshape(count, -1).astype(jnp.bfloat16)


SIDE = 4


def group_of(first, a_coord, b_coord):
    return b_coord * SIDE + a_coord if first == "gz" else a_coord * SIDE + b_coord


def route(locals_, wanteds, first, second):
    coords = {"gx": lax.axis_index("gx"), "gz": lax.axis_index("gz")}
    own_a, own_b = coords[first], coords[second]
    items = [local.reshape(local.shape[0], -1) for local in locals_]
    packed = jnp.concatenate([item.reshape(-1) for item in items])
    held_all = lax.all_gather(packed, first, axis=0, tiled=False)
    dests = group_of(first, own_a, jnp.arange(SIDE))
    me = group_of(first, own_a, own_b)
    payloads, picks, offset = [], [], 0
    for item, wanted in zip(items, wanteds):
        per_owner, width = item.shape
        held = held_all[:, offset:offset + per_owner * width].reshape(SIDE * per_owner, width)
        offset += per_owner * width
        owner = wanted // per_owner
        owner_a = (owner // SIDE, owner % SIDE)[first == "gz"]
        owner_b = (owner // SIDE, owner % SIDE)[second == "gz"]
        source = owner_a[dests] * per_owner + (wanted % per_owner)[dests]
        select = (source[..., None] == jnp.arange(SIDE * per_owner)).astype(item.dtype)
        payloads.append(
            jnp.einsum("dsj,jn->dsn", select, held, preferred_element_type=jnp.float32).astype(
                item.dtype
            )
        )
        slots = wanted.shape[1]
        picks.append(owner_b[me] * slots + jnp.arange(slots))
    widths = [p.shape[2] for p in payloads]
    received = lax.all_to_all(
        jnp.concatenate(payloads, axis=2), second, split_axis=0, concat_axis=0, tiled=True
    )
    received = received.reshape(SIDE * received.shape[1], -1)
    results, offset = [], 0
    for local, width, pick in zip(locals_, widths, picks):
        part = received[:, offset:offset + width]
        offset += width
        select = (pick[:, None] == jnp.arange(part.shape[0])).astype(part.dtype)
        chosen = jnp.dot(select, part, preferred_element_type=jnp.float32).astype(part.dtype)
        results.append(chosen.reshape(pick.shape[0], *local.shape[1:]))
    return results


def on_device(
    stream,
    prenorm_gain,
    query_weight,
    key_weight,
    value_weight,
    output_weight,
    adapter_down_rows,
    adapter_up_query,
    request_adapter,
    adapter_row_index,
    request_token_length,
    continues_previous,
    request_cache_block,
    cached_length,
    cached_rotated_keys,
    cached_value_rows,
):
    count = stream.shape[0]
    group_at = lax.axis_index(("gx", "gz"))
    wanted = adapter_row_index[request_adapter]
    down_width = adapter_down_rows.shape[2]
    adapters = jnp.concatenate([adapter_down_rows, adapter_up_query], axis=2)
    chosen, cache_keys = route(
        (adapters, cached_rotated_keys), (wanted, request_cache_block), "gz", "gx"
    )
    (cache_values,) = route((cached_value_rows,), (request_cache_block,), "gx", "gz")
    chosen_down = chosen[:, :, :down_width]
    chosen_up = chosen[:, :, down_width:]
    full_down = lax.all_gather(chosen_down, ("my", "mc"), axis=2, tiled=True)

    whole = lax.all_gather(stream, ("my", "mc"), axis=1, tiled=True)
    wide = whole.astype(jnp.float32)
    normalized_input = (
        wide * lax.rsqrt(jnp.mean(wide * wide, axis=1, keepdims=True) + 1e-06) * prenorm_gain
    ).astype(jnp.bfloat16)
    before = jnp.maximum(group_at - 1, 0)
    lengths = request_token_length[group_at]
    cached = cached_length[group_at]
    split_flag = continues_previous[group_at]
    prev_len = request_token_length[before, REQS - 1]
    member, request, position = layout(lengths, cached, split_flag, prev_len, count)
    rank_index = adapter_down_rows.shape[1]
    low = jnp.einsum(
        "td,rkd->trk", normalized_input, full_down, preferred_element_type=jnp.float32
    ).reshape(count, REQS * rank_index).astype(jnp.bfloat16)
    own_columns = jnp.repeat(member, rank_index, axis=1).astype(jnp.bfloat16)
    query_update = jnp.dot(
        low * own_columns,
        chosen_up.reshape(REQS * rank_index, -1),
        preferred_element_type=jnp.float32,
    )
    query_vectors = (
        jnp.dot(normalized_input, query_weight, preferred_element_type=jnp.float32)
        + adapter_scale * query_update
    )
    query_vectors = rotate(query_vectors, position, HEAD_WIDTH).astype(jnp.bfloat16)
    keys = rotate(
        jnp.dot(normalized_input, key_weight, preferred_element_type=jnp.float32),
        position,
        HEAD_WIDTH,
    ).astype(jnp.bfloat16)
    values = jnp.dot(normalized_input, value_weight, preferred_element_type=jnp.float32).astype(
        jnp.bfloat16
    )
    prev_both = shifted(jnp.concatenate([keys, values], axis=1), ("gx", "gz"), 1)
    prev_keys, prev_values = prev_both[:, : keys.shape[1]], prev_both[:, keys.shape[1]:]
    attended = attend(
        query_vectors,
        keys,
        values,
        prev_keys,
        prev_values,
        cache_keys,
        cache_values,
        request,
        cached,
        split_flag,
        prev_len,
        HEAD_WIDTH,
    )
    partial_out = jnp.dot(attended, output_weight, preferred_element_type=jnp.float32)
    return lax.psum_scatter(
        partial_out.astype(jnp.bfloat16), ("my", "mc"), scatter_dimension=1, tiled=True
    )


def solution(mesh):
    split = Mesh(mesh.devices.reshape(SIDE, SIDE, 4, 2), ("gx", "gz", "my", "mc"))
    groups = ("gx", "gz")
    model = ("my", "mc")
    placed = (
        P(groups, model),
        P(),
        P(None, model),
        P(None, model),
        P(None, model),
        P(model, None),
        P(groups, None, model),
        P(groups, None, model),
        P(),
        P(),
        P(),
        P(),
        P(),
        P(),
        P(groups, None, model),
        P(groups, None, model),
    )
    return jax.shard_map(
        on_device, mesh=split, in_specs=placed, out_specs=P(groups, model), check_vma=False
    )
```

```python
import jax
import jax.numpy as jnp
from jax import lax
from jax.sharding import Mesh, PartitionSpec as P

HEAD_WIDTH = 256
REQS = 4


adapter_scale = 2.0


def shifted(value, axis, steps):
    count = lax.axis_size(axis)
    first, last = (max(0, -steps), min(count, count - steps))
    return lax.ppermute(value, axis, [(source, source + steps) for source in range(first, last)])


def rotate(values, position, head_size):
    count = values.shape[0]
    shaped = values.reshape(count, -1, head_size)
    half = head_size // 2
    freq = 10000.0 ** (-jnp.arange(half, dtype=jnp.float32) / half)
    angle = position[:, None, None] * freq[None, None, :]
    cosine = jnp.cos(angle)
    sine = jnp.sin(angle)
    first = shaped[..., :half]
    second = shaped[..., half:]
    turned = jnp.concatenate(
        [first * cosine - second * sine, second * cosine + first * sine], axis=-1
    )
    return turned.reshape(count, -1)


def layout(lengths, cached, split_flag, prev_len, count):
    ends = jnp.cumsum(lengths)
    starts = ends - lengths
    place = jnp.arange(count, dtype=jnp.int32)
    member = ((place[:, None] >= starts[None, :]) & (place[:, None] < ends[None, :])).astype(
        jnp.int32
    )
    request = jnp.sum(member * jnp.arange(lengths.shape[0], dtype=jnp.int32)[None, :], axis=1)
    offset = place - jnp.sum(member * starts[None, :], axis=1)
    extra = jnp.where(request == 0, split_flag * prev_len, 0)
    position = jnp.sum(member * cached[None, :], axis=1) + extra + offset
    return (member, request, position.astype(jnp.float32))


def attend(
    query_vectors,
    keys,
    values,
    prev_keys,
    prev_values,
    cache_keys,
    cache_values,
    request,
    cached,
    split_flag,
    prev_len,
    head_size,
):
    count = query_vectors.shape[0]
    kv_heads = keys.shape[1] // head_size
    ratio = query_vectors.shape[1] // keys.shape[1]
    block = cache_keys.shape[1]
    slots = cache_keys.shape[0] * block
    every_key = jnp.concatenate([cache_keys.reshape(slots, -1), prev_keys, keys], 0).reshape(
        -1, kv_heads, head_size
    )
    every_value = jnp.concatenate(
        [cache_values.reshape(slots, -1), prev_values, values], 0
    ).reshape(-1, kv_heads, head_size)
    slot_req = jnp.arange(slots, dtype=jnp.int32) // block
    slot_col = jnp.arange(slots, dtype=jnp.int32) % block
    cache_ok = (request[:, None] == slot_req[None, :]) & (
        slot_col[None, :] < cached[slot_req][None, :]
    )
    place = jnp.arange(count, dtype=jnp.int32)
    prev_ok = (split_flag == 1) & (request[:, None] == 0) & (place[None, :] >= count - prev_len)
    own_ok = (request[:, None] == request[None, :]) & (place[None, :] <= place[:, None])
    allowed = jnp.concatenate([cache_ok, prev_ok, own_ok], 1)
    grouped = query_vectors.reshape(count, kv_heads, ratio, head_size)
    scores = jnp.einsum(
        "tkrd,skd->krts", grouped, every_key, preferred_element_type=jnp.float32
    ) * head_size ** (-0.5)
    scores = jnp.where(allowed[None, None], scores, jnp.float32(-1e30))
    top = jnp.max(scores, axis=-1, keepdims=True)
    weights = jnp.exp(scores - top)
    total = jnp.sum(weights, axis=-1)
    numer = jnp.einsum(
        "krts,skd->tkrd",
        weights.astype(jnp.bfloat16),
        every_value,
        preferred_element_type=jnp.float32,
    )
    result = numer / jnp.transpose(total, (2, 0, 1))[..., None]
    return result.reshape(count, -1).astype(jnp.bfloat16)


SIDE = 4


def group_of(first, a_coord, b_coord):
    return b_coord * SIDE + a_coord if first == "gz" else a_coord * SIDE + b_coord


def route(locals_, wanteds, first, second):
    coords = {"gx": lax.axis_index("gx"), "gz": lax.axis_index("gz")}
    own_a, own_b = coords[first], coords[second]
    items = [local.reshape(local.shape[0], -1) for local in locals_]
    packed = jnp.concatenate([item.reshape(-1) for item in items])
    held_all = lax.all_to_all(
        jnp.broadcast_to(packed, (SIDE, packed.shape[0])), first, 0, 0, tiled=True
    )
    dests = group_of(first, own_a, jnp.arange(SIDE))
    me = group_of(first, own_a, own_b)
    payloads, picks, offset = [], [], 0
    for item, wanted in zip(items, wanteds):
        per_owner, width = item.shape
        held = held_all[:, offset:offset + per_owner * width].reshape(SIDE * per_owner, width)
        offset += per_owner * width
        owner = wanted // per_owner
        owner_a = (owner // SIDE, owner % SIDE)[first == "gz"]
        owner_b = (owner // SIDE, owner % SIDE)[second == "gz"]
        source = owner_a[dests] * per_owner + (wanted % per_owner)[dests]
        select = (source[..., None] == jnp.arange(SIDE * per_owner)).astype(item.dtype)
        payloads.append(
            jnp.einsum("dsj,jn->dsn", select, held, preferred_element_type=jnp.float32).astype(
                item.dtype
            )
        )
        slots = wanted.shape[1]
        picks.append(owner_b[me] * slots + jnp.arange(slots))
    widths = [p.shape[2] for p in payloads]
    received = lax.all_to_all(
        jnp.concatenate(payloads, axis=2), second, split_axis=0, concat_axis=0, tiled=True
    )
    received = received.reshape(SIDE * received.shape[1], -1)
    results, offset = [], 0
    for local, width, pick in zip(locals_, widths, picks):
        part = received[:, offset:offset + width]
        offset += width
        select = (pick[:, None] == jnp.arange(part.shape[0])).astype(part.dtype)
        chosen = jnp.dot(select, part, preferred_element_type=jnp.float32).astype(part.dtype)
        results.append(chosen.reshape(pick.shape[0], *local.shape[1:]))
    return results


def on_device(
    stream,
    prenorm_gain,
    query_weight,
    key_weight,
    value_weight,
    output_weight,
    adapter_down_rows,
    adapter_up_query,
    request_adapter,
    adapter_row_index,
    request_token_length,
    continues_previous,
    request_cache_block,
    cached_length,
    cached_rotated_keys,
    cached_value_rows,
):
    count = stream.shape[0]
    group_at = lax.axis_index(("gx", "gz"))
    wanted = adapter_row_index[request_adapter]
    down_width = adapter_down_rows.shape[2]
    adapters = jnp.concatenate([adapter_down_rows, adapter_up_query], axis=2)
    (chosen,) = route((adapters,), (wanted,), "gz", "gx")
    (cache_keys,) = route((cached_rotated_keys,), (request_cache_block,), "gz", "gx")
    (cache_values,) = route((cached_value_rows,), (request_cache_block,), "gx", "gz")
    chosen_down = chosen[:, :, :down_width]
    chosen_up = chosen[:, :, down_width:]
    model_count = lax.axis_size(("my", "mc"))
    spread = lax.all_to_all(
        jnp.broadcast_to(chosen_down, (model_count, *chosen_down.shape)),
        ("my", "mc"),
        0,
        0,
        tiled=True,
    )
    full_down = jnp.moveaxis(spread, 0, 2).reshape(
        *chosen_down.shape[:2], model_count * down_width
    )

    whole = lax.all_gather(stream, ("my", "mc"), axis=1, tiled=True)
    wide = whole.astype(jnp.float32)
    normalized_input = (
        wide * lax.rsqrt(jnp.mean(wide * wide, axis=1, keepdims=True) + 1e-06) * prenorm_gain
    ).astype(jnp.bfloat16)
    before = jnp.maximum(group_at - 1, 0)
    lengths = request_token_length[group_at]
    cached = cached_length[group_at]
    split_flag = continues_previous[group_at]
    prev_len = request_token_length[before, REQS - 1]
    member, request, position = layout(lengths, cached, split_flag, prev_len, count)
    rank_index = adapter_down_rows.shape[1]
    low = jnp.einsum(
        "td,rkd->trk", normalized_input, full_down, preferred_element_type=jnp.float32
    ).reshape(count, REQS * rank_index).astype(jnp.bfloat16)
    own_columns = jnp.repeat(member, rank_index, axis=1).astype(jnp.bfloat16)
    query_update = jnp.dot(
        low * own_columns,
        chosen_up.reshape(REQS * rank_index, -1),
        preferred_element_type=jnp.float32,
    )
    query_vectors = (
        jnp.dot(normalized_input, query_weight, preferred_element_type=jnp.float32)
        + adapter_scale * query_update
    )
    query_vectors = rotate(query_vectors, position, HEAD_WIDTH).astype(jnp.bfloat16)
    keys = rotate(
        jnp.dot(normalized_input, key_weight, preferred_element_type=jnp.float32),
        position,
        HEAD_WIDTH,
    ).astype(jnp.bfloat16)
    values = jnp.dot(normalized_input, value_weight, preferred_element_type=jnp.float32).astype(
        jnp.bfloat16
    )
    prev_both = shifted(jnp.concatenate([keys, values], axis=1), ("gx", "gz"), 1)
    prev_keys, prev_values = prev_both[:, : keys.shape[1]], prev_both[:, keys.shape[1]:]
    attended = attend(
        query_vectors,
        keys,
        values,
        prev_keys,
        prev_values,
        cache_keys,
        cache_values,
        request,
        cached,
        split_flag,
        prev_len,
        HEAD_WIDTH,
    )
    partial_out = jnp.dot(attended, output_weight, preferred_element_type=jnp.float32)
    return lax.psum_scatter(
        partial_out.astype(jnp.bfloat16), ("my", "mc"), scatter_dimension=1, tiled=True
    )


def solution(mesh):
    split = Mesh(mesh.devices.reshape(SIDE, SIDE, 4, 2), ("gx", "gz", "my", "mc"))
    groups = ("gx", "gz")
    model = ("my", "mc")
    placed = (
        P(groups, model),
        P(),
        P(None, model),
        P(None, model),
        P(None, model),
        P(model, None),
        P(groups, None, model),
        P(groups, None, model),
        P(),
        P(),
        P(),
        P(),
        P(),
        P(),
        P(groups, None, model),
        P(groups, None, model),
    )
    return jax.shard_map(
        on_device, mesh=split, in_specs=placed, out_specs=P(groups, model), check_vma=False
    )
```

```python
import jax
import jax.numpy as jnp
from jax import lax
from jax.sharding import Mesh, PartitionSpec as P

HEAD_WIDTH = 256
REQS = 4


adapter_scale = 2.0


def shifted(value, axis, steps):
    count = lax.axis_size(axis)
    first, last = (max(0, -steps), min(count, count - steps))
    return lax.ppermute(value, axis, [(source, source + steps) for source in range(first, last)])


def rotate(values, position, head_size):
    count = values.shape[0]
    shaped = values.reshape(count, -1, head_size)
    half = head_size // 2
    freq = 10000.0 ** (-jnp.arange(half, dtype=jnp.float32) / half)
    angle = position[:, None, None] * freq[None, None, :]
    cosine = jnp.cos(angle)
    sine = jnp.sin(angle)
    first = shaped[..., :half]
    second = shaped[..., half:]
    turned = jnp.concatenate(
        [first * cosine - second * sine, second * cosine + first * sine], axis=-1
    )
    return turned.reshape(count, -1)


def layout(lengths, cached, split_flag, prev_len, count):
    ends = jnp.cumsum(lengths)
    starts = ends - lengths
    place = jnp.arange(count, dtype=jnp.int32)
    member = ((place[:, None] >= starts[None, :]) & (place[:, None] < ends[None, :])).astype(
        jnp.int32
    )
    request = jnp.sum(member * jnp.arange(lengths.shape[0], dtype=jnp.int32)[None, :], axis=1)
    offset = place - jnp.sum(member * starts[None, :], axis=1)
    extra = jnp.where(request == 0, split_flag * prev_len, 0)
    position = jnp.sum(member * cached[None, :], axis=1) + extra + offset
    return (member, request, position.astype(jnp.float32))


def attend(
    query_vectors,
    keys,
    values,
    prev_keys,
    prev_values,
    cache_keys,
    cache_values,
    request,
    cached,
    split_flag,
    prev_len,
    head_size,
):
    count = query_vectors.shape[0]
    kv_heads = keys.shape[1] // head_size
    ratio = query_vectors.shape[1] // keys.shape[1]
    block = cache_keys.shape[1]
    slots = cache_keys.shape[0] * block
    every_key = jnp.concatenate([cache_keys.reshape(slots, -1), prev_keys, keys], 0).reshape(
        -1, kv_heads, head_size
    )
    every_value = jnp.concatenate(
        [cache_values.reshape(slots, -1), prev_values, values], 0
    ).reshape(-1, kv_heads, head_size)
    slot_req = jnp.arange(slots, dtype=jnp.int32) // block
    slot_col = jnp.arange(slots, dtype=jnp.int32) % block
    cache_ok = (request[:, None] == slot_req[None, :]) & (
        slot_col[None, :] < cached[slot_req][None, :]
    )
    place = jnp.arange(count, dtype=jnp.int32)
    prev_ok = (split_flag == 1) & (request[:, None] == 0) & (place[None, :] >= count - prev_len)
    own_ok = (request[:, None] == request[None, :]) & (place[None, :] <= place[:, None])
    allowed = jnp.concatenate([cache_ok, prev_ok, own_ok], 1)
    grouped = query_vectors.reshape(count, kv_heads, ratio, head_size)
    scores = jnp.einsum(
        "tkrd,skd->krts", grouped, every_key, preferred_element_type=jnp.float32
    ) * head_size ** (-0.5)
    scores = jnp.where(allowed[None, None], scores, jnp.float32(-1e30))
    top = jnp.max(scores, axis=-1, keepdims=True)
    weights = jnp.exp(scores - top)
    total = jnp.sum(weights, axis=-1)
    numer = jnp.einsum(
        "krts,skd->tkrd",
        weights.astype(jnp.bfloat16),
        every_value,
        preferred_element_type=jnp.float32,
    )
    result = numer / jnp.transpose(total, (2, 0, 1))[..., None]
    return result.reshape(count, -1).astype(jnp.bfloat16)


SIDE = 4


def group_of(first, a_coord, b_coord):
    return b_coord * SIDE + a_coord if first == "gz" else a_coord * SIDE + b_coord


def ring_send(value, axis, step):
    return lax.ppermute(value, axis, [(i, (i + step) % SIDE) for i in range(SIDE)])


def route(locals_, wanteds, first, second):
    coords = {"gx": lax.axis_index("gx"), "gz": lax.axis_index("gz")}
    own_a, own_b = coords[first], coords[second]
    items = [local.reshape(local.shape[0], -1) for local in locals_]
    packed = jnp.concatenate([item.reshape(-1) for item in items])
    held_all = jnp.stack([packed] + [ring_send(packed, first, step) for step in range(1, SIDE)])
    dests = group_of(first, own_a, (own_b + jnp.arange(1, SIDE)) % SIDE)
    me = group_of(first, own_a, own_b)
    payloads, picks, offset = [], [], 0
    for item, wanted in zip(items, wanteds):
        per_owner, width = item.shape
        held = held_all[:, offset:offset + per_owner * width].reshape(SIDE * per_owner, width)
        offset += per_owner * width
        owner = wanted // per_owner
        owner_a = (owner // SIDE, owner % SIDE)[first == "gz"]
        owner_b = (owner // SIDE, owner % SIDE)[second == "gz"]
        askers = jnp.concatenate([me[None], dests])
        source = ((own_a - owner_a[askers]) % SIDE) * per_owner + (wanted % per_owner)[askers]
        payloads.append(jnp.take(held, source, axis=0))
        slots = wanted.shape[1]
        picks.append(((own_b - owner_b[me]) % SIDE) * slots + jnp.arange(slots))
    widths = [p.shape[2] for p in payloads]
    outgoing = jnp.concatenate(payloads, axis=2)
    received = jnp.stack(
        [outgoing[0]] + [ring_send(outgoing[step], second, step) for step in range(1, SIDE)]
    )
    received = received.reshape(SIDE * received.shape[1], -1)
    results, offset = [], 0
    for local, width, pick in zip(locals_, widths, picks):
        chosen = jnp.take(received[:, offset:offset + width], pick, axis=0)
        offset += width
        results.append(chosen.reshape(pick.shape[0], *local.shape[1:]))
    return results


def on_device(
    stream,
    prenorm_gain,
    query_weight,
    key_weight,
    value_weight,
    output_weight,
    adapter_down_rows,
    adapter_up_query,
    request_adapter,
    adapter_row_index,
    request_token_length,
    continues_previous,
    request_cache_block,
    cached_length,
    cached_rotated_keys,
    cached_value_rows,
):
    count = stream.shape[0]
    group_at = lax.axis_index(("gx", "gz"))
    wanted = adapter_row_index[request_adapter]
    down_width = adapter_down_rows.shape[2]
    adapters = jnp.concatenate([adapter_down_rows, adapter_up_query], axis=2)
    chosen, cache_keys = route(
        (adapters, cached_rotated_keys), (wanted, request_cache_block), "gz", "gx"
    )
    (cache_values,) = route((cached_value_rows,), (request_cache_block,), "gx", "gz")
    chosen_down = chosen[:, :, :down_width]
    chosen_up = chosen[:, :, down_width:]
    model_count = lax.axis_size(("my", "mc"))
    spread = lax.all_to_all(
        jnp.broadcast_to(chosen_down, (model_count, *chosen_down.shape)),
        ("my", "mc"),
        0,
        0,
        tiled=True,
    )
    full_down = jnp.moveaxis(spread, 0, 2).reshape(
        *chosen_down.shape[:2], model_count * down_width
    )

    whole = lax.all_gather(stream, ("my", "mc"), axis=1, tiled=True)
    wide = whole.astype(jnp.float32)
    normalized_input = (
        wide * lax.rsqrt(jnp.mean(wide * wide, axis=1, keepdims=True) + 1e-06) * prenorm_gain
    ).astype(jnp.bfloat16)
    before = jnp.maximum(group_at - 1, 0)
    lengths = request_token_length[group_at]
    cached = cached_length[group_at]
    split_flag = continues_previous[group_at]
    prev_len = request_token_length[before, REQS - 1]
    member, request, position = layout(lengths, cached, split_flag, prev_len, count)
    rank_index = adapter_down_rows.shape[1]
    low = jnp.einsum(
        "td,rkd->trk", normalized_input, full_down, preferred_element_type=jnp.float32
    ).reshape(count, REQS * rank_index).astype(jnp.bfloat16)
    own_columns = jnp.repeat(member, rank_index, axis=1).astype(jnp.bfloat16)
    query_update = jnp.dot(
        low * own_columns,
        chosen_up.reshape(REQS * rank_index, -1),
        preferred_element_type=jnp.float32,
    )
    query_vectors = (
        jnp.dot(normalized_input, query_weight, preferred_element_type=jnp.float32)
        + adapter_scale * query_update
    )
    query_vectors = rotate(query_vectors, position, HEAD_WIDTH).astype(jnp.bfloat16)
    keys = rotate(
        jnp.dot(normalized_input, key_weight, preferred_element_type=jnp.float32),
        position,
        HEAD_WIDTH,
    ).astype(jnp.bfloat16)
    values = jnp.dot(normalized_input, value_weight, preferred_element_type=jnp.float32).astype(
        jnp.bfloat16
    )
    prev_both = shifted(jnp.concatenate([keys, values], axis=1), ("gx", "gz"), 1)
    prev_keys, prev_values = prev_both[:, : keys.shape[1]], prev_both[:, keys.shape[1]:]
    attended = attend(
        query_vectors,
        keys,
        values,
        prev_keys,
        prev_values,
        cache_keys,
        cache_values,
        request,
        cached,
        split_flag,
        prev_len,
        HEAD_WIDTH,
    )
    partial_out = jnp.dot(attended, output_weight, preferred_element_type=jnp.float32)
    return lax.psum_scatter(
        partial_out.astype(jnp.bfloat16), ("my", "mc"), scatter_dimension=1, tiled=True
    )


def solution(mesh):
    split = Mesh(mesh.devices.reshape(SIDE, SIDE, 4, 2), ("gx", "gz", "my", "mc"))
    groups = ("gx", "gz")
    model = ("my", "mc")
    placed = (
        P(groups, model),
        P(),
        P(None, model),
        P(None, model),
        P(None, model),
        P(model, None),
        P(groups, None, model),
        P(groups, None, model),
        P(),
        P(),
        P(),
        P(),
        P(),
        P(),
        P(groups, None, model),
        P(groups, None, model),
    )
    return jax.shard_map(
        on_device, mesh=split, in_specs=placed, out_specs=P(groups, model), check_vma=False
    )
```

```python
import jax
import jax.numpy as jnp
from jax import lax
from jax.sharding import Mesh, PartitionSpec as P

HEAD_WIDTH = 256
REQS = 4


adapter_scale = 2.0


def shifted(value, axis, steps):
    count = lax.axis_size(axis)
    first, last = (max(0, -steps), min(count, count - steps))
    return lax.ppermute(value, axis, [(source, source + steps) for source in range(first, last)])


def rotate(values, position, head_size):
    count = values.shape[0]
    shaped = values.reshape(count, -1, head_size)
    half = head_size // 2
    freq = 10000.0 ** (-jnp.arange(half, dtype=jnp.float32) / half)
    angle = position[:, None, None] * freq[None, None, :]
    cosine = jnp.cos(angle)
    sine = jnp.sin(angle)
    first = shaped[..., :half]
    second = shaped[..., half:]
    turned = jnp.concatenate(
        [first * cosine - second * sine, second * cosine + first * sine], axis=-1
    )
    return turned.reshape(count, -1)


def layout(lengths, cached, split_flag, prev_len, count):
    ends = jnp.cumsum(lengths)
    starts = ends - lengths
    place = jnp.arange(count, dtype=jnp.int32)
    member = ((place[:, None] >= starts[None, :]) & (place[:, None] < ends[None, :])).astype(
        jnp.int32
    )
    request = jnp.sum(member * jnp.arange(lengths.shape[0], dtype=jnp.int32)[None, :], axis=1)
    offset = place - jnp.sum(member * starts[None, :], axis=1)
    extra = jnp.where(request == 0, split_flag * prev_len, 0)
    position = jnp.sum(member * cached[None, :], axis=1) + extra + offset
    return (member, request, position.astype(jnp.float32))


def attend(
    query_vectors,
    keys,
    values,
    prev_keys,
    prev_values,
    cache_keys,
    cache_values,
    request,
    cached,
    split_flag,
    prev_len,
    head_size,
):
    count = query_vectors.shape[0]
    kv_heads = keys.shape[1] // head_size
    ratio = query_vectors.shape[1] // keys.shape[1]
    block = cache_keys.shape[1]
    slots = cache_keys.shape[0] * block
    every_key = jnp.concatenate([cache_keys.reshape(slots, -1), prev_keys, keys], 0).reshape(
        -1, kv_heads, head_size
    )
    every_value = jnp.concatenate(
        [cache_values.reshape(slots, -1), prev_values, values], 0
    ).reshape(-1, kv_heads, head_size)
    slot_req = jnp.arange(slots, dtype=jnp.int32) // block
    slot_col = jnp.arange(slots, dtype=jnp.int32) % block
    cache_ok = (request[:, None] == slot_req[None, :]) & (
        slot_col[None, :] < cached[slot_req][None, :]
    )
    place = jnp.arange(count, dtype=jnp.int32)
    prev_ok = (split_flag == 1) & (request[:, None] == 0) & (place[None, :] >= count - prev_len)
    own_ok = (request[:, None] == request[None, :]) & (place[None, :] <= place[:, None])
    allowed = jnp.concatenate([cache_ok, prev_ok, own_ok], 1)
    grouped = query_vectors.reshape(count, kv_heads, ratio, head_size)
    scores = jnp.einsum(
        "tkrd,skd->krts", grouped, every_key, preferred_element_type=jnp.float32
    ) * head_size ** (-0.5)
    scores = jnp.where(allowed[None, None], scores, jnp.float32(-1e30))
    top = jnp.max(scores, axis=-1, keepdims=True)
    weights = jnp.exp(scores - top)
    total = jnp.sum(weights, axis=-1)
    numer = jnp.einsum(
        "krts,skd->tkrd",
        weights.astype(jnp.bfloat16),
        every_value,
        preferred_element_type=jnp.float32,
    )
    result = numer / jnp.transpose(total, (2, 0, 1))[..., None]
    return result.reshape(count, -1).astype(jnp.bfloat16)


SIDE = 4


def group_of(first, a_coord, b_coord):
    return b_coord * SIDE + a_coord if first == "gz" else a_coord * SIDE + b_coord


def ring_send(value, axis, step):
    return lax.ppermute(value, axis, [(i, (i + step) % SIDE) for i in range(SIDE)])


def route(local, wanted, first, second):
    coords = {"gx": lax.axis_index("gx"), "gz": lax.axis_index("gz")}
    own_a, own_b = coords[first], coords[second]
    per_owner = local.shape[0]
    slots = wanted.shape[1]
    held = jnp.concatenate([local] + [ring_send(local, first, step) for step in range(1, SIDE)])
    me = group_of(first, own_a, own_b)
    askers = group_of(first, own_a, (own_b + jnp.arange(SIDE)) % SIDE)
    owner = wanted // per_owner
    owner_a = (owner // SIDE, owner % SIDE)[first == "gz"]
    owner_b = (owner // SIDE, owner % SIDE)[second == "gz"]
    source = ((own_a - owner_a[askers]) % SIDE) * per_owner + (wanted % per_owner)[askers]
    outgoing = jnp.take(held, source.reshape(-1), axis=0, mode="clip")
    received = jnp.concatenate(
        [outgoing[:slots]]
        + [
            ring_send(outgoing[step * slots:(step + 1) * slots], second, step)
            for step in range(1, SIDE)
        ]
    )
    pick = ((own_b - owner_b[me]) % SIDE) * slots + jnp.arange(slots)
    return jnp.take(received, pick, axis=0, mode="clip")


def on_device(
    stream,
    prenorm_gain,
    query_weight,
    key_weight,
    value_weight,
    output_weight,
    adapter_down_rows,
    adapter_up_query,
    request_adapter,
    adapter_row_index,
    request_token_length,
    continues_previous,
    request_cache_block,
    cached_length,
    cached_rotated_keys,
    cached_value_rows,
):
    count = stream.shape[0]
    group_at = lax.axis_index(("gx", "gz"))
    wanted = adapter_row_index[request_adapter]
    down_width = adapter_down_rows.shape[2]
    adapters = jnp.concatenate([adapter_down_rows, adapter_up_query], axis=2)
    chosen = route(adapters, wanted, "gz", "gx")
    cache_keys = route(cached_rotated_keys, request_cache_block, "gz", "gx")
    cache_values = route(cached_value_rows, request_cache_block, "gx", "gz")
    chosen_down = chosen[:, :, :down_width]
    chosen_up = chosen[:, :, down_width:]
    model_count = lax.axis_size(("my", "mc"))
    spread = lax.all_to_all(
        jnp.broadcast_to(chosen_down, (model_count, *chosen_down.shape)),
        ("my", "mc"),
        0,
        0,
        tiled=True,
    )
    full_down = jnp.moveaxis(spread, 0, 2).reshape(
        *chosen_down.shape[:2], model_count * down_width
    )

    whole = lax.all_gather(stream, ("my", "mc"), axis=1, tiled=True)
    wide = whole.astype(jnp.float32)
    normalized_input = (
        wide * lax.rsqrt(jnp.mean(wide * wide, axis=1, keepdims=True) + 1e-06) * prenorm_gain
    ).astype(jnp.bfloat16)
    before = jnp.maximum(group_at - 1, 0)
    lengths = request_token_length[group_at]
    cached = cached_length[group_at]
    split_flag = continues_previous[group_at]
    prev_len = request_token_length[before, REQS - 1]
    member, request, position = layout(lengths, cached, split_flag, prev_len, count)
    rank_index = adapter_down_rows.shape[1]
    low = jnp.einsum(
        "td,rkd->trk", normalized_input, full_down, preferred_element_type=jnp.float32
    ).reshape(count, REQS * rank_index).astype(jnp.bfloat16)
    own_columns = jnp.repeat(member, rank_index, axis=1).astype(jnp.bfloat16)
    query_update = jnp.dot(
        low * own_columns,
        chosen_up.reshape(REQS * rank_index, -1),
        preferred_element_type=jnp.float32,
    )
    query_vectors = (
        jnp.dot(normalized_input, query_weight, preferred_element_type=jnp.float32)
        + adapter_scale * query_update
    )
    query_vectors = rotate(query_vectors, position, HEAD_WIDTH).astype(jnp.bfloat16)
    keys = rotate(
        jnp.dot(normalized_input, key_weight, preferred_element_type=jnp.float32),
        position,
        HEAD_WIDTH,
    ).astype(jnp.bfloat16)
    values = jnp.dot(normalized_input, value_weight, preferred_element_type=jnp.float32).astype(
        jnp.bfloat16
    )
    prev_both = shifted(jnp.concatenate([keys, values], axis=1), ("gx", "gz"), 1)
    prev_keys, prev_values = prev_both[:, : keys.shape[1]], prev_both[:, keys.shape[1]:]
    attended = attend(
        query_vectors,
        keys,
        values,
        prev_keys,
        prev_values,
        cache_keys,
        cache_values,
        request,
        cached,
        split_flag,
        prev_len,
        HEAD_WIDTH,
    )
    partial_out = jnp.dot(attended, output_weight, preferred_element_type=jnp.float32)
    return lax.psum_scatter(
        partial_out.astype(jnp.bfloat16), ("my", "mc"), scatter_dimension=1, tiled=True
    )


def solution(mesh):
    split = Mesh(mesh.devices.reshape(SIDE, SIDE, 4, 2), ("gx", "gz", "my", "mc"))
    groups = ("gx", "gz")
    model = ("my", "mc")
    placed = (
        P(groups, model),
        P(),
        P(None, model),
        P(None, model),
        P(None, model),
        P(model, None),
        P(groups, None, model),
        P(groups, None, model),
        P(),
        P(),
        P(),
        P(),
        P(),
        P(),
        P(groups, None, model),
        P(groups, None, model),
    )
    return jax.shard_map(
        on_device, mesh=split, in_specs=placed, out_specs=P(groups, model), check_vma=False
    )
```

```python
import jax
import jax.numpy as jnp
from jax import lax
from jax.sharding import Mesh, PartitionSpec as P

HEAD_WIDTH = 256
REQS = 4


adapter_scale = 2.0


def shifted(value, axis, steps):
    count = lax.axis_size(axis)
    first, last = (max(0, -steps), min(count, count - steps))
    return lax.ppermute(value, axis, [(source, source + steps) for source in range(first, last)])


def rotate(values, position, head_size):
    count = values.shape[0]
    shaped = values.reshape(count, -1, head_size)
    half = head_size // 2
    freq = 10000.0 ** (-jnp.arange(half, dtype=jnp.float32) / half)
    angle = position[:, None, None] * freq[None, None, :]
    cosine = jnp.cos(angle)
    sine = jnp.sin(angle)
    first = shaped[..., :half]
    second = shaped[..., half:]
    turned = jnp.concatenate(
        [first * cosine - second * sine, second * cosine + first * sine], axis=-1
    )
    return turned.reshape(count, -1)


def layout(lengths, cached, split_flag, prev_len, count):
    ends = jnp.cumsum(lengths)
    starts = ends - lengths
    place = jnp.arange(count, dtype=jnp.int32)
    member = ((place[:, None] >= starts[None, :]) & (place[:, None] < ends[None, :])).astype(
        jnp.int32
    )
    request = jnp.sum(member * jnp.arange(lengths.shape[0], dtype=jnp.int32)[None, :], axis=1)
    offset = place - jnp.sum(member * starts[None, :], axis=1)
    extra = jnp.where(request == 0, split_flag * prev_len, 0)
    position = jnp.sum(member * cached[None, :], axis=1) + extra + offset
    return (member, request, position.astype(jnp.float32))


def attend(
    query_vectors,
    keys,
    values,
    prev_keys,
    prev_values,
    cache_keys,
    cache_values,
    request,
    cached,
    split_flag,
    prev_len,
    head_size,
):
    count = query_vectors.shape[0]
    kv_heads = keys.shape[1] // head_size
    ratio = query_vectors.shape[1] // keys.shape[1]
    block = cache_keys.shape[1]
    slots = cache_keys.shape[0] * block
    every_key = jnp.concatenate([cache_keys.reshape(slots, -1), prev_keys, keys], 0).reshape(
        -1, kv_heads, head_size
    )
    every_value = jnp.concatenate(
        [cache_values.reshape(slots, -1), prev_values, values], 0
    ).reshape(-1, kv_heads, head_size)
    slot_req = jnp.arange(slots, dtype=jnp.int32) // block
    slot_col = jnp.arange(slots, dtype=jnp.int32) % block
    cache_ok = (request[:, None] == slot_req[None, :]) & (
        slot_col[None, :] < cached[slot_req][None, :]
    )
    place = jnp.arange(count, dtype=jnp.int32)
    prev_ok = (split_flag == 1) & (request[:, None] == 0) & (place[None, :] >= count - prev_len)
    own_ok = (request[:, None] == request[None, :]) & (place[None, :] <= place[:, None])
    allowed = jnp.concatenate([cache_ok, prev_ok, own_ok], 1)
    grouped = query_vectors.reshape(count, kv_heads, ratio, head_size)
    scores = jnp.einsum(
        "tkrd,skd->krts", grouped, every_key, preferred_element_type=jnp.float32
    ) * head_size ** (-0.5)
    scores = jnp.where(allowed[None, None], scores, jnp.float32(-1e30))
    top = jnp.max(scores, axis=-1, keepdims=True)
    weights = jnp.exp(scores - top)
    total = jnp.sum(weights, axis=-1)
    numer = jnp.einsum(
        "krts,skd->tkrd",
        weights.astype(jnp.bfloat16),
        every_value,
        preferred_element_type=jnp.float32,
    )
    result = numer / jnp.transpose(total, (2, 0, 1))[..., None]
    return result.reshape(count, -1).astype(jnp.bfloat16)


SIDE = 4


def group_of(first, a_coord, b_coord):
    return b_coord * SIDE + a_coord if first == "gz" else a_coord * SIDE + b_coord


def ring_send(value, axis, step):
    return lax.ppermute(value, axis, [(i, (i + step) % SIDE) for i in range(SIDE)])


def route(local, wanted, first, second):
    coords = {"gx": lax.axis_index("gx"), "gz": lax.axis_index("gz")}
    own_a, own_b = coords[first], coords[second]
    per_owner = local.shape[0]
    slots = wanted.shape[1]
    held = jnp.concatenate([local] + [ring_send(local, first, step) for step in range(1, SIDE)])
    me = group_of(first, own_a, own_b)
    askers = group_of(first, own_a, (own_b + jnp.arange(SIDE)) % SIDE)
    owner = wanted // per_owner
    owner_a = (owner // SIDE, owner % SIDE)[first == "gz"]
    owner_b = (owner // SIDE, owner % SIDE)[second == "gz"]
    source = ((own_a - owner_a[askers]) % SIDE) * per_owner + (wanted % per_owner)[askers]
    outgoing = jnp.take(held, source.reshape(-1), axis=0, mode="clip")
    received = jnp.concatenate(
        [outgoing[:slots]]
        + [
            ring_send(outgoing[step * slots:(step + 1) * slots], second, step)
            for step in range(1, SIDE)
        ]
    )
    pick = ((own_b - owner_b[me]) % SIDE) * slots + jnp.arange(slots)
    return jnp.take(received, pick, axis=0, mode="clip")


def route_with_adapters(blocks, adapters, block_wanted, adapter_wanted, first, second):
    coords = {"gx": lax.axis_index("gx"), "gz": lax.axis_index("gz")}
    own_a, own_b = coords[first], coords[second]
    rows, lanes = blocks.shape[1], blocks.shape[2]
    pieces = adapters.shape[0]
    tile = rows // pieces
    flat = adapters.reshape(pieces, -1)
    padded = jnp.pad(flat, ((0, 0), (0, tile * lanes - flat.shape[1])))
    local = jnp.concatenate([blocks, padded.reshape(1, rows, lanes)])
    per_block = local.shape[0]
    held = jnp.concatenate([local] + [ring_send(local, first, step) for step in range(1, SIDE)])
    held = held.reshape(-1, tile, lanes)
    me = group_of(first, own_a, own_b)
    askers = group_of(first, own_a, (own_b + jnp.arange(SIDE)) % SIDE)

    def owners(wanted, per_owner):
        owner = wanted // per_owner
        owner_a = (owner // SIDE, owner % SIDE)[first == "gz"]
        owner_b = (owner // SIDE, owner % SIDE)[second == "gz"]
        return owner_a, owner_b, wanted % per_owner

    block_a, block_b, block_part = owners(block_wanted, blocks.shape[0])
    adapter_a, adapter_b, adapter_part = owners(adapter_wanted, pieces)
    quarter = jnp.arange(pieces)
    block_items = (
        (((own_a - block_a[askers]) % SIDE) * per_block + block_part[askers]) * pieces
    )[..., None] + quarter
    adapter_items = (
        ((own_a - adapter_a[askers]) % SIDE) * per_block + per_block - 1
    ) * pieces + adapter_part[askers]
    source = jnp.concatenate(
        [block_items.reshape(SIDE, -1), adapter_items.reshape(SIDE, -1)], axis=1
    )
    width = source.shape[1]
    outgoing = jnp.take(held, source.reshape(-1), axis=0, mode="clip")
    received = jnp.concatenate(
        [outgoing[:width]]
        + [
            ring_send(outgoing[step * width:(step + 1) * width], second, step)
            for step in range(1, SIDE)
        ]
    )
    slots = block_wanted.shape[1]
    slot = jnp.arange(slots)
    block_pick = (
        (((own_b - block_b[me]) % SIDE) * width + slot * pieces)[:, None] + quarter
    ).reshape(-1)
    adapter_pick = ((own_b - adapter_b[me]) % SIDE) * width + slots * pieces + slot
    chosen_blocks = jnp.take(received, block_pick, axis=0, mode="clip").reshape(
        slots, rows, lanes
    )
    chosen_adapters = jnp.take(received, adapter_pick, axis=0, mode="clip").reshape(slots, -1)
    chosen_adapters = chosen_adapters[:, : flat.shape[1]].reshape(slots, *adapters.shape[1:])
    return chosen_blocks, chosen_adapters


def on_device(
    stream,
    prenorm_gain,
    query_weight,
    key_weight,
    value_weight,
    output_weight,
    adapter_down_rows,
    adapter_up_query,
    request_adapter,
    adapter_row_index,
    request_token_length,
    continues_previous,
    request_cache_block,
    cached_length,
    cached_rotated_keys,
    cached_value_rows,
):
    count = stream.shape[0]
    group_at = lax.axis_index(("gx", "gz"))
    wanted = adapter_row_index[request_adapter]
    down_width = adapter_down_rows.shape[2]
    adapters = jnp.concatenate([adapter_down_rows, adapter_up_query], axis=2)
    cache_keys, chosen = route_with_adapters(
        cached_rotated_keys, adapters, request_cache_block, wanted, "gz", "gx"
    )
    cache_values = route(cached_value_rows, request_cache_block, "gx", "gz")
    chosen_down = chosen[:, :, :down_width]
    chosen_up = chosen[:, :, down_width:]
    model_count = lax.axis_size(("my", "mc"))
    spread = lax.all_to_all(
        jnp.broadcast_to(chosen_down, (model_count, *chosen_down.shape)),
        ("my", "mc"),
        0,
        0,
        tiled=True,
    )
    full_down = jnp.moveaxis(spread, 0, 2).reshape(
        *chosen_down.shape[:2], model_count * down_width
    )

    whole = lax.all_gather(stream, ("my", "mc"), axis=1, tiled=True)
    wide = whole.astype(jnp.float32)
    normalized_input = (
        wide * lax.rsqrt(jnp.mean(wide * wide, axis=1, keepdims=True) + 1e-06) * prenorm_gain
    ).astype(jnp.bfloat16)
    before = jnp.maximum(group_at - 1, 0)
    lengths = request_token_length[group_at]
    cached = cached_length[group_at]
    split_flag = continues_previous[group_at]
    prev_len = request_token_length[before, REQS - 1]
    member, request, position = layout(lengths, cached, split_flag, prev_len, count)
    rank_index = adapter_down_rows.shape[1]
    low = jnp.einsum(
        "td,rkd->trk", normalized_input, full_down, preferred_element_type=jnp.float32
    ).reshape(count, REQS * rank_index).astype(jnp.bfloat16)
    own_columns = jnp.repeat(member, rank_index, axis=1).astype(jnp.bfloat16)
    query_update = jnp.dot(
        low * own_columns,
        chosen_up.reshape(REQS * rank_index, -1),
        preferred_element_type=jnp.float32,
    )
    query_vectors = (
        jnp.dot(normalized_input, query_weight, preferred_element_type=jnp.float32)
        + adapter_scale * query_update
    )
    query_vectors = rotate(query_vectors, position, HEAD_WIDTH).astype(jnp.bfloat16)
    keys = rotate(
        jnp.dot(normalized_input, key_weight, preferred_element_type=jnp.float32),
        position,
        HEAD_WIDTH,
    ).astype(jnp.bfloat16)
    values = jnp.dot(normalized_input, value_weight, preferred_element_type=jnp.float32).astype(
        jnp.bfloat16
    )
    prev_both = shifted(jnp.concatenate([keys, values], axis=1), ("gx", "gz"), 1)
    prev_keys, prev_values = prev_both[:, : keys.shape[1]], prev_both[:, keys.shape[1]:]
    attended = attend(
        query_vectors,
        keys,
        values,
        prev_keys,
        prev_values,
        cache_keys,
        cache_values,
        request,
        cached,
        split_flag,
        prev_len,
        HEAD_WIDTH,
    )
    partial_out = jnp.dot(attended, output_weight, preferred_element_type=jnp.float32)
    return lax.psum_scatter(
        partial_out.astype(jnp.bfloat16), ("my", "mc"), scatter_dimension=1, tiled=True
    )


def solution(mesh):
    split = Mesh(mesh.devices.reshape(SIDE, SIDE, 4, 2), ("gx", "gz", "my", "mc"))
    groups = ("gx", "gz")
    model = ("my", "mc")
    placed = (
        P(groups, model),
        P(),
        P(None, model),
        P(None, model),
        P(None, model),
        P(model, None),
        P(groups, None, model),
        P(groups, None, model),
        P(),
        P(),
        P(),
        P(),
        P(),
        P(),
        P(groups, None, model),
        P(groups, None, model),
    )
    return jax.shard_map(
        on_device, mesh=split, in_specs=placed, out_specs=P(groups, model), check_vma=False
    )
```

```python
import jax
import jax.numpy as jnp
from jax import lax
from jax.sharding import Mesh, PartitionSpec as P

HEAD_WIDTH = 256
REQS = 4


adapter_scale = 2.0


def shifted(value, axis, steps):
    count = lax.axis_size(axis)
    first, last = (max(0, -steps), min(count, count - steps))
    return lax.ppermute(value, axis, [(source, source + steps) for source in range(first, last)])


def rotate(values, position, head_size):
    count = values.shape[0]
    shaped = values.reshape(count, -1, head_size)
    half = head_size // 2
    freq = 10000.0 ** (-jnp.arange(half, dtype=jnp.float32) / half)
    angle = position[:, None, None] * freq[None, None, :]
    cosine = jnp.cos(angle)
    sine = jnp.sin(angle)
    first = shaped[..., :half]
    second = shaped[..., half:]
    turned = jnp.concatenate(
        [first * cosine - second * sine, second * cosine + first * sine], axis=-1
    )
    return turned.reshape(count, -1)


def layout(lengths, cached, split_flag, prev_len, count):
    ends = jnp.cumsum(lengths)
    starts = ends - lengths
    place = jnp.arange(count, dtype=jnp.int32)
    member = ((place[:, None] >= starts[None, :]) & (place[:, None] < ends[None, :])).astype(
        jnp.int32
    )
    request = jnp.sum(member * jnp.arange(lengths.shape[0], dtype=jnp.int32)[None, :], axis=1)
    offset = place - jnp.sum(member * starts[None, :], axis=1)
    extra = jnp.where(request == 0, split_flag * prev_len, 0)
    position = jnp.sum(member * cached[None, :], axis=1) + extra + offset
    return (member, request, position.astype(jnp.float32))


def attend(
    query_vectors,
    keys,
    values,
    prev_keys,
    prev_values,
    cache_keys,
    cache_values,
    request,
    cached,
    split_flag,
    prev_len,
    head_size,
):
    count = query_vectors.shape[0]
    kv_heads = keys.shape[1] // head_size
    ratio = query_vectors.shape[1] // keys.shape[1]
    block = cache_keys.shape[1]
    slots = cache_keys.shape[0] * block
    every_key = jnp.concatenate([cache_keys.reshape(slots, -1), prev_keys, keys], 0).reshape(
        -1, kv_heads, head_size
    )
    every_value = jnp.concatenate(
        [cache_values.reshape(slots, -1), prev_values, values], 0
    ).reshape(-1, kv_heads, head_size)
    owned = jnp.arange(cache_keys.shape[0], dtype=jnp.int32)
    cache_ok = (
        (request[:, None, None] == owned[None, :, None])
        & (jnp.arange(block, dtype=jnp.int32)[None, None, :] < cached[None, :, None])
    ).reshape(count, slots)
    place = jnp.arange(count, dtype=jnp.int32)
    prev_ok = (split_flag == 1) & (request[:, None] == 0) & (place[None, :] >= count - prev_len)
    own_ok = (request[:, None] == request[None, :]) & (place[None, :] <= place[:, None])
    allowed = jnp.concatenate([cache_ok, prev_ok, own_ok], 1)
    grouped = query_vectors.reshape(count, kv_heads, ratio, head_size)
    scores = jnp.einsum(
        "tkrd,skd->krts", grouped, every_key, preferred_element_type=jnp.float32
    ) * head_size ** (-0.5)
    scores = jnp.where(allowed[None, None], scores, jnp.float32(-1e30))
    top = jnp.max(scores, axis=-1, keepdims=True)
    weights = jnp.exp(scores - top)
    total = jnp.sum(weights, axis=-1)
    numer = jnp.einsum(
        "krts,skd->tkrd",
        weights.astype(jnp.bfloat16),
        every_value,
        preferred_element_type=jnp.float32,
    )
    result = numer / jnp.transpose(total, (2, 0, 1))[..., None]
    return result.reshape(count, -1).astype(jnp.bfloat16)


SIDE = 4


def group_of(first, a_coord, b_coord):
    return b_coord * SIDE + a_coord if first == "gz" else a_coord * SIDE + b_coord


def ring_send(value, axis, step):
    return lax.ppermute(value, axis, [(i, (i + step) % SIDE) for i in range(SIDE)])


def route(local, wanted, first, second):
    coords = {"gx": lax.axis_index("gx"), "gz": lax.axis_index("gz")}
    own_a, own_b = coords[first], coords[second]
    per_owner = local.shape[0]
    slots = wanted.shape[1]
    held = jnp.concatenate([local] + [ring_send(local, first, step) for step in range(1, SIDE)])
    me = group_of(first, own_a, own_b)
    askers = group_of(first, own_a, (own_b + jnp.arange(SIDE)) % SIDE)
    owner = wanted // per_owner
    owner_a = (owner // SIDE, owner % SIDE)[first == "gz"]
    owner_b = (owner // SIDE, owner % SIDE)[second == "gz"]
    source = ((own_a - owner_a[askers]) % SIDE) * per_owner + (wanted % per_owner)[askers]
    pieces = [jnp.take(held, source[0], axis=0, mode="clip")] + [
        ring_send(jnp.take(held, source[step], axis=0, mode="clip"), second, step)
        for step in range(1, SIDE)
    ]
    came = (own_b - owner_b[me]) % SIDE
    return pick_piece(came, pieces)


def pick_piece(came, pieces):
    which = came.reshape(came.shape + (1,) * (pieces[0].ndim - 1))
    which = jnp.broadcast_to(which, pieces[0].shape)
    return lax.select_n(which, *pieces)


def route_with_adapters(blocks, adapters, block_wanted, adapter_wanted, first, second):
    coords = {"gx": lax.axis_index("gx"), "gz": lax.axis_index("gz")}
    own_a, own_b = coords[first], coords[second]
    rows, lanes = blocks.shape[1], blocks.shape[2]
    pieces = adapters.shape[0]
    tile = rows // pieces
    flat = adapters.reshape(pieces, -1)
    padded = jnp.pad(flat, ((0, 0), (0, tile * lanes - flat.shape[1])))
    local = jnp.concatenate([blocks, padded.reshape(1, rows, lanes)])
    per_block = local.shape[0]
    held = jnp.concatenate([local] + [ring_send(local, first, step) for step in range(1, SIDE)])
    held = held.reshape(-1, tile, lanes)
    me = group_of(first, own_a, own_b)
    askers = group_of(first, own_a, (own_b + jnp.arange(SIDE)) % SIDE)

    def owners(wanted, per_owner):
        owner = wanted // per_owner
        owner_a = (owner // SIDE, owner % SIDE)[first == "gz"]
        owner_b = (owner // SIDE, owner % SIDE)[second == "gz"]
        return owner_a, owner_b, wanted % per_owner

    block_a, block_b, block_part = owners(block_wanted, blocks.shape[0])
    adapter_a, adapter_b, adapter_part = owners(adapter_wanted, pieces)
    quarter = jnp.arange(pieces)
    block_items = (
        (((own_a - block_a[askers]) % SIDE) * per_block + block_part[askers]) * pieces
    )[..., None] + quarter
    adapter_items = (
        ((own_a - adapter_a[askers]) % SIDE) * per_block + per_block - 1
    ) * pieces + adapter_part[askers]
    source = jnp.concatenate(
        [block_items.reshape(SIDE, -1), adapter_items.reshape(SIDE, -1)], axis=1
    )
    parts = [jnp.take(held, source[0], axis=0, mode="clip")] + [
        ring_send(jnp.take(held, source[step], axis=0, mode="clip"), second, step)
        for step in range(1, SIDE)
    ]
    slots = block_wanted.shape[1]
    came = jnp.concatenate(
        [jnp.repeat((own_b - block_b[me]) % SIDE, pieces), (own_b - adapter_b[me]) % SIDE]
    )
    merged = pick_piece(came, parts)
    chosen_blocks = merged[: slots * adapters.shape[0]].reshape(slots, rows, lanes)
    chosen_adapters = merged[slots * adapters.shape[0]:].reshape(slots, -1)
    chosen_adapters = chosen_adapters[:, : flat.shape[1]].reshape(slots, *adapters.shape[1:])
    return chosen_blocks, chosen_adapters


def on_device(
    stream,
    prenorm_gain,
    query_weight,
    key_weight,
    value_weight,
    output_weight,
    adapter_down_rows,
    adapter_up_query,
    request_adapter,
    adapter_row_index,
    request_token_length,
    continues_previous,
    request_cache_block,
    cached_length,
    cached_rotated_keys,
    cached_value_rows,
):
    count = stream.shape[0]
    group_at = lax.axis_index(("gx", "gz"))
    wanted = adapter_row_index[request_adapter]
    down_width = adapter_down_rows.shape[2]
    adapters = jnp.concatenate([adapter_down_rows, adapter_up_query], axis=2)
    cache_keys, chosen = route_with_adapters(
        cached_rotated_keys, adapters, request_cache_block, wanted, "gz", "gx"
    )
    cache_values = route(cached_value_rows, request_cache_block, "gx", "gz")
    chosen_down = chosen[:, :, :down_width]
    chosen_up = chosen[:, :, down_width:]
    model_count = lax.axis_size(("my", "mc"))
    spread = lax.all_to_all(
        jnp.broadcast_to(chosen_down, (model_count, *chosen_down.shape)),
        ("my", "mc"),
        0,
        0,
        tiled=True,
    )
    full_down = jnp.moveaxis(spread, 0, 2).reshape(
        *chosen_down.shape[:2], model_count * down_width
    )

    whole = lax.all_gather(stream, ("my", "mc"), axis=1, tiled=True)
    wide = whole.astype(jnp.float32)
    normalized_input = (
        wide * lax.rsqrt(jnp.mean(wide * wide, axis=1, keepdims=True) + 1e-06) * prenorm_gain
    ).astype(jnp.bfloat16)
    before = jnp.maximum(group_at - 1, 0)
    lengths = request_token_length[group_at]
    cached = cached_length[group_at]
    split_flag = continues_previous[group_at]
    prev_len = request_token_length[before, REQS - 1]
    member, request, position = layout(lengths, cached, split_flag, prev_len, count)
    rank_index = adapter_down_rows.shape[1]
    low = jnp.einsum(
        "td,rkd->trk", normalized_input, full_down, preferred_element_type=jnp.float32
    ).reshape(count, REQS * rank_index).astype(jnp.bfloat16)
    own_columns = jnp.repeat(member, rank_index, axis=1).astype(jnp.bfloat16)
    query_update = jnp.dot(
        low * own_columns,
        chosen_up.reshape(REQS * rank_index, -1),
        preferred_element_type=jnp.float32,
    )
    query_vectors = (
        jnp.dot(normalized_input, query_weight, preferred_element_type=jnp.float32)
        + adapter_scale * query_update
    )
    query_vectors = rotate(query_vectors, position, HEAD_WIDTH).astype(jnp.bfloat16)
    keys = rotate(
        jnp.dot(normalized_input, key_weight, preferred_element_type=jnp.float32),
        position,
        HEAD_WIDTH,
    ).astype(jnp.bfloat16)
    values = jnp.dot(normalized_input, value_weight, preferred_element_type=jnp.float32).astype(
        jnp.bfloat16
    )
    prev_both = shifted(jnp.concatenate([keys, values], axis=1), ("gx", "gz"), 1)
    prev_keys, prev_values = prev_both[:, : keys.shape[1]], prev_both[:, keys.shape[1]:]
    attended = attend(
        query_vectors,
        keys,
        values,
        prev_keys,
        prev_values,
        cache_keys,
        cache_values,
        request,
        cached,
        split_flag,
        prev_len,
        HEAD_WIDTH,
    )
    partial_out = jnp.dot(attended, output_weight, preferred_element_type=jnp.float32)
    return lax.psum_scatter(
        partial_out.astype(jnp.bfloat16), ("my", "mc"), scatter_dimension=1, tiled=True
    )


def solution(mesh):
    split = Mesh(mesh.devices.reshape(SIDE, SIDE, 4, 2), ("gx", "gz", "my", "mc"))
    groups = ("gx", "gz")
    model = ("my", "mc")
    placed = (
        P(groups, model),
        P(),
        P(None, model),
        P(None, model),
        P(None, model),
        P(model, None),
        P(groups, None, model),
        P(groups, None, model),
        P(),
        P(),
        P(),
        P(),
        P(),
        P(),
        P(groups, None, model),
        P(groups, None, model),
    )
    return jax.shard_map(
        on_device, mesh=split, in_specs=placed, out_specs=P(groups, model), check_vma=False
    )
```

```python
import jax
import jax.numpy as jnp
from jax import lax
from jax.sharding import Mesh, PartitionSpec as P

HEAD_WIDTH = 256
REQS = 4


adapter_scale = 2.0


def shifted(value, axis, steps):
    count = lax.axis_size(axis)
    first, last = (max(0, -steps), min(count, count - steps))
    return lax.ppermute(value, axis, [(source, source + steps) for source in range(first, last)])


def rotate(values, position, head_size):
    count = values.shape[0]
    shaped = values.reshape(count, -1, head_size)
    half = head_size // 2
    freq = 10000.0 ** (-jnp.arange(half, dtype=jnp.float32) / half)
    angle = position[:, None, None] * freq[None, None, :]
    cosine = jnp.cos(angle)
    sine = jnp.sin(angle)
    first = shaped[..., :half]
    second = shaped[..., half:]
    turned = jnp.concatenate(
        [first * cosine - second * sine, second * cosine + first * sine], axis=-1
    )
    return turned.reshape(count, -1)


def layout(lengths, cached, split_flag, prev_len, count):
    ends = jnp.cumsum(lengths)
    starts = ends - lengths
    place = jnp.arange(count, dtype=jnp.int32)
    member = ((place[:, None] >= starts[None, :]) & (place[:, None] < ends[None, :])).astype(
        jnp.int32
    )
    request = jnp.sum(member * jnp.arange(lengths.shape[0], dtype=jnp.int32)[None, :], axis=1)
    offset = place - jnp.sum(member * starts[None, :], axis=1)
    extra = jnp.where(request == 0, split_flag * prev_len, 0)
    position = jnp.sum(member * cached[None, :], axis=1) + extra + offset
    return (member, request, position.astype(jnp.float32))


def attend(
    query_vectors,
    keys,
    values,
    prev_keys,
    prev_values,
    cache_keys,
    cache_values,
    request,
    cached,
    split_flag,
    prev_len,
    head_size,
):
    count = query_vectors.shape[0]
    kv_heads = keys.shape[1] // head_size
    ratio = query_vectors.shape[1] // keys.shape[1]
    block = cache_keys.shape[1]
    slots = cache_keys.shape[0] * block
    every_key = jnp.concatenate([cache_keys.reshape(slots, -1), prev_keys, keys], 0).reshape(
        -1, kv_heads, head_size
    )
    every_value = jnp.concatenate(
        [cache_values.reshape(slots, -1), prev_values, values], 0
    ).reshape(-1, kv_heads, head_size)
    slot_req = jnp.arange(slots, dtype=jnp.int32) // block
    slot_col = jnp.arange(slots, dtype=jnp.int32) % block
    cache_ok = (request[:, None] == slot_req[None, :]) & (
        slot_col[None, :] < cached[slot_req][None, :]
    )
    place = jnp.arange(count, dtype=jnp.int32)
    prev_ok = (split_flag == 1) & (request[:, None] == 0) & (place[None, :] >= count - prev_len)
    own_ok = (request[:, None] == request[None, :]) & (place[None, :] <= place[:, None])
    allowed = jnp.concatenate([cache_ok, prev_ok, own_ok], 1)
    grouped = query_vectors.reshape(count, kv_heads, ratio, head_size)
    scores = jnp.einsum(
        "tkrd,skd->krts", grouped, every_key, preferred_element_type=jnp.float32
    ) * head_size ** (-0.5)
    scores = jnp.where(allowed[None, None], scores, jnp.float32(-1e30))
    top = jnp.max(scores, axis=-1, keepdims=True)
    weights = jnp.exp(scores - top)
    total = jnp.sum(weights, axis=-1)
    numer = jnp.einsum(
        "krts,skd->tkrd",
        weights.astype(jnp.bfloat16),
        every_value,
        preferred_element_type=jnp.float32,
    )
    result = numer / jnp.transpose(total, (2, 0, 1))[..., None]
    return result.reshape(count, -1).astype(jnp.bfloat16)


SIDE = 4


def group_of(first, a_coord, b_coord):
    return b_coord * SIDE + a_coord if first == "gz" else a_coord * SIDE + b_coord


def ring_send(value, axis, step):
    return lax.ppermute(value, axis, [(i, (i + step) % SIDE) for i in range(SIDE)])


def ring_collect(local, first):
    return jnp.concatenate([local] + [ring_send(local, first, step) for step in range(1, SIDE)])


def route(held, per_owner, wanted, first, second):
    coords = {"gx": lax.axis_index("gx"), "gz": lax.axis_index("gz")}
    own_a, own_b = coords[first], coords[second]
    slots = wanted.shape[1]
    me = group_of(first, own_a, own_b)
    askers = group_of(first, own_a, (own_b + jnp.arange(SIDE)) % SIDE)
    owner = wanted // per_owner
    owner_a = (owner // SIDE, owner % SIDE)[first == "gz"]
    owner_b = (owner // SIDE, owner % SIDE)[second == "gz"]
    source = ((own_a - owner_a[askers]) % SIDE) * per_owner + (wanted % per_owner)[askers]
    outgoing = jnp.take(held, source.reshape(-1), axis=0, mode="clip")
    received = jnp.concatenate(
        [outgoing[:slots]]
        + [
            ring_send(outgoing[step * slots:(step + 1) * slots], second, step)
            for step in range(1, SIDE)
        ]
    )
    pick = ((own_b - owner_b[me]) % SIDE) * slots + jnp.arange(slots)
    return jnp.take(received, pick, axis=0, mode="clip")


def pack_with_adapters(blocks, adapters):
    rows, lanes = blocks.shape[1], blocks.shape[2]
    pieces = adapters.shape[0]
    flat = adapters.reshape(pieces, -1)
    padded = jnp.pad(flat, ((0, 0), (0, (rows // pieces) * lanes - flat.shape[1])))
    return jnp.concatenate([blocks, padded.reshape(1, rows, lanes)])


def route_with_adapters(held, blocks, adapters, block_wanted, adapter_wanted, first, second):
    coords = {"gx": lax.axis_index("gx"), "gz": lax.axis_index("gz")}
    own_a, own_b = coords[first], coords[second]
    rows, lanes = blocks.shape[1], blocks.shape[2]
    pieces = adapters.shape[0]
    tile = rows // pieces
    flat = adapters.reshape(pieces, -1)
    per_block = blocks.shape[0] + 1
    held = held.reshape(-1, tile, lanes)
    me = group_of(first, own_a, own_b)
    askers = group_of(first, own_a, (own_b + jnp.arange(SIDE)) % SIDE)

    def owners(wanted, per_owner):
        owner = wanted // per_owner
        owner_a = (owner // SIDE, owner % SIDE)[first == "gz"]
        owner_b = (owner // SIDE, owner % SIDE)[second == "gz"]
        return owner_a, owner_b, wanted % per_owner

    block_a, block_b, block_part = owners(block_wanted, blocks.shape[0])
    adapter_a, adapter_b, adapter_part = owners(adapter_wanted, pieces)
    quarter = jnp.arange(pieces)
    block_items = (
        (((own_a - block_a[askers]) % SIDE) * per_block + block_part[askers]) * pieces
    )[..., None] + quarter
    adapter_items = (
        ((own_a - adapter_a[askers]) % SIDE) * per_block + per_block - 1
    ) * pieces + adapter_part[askers]
    source = jnp.concatenate(
        [block_items.reshape(SIDE, -1), adapter_items.reshape(SIDE, -1)], axis=1
    )
    width = source.shape[1]
    outgoing = jnp.take(held, source.reshape(-1), axis=0, mode="clip")
    received = jnp.concatenate(
        [outgoing[:width]]
        + [
            ring_send(outgoing[step * width:(step + 1) * width], second, step)
            for step in range(1, SIDE)
        ]
    )
    slots = block_wanted.shape[1]
    slot = jnp.arange(slots)
    block_pick = (
        (((own_b - block_b[me]) % SIDE) * width + slot * pieces)[:, None] + quarter
    ).reshape(-1)
    adapter_pick = ((own_b - adapter_b[me]) % SIDE) * width + slots * pieces + slot
    chosen_blocks = jnp.take(received, block_pick, axis=0, mode="clip").reshape(
        slots, rows, lanes
    )
    chosen_adapters = jnp.take(received, adapter_pick, axis=0, mode="clip").reshape(slots, -1)
    chosen_adapters = chosen_adapters[:, : flat.shape[1]].reshape(slots, *adapters.shape[1:])
    return chosen_blocks, chosen_adapters


def on_device(
    stream,
    prenorm_gain,
    query_weight,
    key_weight,
    value_weight,
    output_weight,
    adapter_down_rows,
    adapter_up_query,
    request_adapter,
    adapter_row_index,
    request_token_length,
    continues_previous,
    request_cache_block,
    cached_length,
    cached_rotated_keys,
    cached_value_rows,
):
    count = stream.shape[0]
    group_at = lax.axis_index(("gx", "gz"))
    wanted = adapter_row_index[request_adapter]
    down_width = adapter_down_rows.shape[2]
    adapters = jnp.concatenate([adapter_down_rows, adapter_up_query], axis=2)
    held_keys = ring_collect(pack_with_adapters(cached_rotated_keys, adapters), "gz")
    held_values = ring_collect(cached_value_rows, "gx")
    whole = lax.all_gather(stream, ("my", "mc"), axis=1, tiled=True)
    held_keys, held_values, whole = lax.optimization_barrier((held_keys, held_values, whole))
    cache_keys, chosen = route_with_adapters(
        held_keys, cached_rotated_keys, adapters, request_cache_block, wanted, "gz", "gx"
    )
    cache_values = route(
        held_values, cached_value_rows.shape[0], request_cache_block, "gx", "gz"
    )
    chosen_down = chosen[:, :, :down_width]
    chosen_up = chosen[:, :, down_width:]
    model_count = lax.axis_size(("my", "mc"))
    spread = lax.all_to_all(
        jnp.broadcast_to(chosen_down, (model_count, *chosen_down.shape)),
        ("my", "mc"),
        0,
        0,
        tiled=True,
    )
    full_down = jnp.moveaxis(spread, 0, 2).reshape(
        *chosen_down.shape[:2], model_count * down_width
    )

    wide = whole.astype(jnp.float32)
    normalized_input = (
        wide * lax.rsqrt(jnp.mean(wide * wide, axis=1, keepdims=True) + 1e-06) * prenorm_gain
    ).astype(jnp.bfloat16)
    before = jnp.maximum(group_at - 1, 0)
    lengths = request_token_length[group_at]
    cached = cached_length[group_at]
    split_flag = continues_previous[group_at]
    prev_len = request_token_length[before, REQS - 1]
    member, request, position = layout(lengths, cached, split_flag, prev_len, count)
    rank_index = adapter_down_rows.shape[1]
    low = jnp.einsum(
        "td,rkd->trk", normalized_input, full_down, preferred_element_type=jnp.float32
    ).reshape(count, REQS * rank_index).astype(jnp.bfloat16)
    own_columns = jnp.repeat(member, rank_index, axis=1).astype(jnp.bfloat16)
    query_update = jnp.dot(
        low * own_columns,
        chosen_up.reshape(REQS * rank_index, -1),
        preferred_element_type=jnp.float32,
    )
    query_vectors = (
        jnp.dot(normalized_input, query_weight, preferred_element_type=jnp.float32)
        + adapter_scale * query_update
    )
    query_vectors = rotate(query_vectors, position, HEAD_WIDTH).astype(jnp.bfloat16)
    keys = rotate(
        jnp.dot(normalized_input, key_weight, preferred_element_type=jnp.float32),
        position,
        HEAD_WIDTH,
    ).astype(jnp.bfloat16)
    values = jnp.dot(normalized_input, value_weight, preferred_element_type=jnp.float32).astype(
        jnp.bfloat16
    )
    prev_both = shifted(jnp.concatenate([keys, values], axis=1), ("gx", "gz"), 1)
    prev_keys, prev_values = prev_both[:, : keys.shape[1]], prev_both[:, keys.shape[1]:]
    attended = attend(
        query_vectors,
        keys,
        values,
        prev_keys,
        prev_values,
        cache_keys,
        cache_values,
        request,
        cached,
        split_flag,
        prev_len,
        HEAD_WIDTH,
    )
    partial_out = jnp.dot(attended, output_weight, preferred_element_type=jnp.float32)
    return lax.psum_scatter(
        partial_out.astype(jnp.bfloat16), ("my", "mc"), scatter_dimension=1, tiled=True
    )


def solution(mesh):
    split = Mesh(mesh.devices.reshape(SIDE, SIDE, 4, 2), ("gx", "gz", "my", "mc"))
    groups = ("gx", "gz")
    model = ("my", "mc")
    placed = (
        P(groups, model),
        P(),
        P(None, model),
        P(None, model),
        P(None, model),
        P(model, None),
        P(groups, None, model),
        P(groups, None, model),
        P(),
        P(),
        P(),
        P(),
        P(),
        P(),
        P(groups, None, model),
        P(groups, None, model),
    )
    return jax.shard_map(
        on_device, mesh=split, in_specs=placed, out_specs=P(groups, model), check_vma=False
    )
```

```python
import jax
import jax.numpy as jnp
from jax import lax
from jax.sharding import Mesh, PartitionSpec as P

HEAD_WIDTH = 256
REQS = 4


adapter_scale = 2.0


def shifted(value, axis, steps):
    count = lax.axis_size(axis)
    first, last = (max(0, -steps), min(count, count - steps))
    return lax.ppermute(value, axis, [(source, source + steps) for source in range(first, last)])


def rotate(values, position, head_size):
    count = values.shape[0]
    shaped = values.reshape(count, -1, head_size)
    half = head_size // 2
    freq = 10000.0 ** (-jnp.arange(half, dtype=jnp.float32) / half)
    angle = position[:, None, None] * freq[None, None, :]
    cosine = jnp.cos(angle)
    sine = jnp.sin(angle)
    first = shaped[..., :half]
    second = shaped[..., half:]
    turned = jnp.concatenate(
        [first * cosine - second * sine, second * cosine + first * sine], axis=-1
    )
    return turned.reshape(count, -1)


def layout(lengths, cached, split_flag, prev_len, count):
    ends = jnp.cumsum(lengths)
    starts = ends - lengths
    place = jnp.arange(count, dtype=jnp.int32)
    member = ((place[:, None] >= starts[None, :]) & (place[:, None] < ends[None, :])).astype(
        jnp.int32
    )
    request = jnp.sum(member * jnp.arange(lengths.shape[0], dtype=jnp.int32)[None, :], axis=1)
    offset = place - jnp.sum(member * starts[None, :], axis=1)
    extra = jnp.where(request == 0, split_flag * prev_len, 0)
    position = jnp.sum(member * cached[None, :], axis=1) + extra + offset
    return (member, request, position.astype(jnp.float32))


def attend(
    query_vectors,
    keys,
    values,
    prev_keys,
    prev_values,
    cache_keys,
    cache_values,
    request,
    cached,
    split_flag,
    prev_len,
    head_size,
):
    count = query_vectors.shape[0]
    kv_heads = keys.shape[1] // head_size
    ratio = query_vectors.shape[1] // keys.shape[1]
    block = cache_keys.shape[1]
    slots = cache_keys.shape[0] * block
    every_key = jnp.concatenate([cache_keys.reshape(slots, -1), prev_keys, keys], 0).reshape(
        -1, kv_heads, head_size
    )
    every_value = jnp.concatenate(
        [cache_values.reshape(slots, -1), prev_values, values], 0
    ).reshape(-1, kv_heads, head_size)
    slot_req = jnp.arange(slots, dtype=jnp.int32) // block
    slot_col = jnp.arange(slots, dtype=jnp.int32) % block
    cache_ok = (request[:, None] == slot_req[None, :]) & (
        slot_col[None, :] < cached[slot_req][None, :]
    )
    place = jnp.arange(count, dtype=jnp.int32)
    prev_ok = (split_flag == 1) & (request[:, None] == 0) & (place[None, :] >= count - prev_len)
    own_ok = (request[:, None] == request[None, :]) & (place[None, :] <= place[:, None])
    allowed = jnp.concatenate([cache_ok, prev_ok, own_ok], 1)
    grouped = query_vectors.reshape(count, kv_heads, ratio, head_size)
    scores = jnp.einsum(
        "tkrd,skd->krts", grouped, every_key, preferred_element_type=jnp.float32
    ) * head_size ** (-0.5)
    scores = jnp.where(allowed[None, None], scores, jnp.float32(-1e30))
    top = jnp.max(scores, axis=-1, keepdims=True)
    weights = jnp.exp(scores - top)
    total = jnp.sum(weights, axis=-1)
    numer = jnp.einsum(
        "krts,skd->tkrd",
        weights.astype(jnp.bfloat16),
        every_value,
        preferred_element_type=jnp.float32,
    )
    result = numer / jnp.transpose(total, (2, 0, 1))[..., None]
    return result.reshape(count, -1).astype(jnp.bfloat16)


SIDE = 4


def group_of(first, a_coord, b_coord):
    return b_coord * SIDE + a_coord if first == "gz" else a_coord * SIDE + b_coord


def ring_send(value, axis, step):
    return lax.ppermute(value, axis, [(i, (i + step) % SIDE) for i in range(SIDE)])


def route(local, wanted, first, second):
    coords = {"gx": lax.axis_index("gx"), "gz": lax.axis_index("gz")}
    own_a, own_b = coords[first], coords[second]
    per_owner = local.shape[0]
    slots = wanted.shape[1]
    held = jnp.concatenate([local] + [ring_send(local, first, step) for step in range(1, SIDE)])
    me = group_of(first, own_a, own_b)
    askers = group_of(first, own_a, (own_b + jnp.arange(SIDE)) % SIDE)
    owner = wanted // per_owner
    owner_a = (owner // SIDE, owner % SIDE)[first == "gz"]
    owner_b = (owner // SIDE, owner % SIDE)[second == "gz"]
    source = ((own_a - owner_a[askers]) % SIDE) * per_owner + (wanted % per_owner)[askers]
    outgoing = jnp.take(held, source.reshape(-1), axis=0, mode="clip")
    received = jnp.concatenate(
        [outgoing[:slots]]
        + [
            ring_send(outgoing[step * slots:(step + 1) * slots], second, step)
            for step in range(1, SIDE)
        ]
    )
    pick = ((own_b - owner_b[me]) % SIDE) * slots + jnp.arange(slots)
    return jnp.take(received, pick, axis=0, mode="clip")


def route_with_adapters(blocks, adapters, block_wanted, adapter_wanted, first, second):
    coords = {"gx": lax.axis_index("gx"), "gz": lax.axis_index("gz")}
    own_a, own_b = coords[first], coords[second]
    rows, lanes = blocks.shape[1], blocks.shape[2]
    pieces = adapters.shape[0]
    tile = rows // pieces
    flat = adapters.reshape(pieces, -1)
    padded = jnp.pad(flat, ((0, 0), (0, tile * lanes - flat.shape[1])))
    local = jnp.concatenate([blocks, padded.reshape(1, rows, lanes)])
    per_block = local.shape[0]
    held = jnp.concatenate([local] + [ring_send(local, first, step) for step in range(1, SIDE)])
    held = held.reshape(-1, tile, lanes)
    me = group_of(first, own_a, own_b)
    askers = group_of(first, own_a, (own_b + jnp.arange(SIDE)) % SIDE)

    def owners(wanted, per_owner):
        owner = wanted // per_owner
        owner_a = (owner // SIDE, owner % SIDE)[first == "gz"]
        owner_b = (owner // SIDE, owner % SIDE)[second == "gz"]
        return owner_a, owner_b, wanted % per_owner

    block_a, block_b, block_part = owners(block_wanted, blocks.shape[0])
    adapter_a, adapter_b, adapter_part = owners(adapter_wanted, pieces)
    quarter = jnp.arange(pieces)
    block_items = (
        (((own_a - block_a[askers]) % SIDE) * per_block + block_part[askers]) * pieces
    )[..., None] + quarter
    adapter_items = (
        ((own_a - adapter_a[askers]) % SIDE) * per_block + per_block - 1
    ) * pieces + adapter_part[askers]
    source = jnp.concatenate(
        [block_items.reshape(SIDE, -1), adapter_items.reshape(SIDE, -1)], axis=1
    )
    width = source.shape[1]
    outgoing = jnp.take(held, source.reshape(-1), axis=0, mode="clip")
    received = jnp.concatenate(
        [outgoing[:width]]
        + [
            ring_send(outgoing[step * width:(step + 1) * width], second, step)
            for step in range(1, SIDE)
        ]
    )
    slots = block_wanted.shape[1]
    slot = jnp.arange(slots)
    block_pick = (
        (((own_b - block_b[me]) % SIDE) * width + slot * pieces)[:, None] + quarter
    ).reshape(-1)
    adapter_pick = ((own_b - adapter_b[me]) % SIDE) * width + slots * pieces + slot
    chosen_blocks = jnp.take(received, block_pick, axis=0, mode="clip").reshape(
        slots, rows, lanes
    )
    chosen_adapters = jnp.take(received, adapter_pick, axis=0, mode="clip").reshape(slots, -1)
    chosen_adapters = chosen_adapters[:, : flat.shape[1]].reshape(slots, *adapters.shape[1:])
    return chosen_blocks, chosen_adapters


def scatter_model(partial):
    count, width = partial.shape
    piece = width // (2 * SIDE)
    chip_at, core_at = lax.axis_index("my"), lax.axis_index("mc")
    blocks = partial.astype(jnp.bfloat16).reshape(count, SIDE, 2, piece)
    mine = jnp.take(blocks, core_at, axis=2, mode="clip")
    theirs = jnp.take(blocks, 1 - core_at, axis=2, mode="clip")
    got = lax.ppermute(theirs, "mc", [(0, 1), (1, 0)])
    summed = (mine.astype(jnp.float32) + got.astype(jnp.float32)).astype(jnp.bfloat16)
    total = jnp.take(summed, chip_at, axis=1, mode="clip").astype(jnp.float32)
    for step in range(1, SIDE):
        send = jnp.take(summed, (chip_at + step) % SIDE, axis=1, mode="clip")
        total = total + ring_send(send, "my", step).astype(jnp.float32)
    return total.astype(jnp.bfloat16)


def on_device(
    stream,
    prenorm_gain,
    query_weight,
    key_weight,
    value_weight,
    output_weight,
    adapter_down_rows,
    adapter_up_query,
    request_adapter,
    adapter_row_index,
    request_token_length,
    continues_previous,
    request_cache_block,
    cached_length,
    cached_rotated_keys,
    cached_value_rows,
):
    count = stream.shape[0]
    group_at = lax.axis_index(("gx", "gz"))
    wanted = adapter_row_index[request_adapter]
    down_width = adapter_down_rows.shape[2]
    adapters = jnp.concatenate([adapter_down_rows, adapter_up_query], axis=2)
    cache_keys, chosen = route_with_adapters(
        cached_rotated_keys, adapters, request_cache_block, wanted, "gz", "gx"
    )
    cache_values = route(cached_value_rows, request_cache_block, "gx", "gz")
    chosen_down = chosen[:, :, :down_width]
    chosen_up = chosen[:, :, down_width:]
    model_count = lax.axis_size(("my", "mc"))
    spread = lax.all_to_all(
        jnp.broadcast_to(chosen_down, (model_count, *chosen_down.shape)),
        ("my", "mc"),
        0,
        0,
        tiled=True,
    )
    full_down = jnp.moveaxis(spread, 0, 2).reshape(
        *chosen_down.shape[:2], model_count * down_width
    )

    whole = lax.all_gather(stream, ("my", "mc"), axis=1, tiled=True)
    wide = whole.astype(jnp.float32)
    normalized_input = (
        wide * lax.rsqrt(jnp.mean(wide * wide, axis=1, keepdims=True) + 1e-06) * prenorm_gain
    ).astype(jnp.bfloat16)
    before = jnp.maximum(group_at - 1, 0)
    lengths = request_token_length[group_at]
    cached = cached_length[group_at]
    split_flag = continues_previous[group_at]
    prev_len = request_token_length[before, REQS - 1]
    member, request, position = layout(lengths, cached, split_flag, prev_len, count)
    rank_index = adapter_down_rows.shape[1]
    low = jnp.einsum(
        "td,rkd->trk", normalized_input, full_down, preferred_element_type=jnp.float32
    ).reshape(count, REQS * rank_index).astype(jnp.bfloat16)
    own_columns = jnp.repeat(member, rank_index, axis=1).astype(jnp.bfloat16)
    query_update = jnp.dot(
        low * own_columns,
        chosen_up.reshape(REQS * rank_index, -1),
        preferred_element_type=jnp.float32,
    )
    query_vectors = (
        jnp.dot(normalized_input, query_weight, preferred_element_type=jnp.float32)
        + adapter_scale * query_update
    )
    query_vectors = rotate(query_vectors, position, HEAD_WIDTH).astype(jnp.bfloat16)
    keys = rotate(
        jnp.dot(normalized_input, key_weight, preferred_element_type=jnp.float32),
        position,
        HEAD_WIDTH,
    ).astype(jnp.bfloat16)
    values = jnp.dot(normalized_input, value_weight, preferred_element_type=jnp.float32).astype(
        jnp.bfloat16
    )
    prev_both = shifted(jnp.concatenate([keys, values], axis=1), ("gx", "gz"), 1)
    prev_keys, prev_values = prev_both[:, : keys.shape[1]], prev_both[:, keys.shape[1]:]
    attended = attend(
        query_vectors,
        keys,
        values,
        prev_keys,
        prev_values,
        cache_keys,
        cache_values,
        request,
        cached,
        split_flag,
        prev_len,
        HEAD_WIDTH,
    )
    partial_out = jnp.dot(attended, output_weight, preferred_element_type=jnp.float32)
    return scatter_model(partial_out)


def solution(mesh):
    split = Mesh(mesh.devices.reshape(SIDE, SIDE, 4, 2), ("gx", "gz", "my", "mc"))
    groups = ("gx", "gz")
    model = ("my", "mc")
    placed = (
        P(groups, model),
        P(),
        P(None, model),
        P(None, model),
        P(None, model),
        P(model, None),
        P(groups, None, model),
        P(groups, None, model),
        P(),
        P(),
        P(),
        P(),
        P(),
        P(),
        P(groups, None, model),
        P(groups, None, model),
    )
    return jax.shard_map(
        on_device, mesh=split, in_specs=placed, out_specs=P(groups, model), check_vma=False
    )
```

```python
import jax
import jax.numpy as jnp
from jax import lax
from jax.sharding import Mesh, PartitionSpec as P

HEAD_WIDTH = 256
REQS = 4


adapter_scale = 2.0


def shifted(value, axis, steps):
    count = lax.axis_size(axis)
    first, last = (max(0, -steps), min(count, count - steps))
    return lax.ppermute(value, axis, [(source, source + steps) for source in range(first, last)])


def rotate(values, position, head_size):
    count = values.shape[0]
    shaped = values.reshape(count, -1, head_size)
    half = head_size // 2
    freq = 10000.0 ** (-jnp.arange(half, dtype=jnp.float32) / half)
    angle = position[:, None, None] * freq[None, None, :]
    cosine = jnp.cos(angle)
    sine = jnp.sin(angle)
    first = shaped[..., :half]
    second = shaped[..., half:]
    turned = jnp.concatenate(
        [first * cosine - second * sine, second * cosine + first * sine], axis=-1
    )
    return turned.reshape(count, -1)


def layout(lengths, cached, split_flag, prev_len, count):
    ends = jnp.cumsum(lengths)
    starts = ends - lengths
    place = jnp.arange(count, dtype=jnp.int32)
    member = ((place[:, None] >= starts[None, :]) & (place[:, None] < ends[None, :])).astype(
        jnp.int32
    )
    request = jnp.sum(member * jnp.arange(lengths.shape[0], dtype=jnp.int32)[None, :], axis=1)
    offset = place - jnp.sum(member * starts[None, :], axis=1)
    extra = jnp.where(request == 0, split_flag * prev_len, 0)
    position = jnp.sum(member * cached[None, :], axis=1) + extra + offset
    return (member, request, position.astype(jnp.float32))


def attend(
    query_vectors,
    keys,
    values,
    prev_keys,
    prev_values,
    cache_keys,
    cache_values,
    request,
    cached,
    split_flag,
    prev_len,
    head_size,
):
    count = query_vectors.shape[0]
    kv_heads = keys.shape[1] // head_size
    ratio = query_vectors.shape[1] // keys.shape[1]
    block = cache_keys.shape[1]
    slots = cache_keys.shape[0] * block
    every_key = jnp.concatenate([cache_keys.reshape(slots, -1), prev_keys, keys], 0).reshape(
        -1, kv_heads, head_size
    )
    every_value = jnp.concatenate(
        [cache_values.reshape(slots, -1), prev_values, values], 0
    ).reshape(-1, kv_heads, head_size)
    slot_req = jnp.arange(slots, dtype=jnp.int32) // block
    slot_col = jnp.arange(slots, dtype=jnp.int32) % block
    cache_ok = (request[:, None] == slot_req[None, :]) & (
        slot_col[None, :] < cached[slot_req][None, :]
    )
    place = jnp.arange(count, dtype=jnp.int32)
    prev_ok = (split_flag == 1) & (request[:, None] == 0) & (place[None, :] >= count - prev_len)
    own_ok = (request[:, None] == request[None, :]) & (place[None, :] <= place[:, None])
    allowed = jnp.concatenate([cache_ok, prev_ok, own_ok], 1)
    grouped = query_vectors.reshape(count, kv_heads, ratio, head_size)
    scores = jnp.einsum(
        "tkrd,skd->krts", grouped, every_key, preferred_element_type=jnp.float32
    ) * head_size ** (-0.5)
    scores = jnp.where(allowed[None, None], scores, jnp.float32(-1e30))
    top = jnp.max(scores, axis=-1, keepdims=True)
    weights = jnp.exp(scores - top)
    total = jnp.sum(weights, axis=-1)
    numer = jnp.einsum(
        "krts,skd->tkrd",
        weights.astype(jnp.bfloat16),
        every_value,
        preferred_element_type=jnp.float32,
    )
    result = numer / jnp.transpose(total, (2, 0, 1))[..., None]
    return result.reshape(count, -1).astype(jnp.bfloat16)


SIDE = 4


def group_of(first, a_coord, b_coord):
    return b_coord * SIDE + a_coord if first == "gz" else a_coord * SIDE + b_coord


def ring_send(value, axis, step):
    return lax.ppermute(value, axis, [(i, (i + step) % SIDE) for i in range(SIDE)])


def route(local, wanted, first, second):
    coords = {"gx": lax.axis_index("gx"), "gz": lax.axis_index("gz")}
    own_a, own_b = coords[first], coords[second]
    per_owner = local.shape[0]
    slots = wanted.shape[1]
    held = lax.all_gather(local, first, axis=0, tiled=True)
    me = group_of(first, own_a, own_b)
    askers = group_of(first, own_a, (own_b + jnp.arange(SIDE)) % SIDE)
    owner = wanted // per_owner
    owner_a = (owner // SIDE, owner % SIDE)[first == "gz"]
    owner_b = (owner // SIDE, owner % SIDE)[second == "gz"]
    source = owner_a[askers] * per_owner + (wanted % per_owner)[askers]
    outgoing = jnp.take(held, source.reshape(-1), axis=0, mode="clip")
    received = jnp.concatenate(
        [outgoing[:slots]]
        + [
            ring_send(outgoing[step * slots:(step + 1) * slots], second, step)
            for step in range(1, SIDE)
        ]
    )
    pick = ((own_b - owner_b[me]) % SIDE) * slots + jnp.arange(slots)
    return jnp.take(received, pick, axis=0, mode="clip")


def route_with_adapters(blocks, adapters, block_wanted, adapter_wanted, first, second):
    coords = {"gx": lax.axis_index("gx"), "gz": lax.axis_index("gz")}
    own_a, own_b = coords[first], coords[second]
    rows, lanes = blocks.shape[1], blocks.shape[2]
    pieces = adapters.shape[0]
    tile = rows // pieces
    flat = adapters.reshape(pieces, -1)
    padded = jnp.pad(flat, ((0, 0), (0, tile * lanes - flat.shape[1])))
    local = jnp.concatenate([blocks, padded.reshape(1, rows, lanes)])
    per_block = local.shape[0]
    held = jnp.concatenate([local] + [ring_send(local, first, step) for step in range(1, SIDE)])
    held = held.reshape(-1, tile, lanes)
    me = group_of(first, own_a, own_b)
    askers = group_of(first, own_a, (own_b + jnp.arange(SIDE)) % SIDE)

    def owners(wanted, per_owner):
        owner = wanted // per_owner
        owner_a = (owner // SIDE, owner % SIDE)[first == "gz"]
        owner_b = (owner // SIDE, owner % SIDE)[second == "gz"]
        return owner_a, owner_b, wanted % per_owner

    block_a, block_b, block_part = owners(block_wanted, blocks.shape[0])
    adapter_a, adapter_b, adapter_part = owners(adapter_wanted, pieces)
    quarter = jnp.arange(pieces)
    block_items = (
        (((own_a - block_a[askers]) % SIDE) * per_block + block_part[askers]) * pieces
    )[..., None] + quarter
    adapter_items = (
        ((own_a - adapter_a[askers]) % SIDE) * per_block + per_block - 1
    ) * pieces + adapter_part[askers]
    source = jnp.concatenate(
        [block_items.reshape(SIDE, -1), adapter_items.reshape(SIDE, -1)], axis=1
    )
    width = source.shape[1]
    outgoing = jnp.take(held, source.reshape(-1), axis=0, mode="clip")
    received = jnp.concatenate(
        [outgoing[:width]]
        + [
            ring_send(outgoing[step * width:(step + 1) * width], second, step)
            for step in range(1, SIDE)
        ]
    )
    slots = block_wanted.shape[1]
    slot = jnp.arange(slots)
    block_pick = (
        (((own_b - block_b[me]) % SIDE) * width + slot * pieces)[:, None] + quarter
    ).reshape(-1)
    adapter_pick = ((own_b - adapter_b[me]) % SIDE) * width + slots * pieces + slot
    chosen_blocks = jnp.take(received, block_pick, axis=0, mode="clip").reshape(
        slots, rows, lanes
    )
    chosen_adapters = jnp.take(received, adapter_pick, axis=0, mode="clip").reshape(slots, -1)
    chosen_adapters = chosen_adapters[:, : flat.shape[1]].reshape(slots, *adapters.shape[1:])
    return chosen_blocks, chosen_adapters


def on_device(
    stream,
    prenorm_gain,
    query_weight,
    key_weight,
    value_weight,
    output_weight,
    adapter_down_rows,
    adapter_up_query,
    request_adapter,
    adapter_row_index,
    request_token_length,
    continues_previous,
    request_cache_block,
    cached_length,
    cached_rotated_keys,
    cached_value_rows,
):
    count = stream.shape[0]
    group_at = lax.axis_index(("gx", "gz"))
    wanted = adapter_row_index[request_adapter]
    down_width = adapter_down_rows.shape[2]
    adapters = jnp.concatenate([adapter_down_rows, adapter_up_query], axis=2)
    cache_keys, chosen = route_with_adapters(
        cached_rotated_keys, adapters, request_cache_block, wanted, "gz", "gx"
    )
    cache_values = route(cached_value_rows, request_cache_block, "gx", "gz")
    chosen_down = chosen[:, :, :down_width]
    chosen_up = chosen[:, :, down_width:]
    model_count = lax.axis_size(("my", "mc"))
    spread = lax.all_to_all(
        jnp.broadcast_to(chosen_down, (model_count, *chosen_down.shape)),
        ("my", "mc"),
        0,
        0,
        tiled=True,
    )
    full_down = jnp.moveaxis(spread, 0, 2).reshape(
        *chosen_down.shape[:2], model_count * down_width
    )

    whole = lax.all_gather(stream, ("my", "mc"), axis=1, tiled=True)
    wide = whole.astype(jnp.float32)
    normalized_input = (
        wide * lax.rsqrt(jnp.mean(wide * wide, axis=1, keepdims=True) + 1e-06) * prenorm_gain
    ).astype(jnp.bfloat16)
    before = jnp.maximum(group_at - 1, 0)
    lengths = request_token_length[group_at]
    cached = cached_length[group_at]
    split_flag = continues_previous[group_at]
    prev_len = request_token_length[before, REQS - 1]
    member, request, position = layout(lengths, cached, split_flag, prev_len, count)
    rank_index = adapter_down_rows.shape[1]
    low = jnp.einsum(
        "td,rkd->trk", normalized_input, full_down, preferred_element_type=jnp.float32
    ).reshape(count, REQS * rank_index).astype(jnp.bfloat16)
    own_columns = jnp.repeat(member, rank_index, axis=1).astype(jnp.bfloat16)
    query_update = jnp.dot(
        low * own_columns,
        chosen_up.reshape(REQS * rank_index, -1),
        preferred_element_type=jnp.float32,
    )
    query_vectors = (
        jnp.dot(normalized_input, query_weight, preferred_element_type=jnp.float32)
        + adapter_scale * query_update
    )
    query_vectors = rotate(query_vectors, position, HEAD_WIDTH).astype(jnp.bfloat16)
    keys = rotate(
        jnp.dot(normalized_input, key_weight, preferred_element_type=jnp.float32),
        position,
        HEAD_WIDTH,
    ).astype(jnp.bfloat16)
    values = jnp.dot(normalized_input, value_weight, preferred_element_type=jnp.float32).astype(
        jnp.bfloat16
    )
    prev_both = shifted(jnp.concatenate([keys, values], axis=1), ("gx", "gz"), 1)
    prev_keys, prev_values = prev_both[:, : keys.shape[1]], prev_both[:, keys.shape[1]:]
    attended = attend(
        query_vectors,
        keys,
        values,
        prev_keys,
        prev_values,
        cache_keys,
        cache_values,
        request,
        cached,
        split_flag,
        prev_len,
        HEAD_WIDTH,
    )
    partial_out = jnp.dot(attended, output_weight, preferred_element_type=jnp.float32)
    return lax.psum_scatter(
        partial_out.astype(jnp.bfloat16), ("my", "mc"), scatter_dimension=1, tiled=True
    )


def solution(mesh):
    split = Mesh(mesh.devices.reshape(SIDE, SIDE, 4, 2), ("gx", "gz", "my", "mc"))
    groups = ("gx", "gz")
    model = ("my", "mc")
    placed = (
        P(groups, model),
        P(),
        P(None, model),
        P(None, model),
        P(None, model),
        P(model, None),
        P(groups, None, model),
        P(groups, None, model),
        P(),
        P(),
        P(),
        P(),
        P(),
        P(),
        P(groups, None, model),
        P(groups, None, model),
    )
    return jax.shard_map(
        on_device, mesh=split, in_specs=placed, out_specs=P(groups, model), check_vma=False
    )
```

```python
import jax
import jax.numpy as jnp
from jax import lax
from jax.sharding import Mesh, PartitionSpec as P

HEAD_WIDTH = 256
REQS = 4
MOSTLEN = 256


adapter_scale = 2.0


def shifted(value, axis, steps):
    count = lax.axis_size(axis)
    first, last = (max(0, -steps), min(count, count - steps))
    return lax.ppermute(value, axis, [(source, source + steps) for source in range(first, last)])


def rotate(values, position, head_size):
    count = values.shape[0]
    shaped = values.reshape(count, -1, head_size)
    half = head_size // 2
    freq = 10000.0 ** (-jnp.arange(half, dtype=jnp.float32) / half)
    angle = position[:, None, None] * freq[None, None, :]
    cosine = jnp.cos(angle)
    sine = jnp.sin(angle)
    first = shaped[..., :half]
    second = shaped[..., half:]
    turned = jnp.concatenate(
        [first * cosine - second * sine, second * cosine + first * sine], axis=-1
    )
    return turned.reshape(count, -1)


def layout(lengths, cached, split_flag, prev_len, count):
    ends = jnp.cumsum(lengths)
    starts = ends - lengths
    place = jnp.arange(count, dtype=jnp.int32)
    member = ((place[:, None] >= starts[None, :]) & (place[:, None] < ends[None, :])).astype(
        jnp.int32
    )
    request = jnp.sum(member * jnp.arange(lengths.shape[0], dtype=jnp.int32)[None, :], axis=1)
    offset = place - jnp.sum(member * starts[None, :], axis=1)
    extra = jnp.where(request == 0, split_flag * prev_len, 0)
    position = jnp.sum(member * cached[None, :], axis=1) + extra + offset
    return (member, request, position.astype(jnp.float32))


def attend(
    query_vectors,
    keys,
    values,
    prev_keys,
    prev_values,
    cache_keys,
    cache_values,
    request,
    cached,
    split_flag,
    prev_len,
    head_size,
):
    count = query_vectors.shape[0]
    kv_heads = keys.shape[1] // head_size
    ratio = query_vectors.shape[1] // keys.shape[1]
    block = cache_keys.shape[1]
    slots = cache_keys.shape[0] * block
    every_key = jnp.concatenate([cache_keys.reshape(slots, -1), prev_keys, keys], 0).reshape(
        -1, kv_heads, head_size
    )
    every_value = jnp.concatenate(
        [cache_values.reshape(slots, -1), prev_values, values], 0
    ).reshape(-1, kv_heads, head_size)
    owned = jnp.arange(cache_keys.shape[0], dtype=jnp.int32)
    cache_ok = (
        (request[:, None, None] == owned[None, :, None])
        & (jnp.arange(block, dtype=jnp.int32)[None, None, :] < cached[None, :, None])
    ).reshape(count, slots)
    place = jnp.arange(count, dtype=jnp.int32)
    kept = jnp.arange(prev_keys.shape[0], dtype=jnp.int32)
    prev_ok = (
        (split_flag == 1)
        & (request[:, None] == 0)
        & (kept[None, :] >= prev_keys.shape[0] - prev_len)
    )
    own_ok = (request[:, None] == request[None, :]) & (place[None, :] <= place[:, None])
    allowed = jnp.concatenate([cache_ok, prev_ok, own_ok], 1)
    grouped = query_vectors.reshape(count, kv_heads, ratio, head_size)
    scores = jnp.einsum(
        "tkrd,skd->krts", grouped, every_key, preferred_element_type=jnp.float32
    ) * head_size ** (-0.5)
    scores = jnp.where(allowed[None, None], scores, jnp.float32(-1e30))
    top = jnp.max(scores, axis=-1, keepdims=True)
    weights = jnp.exp(scores - top)
    total = jnp.sum(weights, axis=-1)
    numer = jnp.einsum(
        "krts,skd->tkrd",
        weights.astype(jnp.bfloat16),
        every_value,
        preferred_element_type=jnp.float32,
    )
    result = numer / jnp.transpose(total, (2, 0, 1))[..., None]
    return result.reshape(count, -1).astype(jnp.bfloat16)


SIDE = 4


def group_of(first, a_coord, b_coord):
    return b_coord * SIDE + a_coord if first == "gz" else a_coord * SIDE + b_coord


def ring_send(value, axis, step):
    return lax.ppermute(value, axis, [(i, (i + step) % SIDE) for i in range(SIDE)])


def route(local, wanted, first, second):
    coords = {"gx": lax.axis_index("gx"), "gz": lax.axis_index("gz")}
    own_a, own_b = coords[first], coords[second]
    per_owner = local.shape[0]
    slots = wanted.shape[1]
    held = jnp.concatenate([local] + [ring_send(local, first, step) for step in range(1, SIDE)])
    me = group_of(first, own_a, own_b)
    askers = group_of(first, own_a, (own_b + jnp.arange(SIDE)) % SIDE)
    owner = wanted // per_owner
    owner_a = (owner // SIDE, owner % SIDE)[first == "gz"]
    owner_b = (owner // SIDE, owner % SIDE)[second == "gz"]
    source = ((own_a - owner_a[askers]) % SIDE) * per_owner + (wanted % per_owner)[askers]
    outgoing = jnp.take(held, source.reshape(-1), axis=0, mode="clip")
    received = jnp.concatenate(
        [outgoing[:slots]]
        + [
            ring_send(outgoing[step * slots:(step + 1) * slots], second, step)
            for step in range(1, SIDE)
        ]
    )
    pick = ((own_b - owner_b[me]) % SIDE) * slots + jnp.arange(slots)
    return jnp.take(received, pick, axis=0, mode="clip")


def route_with_adapters(blocks, adapters, block_wanted, adapter_wanted, first, second):
    coords = {"gx": lax.axis_index("gx"), "gz": lax.axis_index("gz")}
    own_a, own_b = coords[first], coords[second]
    rows, lanes = blocks.shape[1], blocks.shape[2]
    pieces = adapters.shape[0]
    tile = rows // pieces
    flat = adapters.reshape(pieces, -1)
    padded = jnp.pad(flat, ((0, 0), (0, tile * lanes - flat.shape[1])))
    local = jnp.concatenate([blocks, padded.reshape(1, rows, lanes)])
    per_block = local.shape[0]
    held = jnp.concatenate([local] + [ring_send(local, first, step) for step in range(1, SIDE)])
    held = held.reshape(-1, tile, lanes)
    me = group_of(first, own_a, own_b)
    askers = group_of(first, own_a, (own_b + jnp.arange(SIDE)) % SIDE)

    def owners(wanted, per_owner):
        owner = wanted // per_owner
        owner_a = (owner // SIDE, owner % SIDE)[first == "gz"]
        owner_b = (owner // SIDE, owner % SIDE)[second == "gz"]
        return owner_a, owner_b, wanted % per_owner

    block_a, block_b, block_part = owners(block_wanted, blocks.shape[0])
    adapter_a, adapter_b, adapter_part = owners(adapter_wanted, pieces)
    quarter = jnp.arange(pieces)
    block_items = (
        (((own_a - block_a[askers]) % SIDE) * per_block + block_part[askers]) * pieces
    )[..., None] + quarter
    adapter_items = (
        ((own_a - adapter_a[askers]) % SIDE) * per_block + per_block - 1
    ) * pieces + adapter_part[askers]
    source = jnp.concatenate(
        [block_items.reshape(SIDE, -1), adapter_items.reshape(SIDE, -1)], axis=1
    )
    width = source.shape[1]
    outgoing = jnp.take(held, source.reshape(-1), axis=0, mode="clip")
    received = jnp.concatenate(
        [outgoing[:width]]
        + [
            ring_send(outgoing[step * width:(step + 1) * width], second, step)
            for step in range(1, SIDE)
        ]
    )
    slots = block_wanted.shape[1]
    slot = jnp.arange(slots)
    block_pick = (
        (((own_b - block_b[me]) % SIDE) * width + slot * pieces)[:, None] + quarter
    ).reshape(-1)
    adapter_pick = ((own_b - adapter_b[me]) % SIDE) * width + slots * pieces + slot
    chosen_blocks = jnp.take(received, block_pick, axis=0, mode="clip").reshape(
        slots, rows, lanes
    )
    chosen_adapters = jnp.take(received, adapter_pick, axis=0, mode="clip").reshape(slots, -1)
    chosen_adapters = chosen_adapters[:, : flat.shape[1]].reshape(slots, *adapters.shape[1:])
    return chosen_blocks, chosen_adapters


def on_device(
    stream,
    prenorm_gain,
    query_weight,
    key_weight,
    value_weight,
    output_weight,
    adapter_down_rows,
    adapter_up_query,
    request_adapter,
    adapter_row_index,
    request_token_length,
    continues_previous,
    request_cache_block,
    cached_length,
    cached_rotated_keys,
    cached_value_rows,
):
    count = stream.shape[0]
    group_at = lax.axis_index(("gx", "gz"))
    wanted = adapter_row_index[request_adapter]
    down_width = adapter_down_rows.shape[2]
    adapters = jnp.concatenate([adapter_down_rows, adapter_up_query], axis=2)
    cache_keys, chosen = route_with_adapters(
        cached_rotated_keys, adapters, request_cache_block, wanted, "gz", "gx"
    )
    cache_values = route(cached_value_rows, request_cache_block, "gx", "gz")
    chosen_down = chosen[:, :, :down_width]
    chosen_up = chosen[:, :, down_width:]
    model_count = lax.axis_size(("my", "mc"))
    spread = lax.all_to_all(
        jnp.broadcast_to(chosen_down, (model_count, *chosen_down.shape)),
        ("my", "mc"),
        0,
        0,
        tiled=True,
    )
    full_down = jnp.moveaxis(spread, 0, 2).reshape(
        *chosen_down.shape[:2], model_count * down_width
    )

    whole = lax.all_gather(stream, ("my", "mc"), axis=1, tiled=True)
    wide = whole.astype(jnp.float32)
    normalized_input = (
        wide * lax.rsqrt(jnp.mean(wide * wide, axis=1, keepdims=True) + 1e-06) * prenorm_gain
    ).astype(jnp.bfloat16)
    before = jnp.maximum(group_at - 1, 0)
    lengths = request_token_length[group_at]
    cached = cached_length[group_at]
    split_flag = continues_previous[group_at]
    prev_len = request_token_length[before, REQS - 1]
    member, request, position = layout(lengths, cached, split_flag, prev_len, count)
    rank_index = adapter_down_rows.shape[1]
    low = jnp.einsum(
        "td,rkd->trk", normalized_input, full_down, preferred_element_type=jnp.float32
    ).reshape(count, REQS * rank_index).astype(jnp.bfloat16)
    own_columns = jnp.repeat(member, rank_index, axis=1).astype(jnp.bfloat16)
    query_update = jnp.dot(
        low * own_columns,
        chosen_up.reshape(REQS * rank_index, -1),
        preferred_element_type=jnp.float32,
    )
    query_vectors = (
        jnp.dot(normalized_input, query_weight, preferred_element_type=jnp.float32)
        + adapter_scale * query_update
    )
    query_vectors = rotate(query_vectors, position, HEAD_WIDTH).astype(jnp.bfloat16)
    keys = rotate(
        jnp.dot(normalized_input, key_weight, preferred_element_type=jnp.float32),
        position,
        HEAD_WIDTH,
    ).astype(jnp.bfloat16)
    values = jnp.dot(normalized_input, value_weight, preferred_element_type=jnp.float32).astype(
        jnp.bfloat16
    )
    tail = count - MOSTLEN
    prev_both = shifted(jnp.concatenate([keys[tail:], values[tail:]], axis=1), ("gx", "gz"), 1)
    prev_keys, prev_values = prev_both[:, : keys.shape[1]], prev_both[:, keys.shape[1]:]
    attended = attend(
        query_vectors,
        keys,
        values,
        prev_keys,
        prev_values,
        cache_keys,
        cache_values,
        request,
        cached,
        split_flag,
        prev_len,
        HEAD_WIDTH,
    )
    partial_out = jnp.dot(attended, output_weight, preferred_element_type=jnp.float32)
    return lax.psum_scatter(
        partial_out.astype(jnp.bfloat16), ("my", "mc"), scatter_dimension=1, tiled=True
    )


def solution(mesh):
    split = Mesh(mesh.devices.reshape(SIDE, SIDE, 4, 2), ("gx", "gz", "my", "mc"))
    groups = ("gx", "gz")
    model = ("my", "mc")
    placed = (
        P(groups, model),
        P(),
        P(None, model),
        P(None, model),
        P(None, model),
        P(model, None),
        P(groups, None, model),
        P(groups, None, model),
        P(),
        P(),
        P(),
        P(),
        P(),
        P(),
        P(groups, None, model),
        P(groups, None, model),
    )
    return jax.shard_map(
        on_device, mesh=split, in_specs=placed, out_specs=P(groups, model), check_vma=False
    )
```

```python
import jax
import jax.numpy as jnp
from jax import lax
from jax.sharding import Mesh, PartitionSpec as P

HEAD_WIDTH = 256
REQS = 4
MOSTLEN = 256


adapter_scale = 2.0


def shifted(value, axis, steps):
    count = lax.axis_size(axis)
    first, last = (max(0, -steps), min(count, count - steps))
    return lax.ppermute(value, axis, [(source, source + steps) for source in range(first, last)])


def rotate(values, position, head_size):
    count = values.shape[0]
    shaped = values.reshape(count, -1, head_size)
    half = head_size // 2
    freq = 10000.0 ** (-jnp.arange(half, dtype=jnp.float32) / half)
    angle = position[:, None, None] * freq[None, None, :]
    cosine = jnp.cos(angle)
    sine = jnp.sin(angle)
    first = shaped[..., :half]
    second = shaped[..., half:]
    turned = jnp.concatenate(
        [first * cosine - second * sine, second * cosine + first * sine], axis=-1
    )
    return turned.reshape(count, -1)


def layout(lengths, cached, split_flag, prev_len, count):
    ends = jnp.cumsum(lengths)
    starts = ends - lengths
    place = jnp.arange(count, dtype=jnp.int32)
    member = ((place[:, None] >= starts[None, :]) & (place[:, None] < ends[None, :])).astype(
        jnp.int32
    )
    request = jnp.sum(member * jnp.arange(lengths.shape[0], dtype=jnp.int32)[None, :], axis=1)
    offset = place - jnp.sum(member * starts[None, :], axis=1)
    extra = jnp.where(request == 0, split_flag * prev_len, 0)
    position = jnp.sum(member * cached[None, :], axis=1) + extra + offset
    return (member, request, position.astype(jnp.float32))


def attend(
    query_vectors,
    keys,
    values,
    prev_keys,
    prev_values,
    cache_keys,
    cache_values,
    request,
    cached,
    split_flag,
    prev_len,
    head_size,
):
    count = query_vectors.shape[0]
    kv_heads = keys.shape[1] // head_size
    ratio = query_vectors.shape[1] // keys.shape[1]
    block = cache_keys.shape[1]
    slots = cache_keys.shape[0] * block
    every_key = jnp.concatenate([cache_keys.reshape(slots, -1), prev_keys, keys], 0).reshape(
        -1, kv_heads, head_size
    )
    every_value = jnp.concatenate(
        [cache_values.reshape(slots, -1), prev_values, values], 0
    ).reshape(-1, kv_heads, head_size)
    owned = jnp.arange(cache_keys.shape[0], dtype=jnp.int32)
    cache_ok = (
        (request[:, None, None] == owned[None, :, None])
        & (jnp.arange(block, dtype=jnp.int32)[None, None, :] < cached[None, :, None])
    ).reshape(count, slots)
    place = jnp.arange(count, dtype=jnp.int32)
    kept = jnp.arange(prev_keys.shape[0], dtype=jnp.int32)
    prev_ok = (
        (split_flag == 1)
        & (request[:, None] == 0)
        & (kept[None, :] >= prev_keys.shape[0] - prev_len)
    )
    own_ok = (request[:, None] == request[None, :]) & (place[None, :] <= place[:, None])
    allowed = jnp.concatenate([cache_ok, prev_ok, own_ok], 1)
    grouped = query_vectors.reshape(count, kv_heads, ratio, head_size)
    scores = jnp.einsum(
        "tkrd,skd->krts", grouped, every_key, preferred_element_type=jnp.float32
    ) * head_size ** (-0.5)
    scores = jnp.where(allowed[None, None], scores, jnp.float32(-1e30))
    top = jnp.max(scores, axis=-1, keepdims=True)
    weights = jnp.exp(scores - top)
    total = jnp.sum(weights, axis=-1)
    numer = jnp.einsum(
        "krts,skd->tkrd",
        weights.astype(jnp.bfloat16),
        every_value,
        preferred_element_type=jnp.float32,
    )
    result = numer / jnp.transpose(total, (2, 0, 1))[..., None]
    return result.reshape(count, -1).astype(jnp.bfloat16)


SIDE = 4


def group_of(first, a_coord, b_coord):
    return b_coord * SIDE + a_coord if first == "gz" else a_coord * SIDE + b_coord


def ring_send(value, axis, step):
    return lax.ppermute(value, axis, [(i, (i + step) % SIDE) for i in range(SIDE)])


def route(local, wanted, first, second):
    coords = {"gx": lax.axis_index("gx"), "gz": lax.axis_index("gz")}
    own_a, own_b = coords[first], coords[second]
    per_owner = local.shape[0]
    slots = wanted.shape[1]
    held = jnp.concatenate([local] + [ring_send(local, first, step) for step in range(1, SIDE)])
    me = group_of(first, own_a, own_b)
    askers = group_of(first, own_a, (own_b + jnp.arange(SIDE)) % SIDE)
    owner = wanted // per_owner
    owner_a = (owner // SIDE, owner % SIDE)[first == "gz"]
    owner_b = (owner // SIDE, owner % SIDE)[second == "gz"]
    source = ((own_a - owner_a[askers]) % SIDE) * per_owner + (wanted % per_owner)[askers]
    outgoing = jnp.take(held, source.reshape(-1), axis=0, mode="clip")
    pieces = [outgoing[:slots]] + [
        ring_send(outgoing[step * slots:(step + 1) * slots], second, step)
        for step in range(1, SIDE)
    ]
    return pick_piece((own_b - owner_b[me]) % SIDE, pieces)


def pick_piece(came, pieces):
    which = came.reshape(came.shape + (1,) * (pieces[0].ndim - 1))
    return lax.select_n(jnp.broadcast_to(which, pieces[0].shape), *pieces)


def route_with_adapters(blocks, adapters, block_wanted, adapter_wanted, first, second):
    coords = {"gx": lax.axis_index("gx"), "gz": lax.axis_index("gz")}
    own_a, own_b = coords[first], coords[second]
    rows, lanes = blocks.shape[1], blocks.shape[2]
    pieces = adapters.shape[0]
    tile = rows // pieces
    flat = adapters.reshape(pieces, -1)
    padded = jnp.pad(flat, ((0, 0), (0, tile * lanes - flat.shape[1])))
    local = jnp.concatenate([blocks, padded.reshape(1, rows, lanes)])
    per_block = local.shape[0]
    held = jnp.concatenate([local] + [ring_send(local, first, step) for step in range(1, SIDE)])
    held = held.reshape(-1, tile, lanes)
    me = group_of(first, own_a, own_b)
    askers = group_of(first, own_a, (own_b + jnp.arange(SIDE)) % SIDE)

    def owners(wanted, per_owner):
        owner = wanted // per_owner
        owner_a = (owner // SIDE, owner % SIDE)[first == "gz"]
        owner_b = (owner // SIDE, owner % SIDE)[second == "gz"]
        return owner_a, owner_b, wanted % per_owner

    block_a, block_b, block_part = owners(block_wanted, blocks.shape[0])
    adapter_a, adapter_b, adapter_part = owners(adapter_wanted, pieces)
    quarter = jnp.arange(pieces)
    block_items = (
        (((own_a - block_a[askers]) % SIDE) * per_block + block_part[askers]) * pieces
    )[..., None] + quarter
    adapter_items = (
        ((own_a - adapter_a[askers]) % SIDE) * per_block + per_block - 1
    ) * pieces + adapter_part[askers]
    source = jnp.concatenate(
        [block_items.reshape(SIDE, -1), adapter_items.reshape(SIDE, -1)], axis=1
    )
    width = source.shape[1]
    outgoing = jnp.take(held, source.reshape(-1), axis=0, mode="clip")
    parts = [outgoing[:width]] + [
        ring_send(outgoing[step * width:(step + 1) * width], second, step)
        for step in range(1, SIDE)
    ]
    slots = block_wanted.shape[1]
    came = jnp.concatenate(
        [jnp.repeat((own_b - block_b[me]) % SIDE, pieces), (own_b - adapter_b[me]) % SIDE]
    )
    merged = pick_piece(came, parts)
    chosen_blocks = merged[: slots * pieces].reshape(slots, rows, lanes)
    chosen_adapters = merged[slots * pieces:].reshape(slots, -1)
    chosen_adapters = chosen_adapters[:, : flat.shape[1]].reshape(slots, *adapters.shape[1:])
    return chosen_blocks, chosen_adapters


def on_device(
    stream,
    prenorm_gain,
    query_weight,
    key_weight,
    value_weight,
    output_weight,
    adapter_down_rows,
    adapter_up_query,
    request_adapter,
    adapter_row_index,
    request_token_length,
    continues_previous,
    request_cache_block,
    cached_length,
    cached_rotated_keys,
    cached_value_rows,
):
    count = stream.shape[0]
    group_at = lax.axis_index(("gx", "gz"))
    wanted = adapter_row_index[request_adapter]
    down_width = adapter_down_rows.shape[2]
    adapters = jnp.concatenate([adapter_down_rows, adapter_up_query], axis=2)
    cache_keys, chosen = route_with_adapters(
        cached_rotated_keys, adapters, request_cache_block, wanted, "gz", "gx"
    )
    cache_values = route(cached_value_rows, request_cache_block, "gx", "gz")
    chosen_down = chosen[:, :, :down_width]
    chosen_up = chosen[:, :, down_width:]
    model_count = lax.axis_size(("my", "mc"))
    spread = lax.all_to_all(
        jnp.broadcast_to(chosen_down, (model_count, *chosen_down.shape)),
        ("my", "mc"),
        0,
        0,
        tiled=True,
    )
    full_down = jnp.moveaxis(spread, 0, 2).reshape(
        *chosen_down.shape[:2], model_count * down_width
    )

    whole = lax.all_gather(stream, ("my", "mc"), axis=1, tiled=True)
    wide = whole.astype(jnp.float32)
    normalized_input = (
        wide * lax.rsqrt(jnp.mean(wide * wide, axis=1, keepdims=True) + 1e-06) * prenorm_gain
    ).astype(jnp.bfloat16)
    before = jnp.maximum(group_at - 1, 0)
    lengths = request_token_length[group_at]
    cached = cached_length[group_at]
    split_flag = continues_previous[group_at]
    prev_len = request_token_length[before, REQS - 1]
    member, request, position = layout(lengths, cached, split_flag, prev_len, count)
    rank_index = adapter_down_rows.shape[1]
    low = jnp.einsum(
        "td,rkd->trk", normalized_input, full_down, preferred_element_type=jnp.float32
    ).reshape(count, REQS * rank_index).astype(jnp.bfloat16)
    own_columns = jnp.repeat(member, rank_index, axis=1).astype(jnp.bfloat16)
    query_update = jnp.dot(
        low * own_columns,
        chosen_up.reshape(REQS * rank_index, -1),
        preferred_element_type=jnp.float32,
    )
    query_vectors = (
        jnp.dot(normalized_input, query_weight, preferred_element_type=jnp.float32)
        + adapter_scale * query_update
    )
    query_vectors = rotate(query_vectors, position, HEAD_WIDTH).astype(jnp.bfloat16)
    keys = rotate(
        jnp.dot(normalized_input, key_weight, preferred_element_type=jnp.float32),
        position,
        HEAD_WIDTH,
    ).astype(jnp.bfloat16)
    values = jnp.dot(normalized_input, value_weight, preferred_element_type=jnp.float32).astype(
        jnp.bfloat16
    )
    tail = count - MOSTLEN
    prev_both = shifted(jnp.concatenate([keys[tail:], values[tail:]], axis=1), ("gx", "gz"), 1)
    prev_keys, prev_values = prev_both[:, : keys.shape[1]], prev_both[:, keys.shape[1]:]
    attended = attend(
        query_vectors,
        keys,
        values,
        prev_keys,
        prev_values,
        cache_keys,
        cache_values,
        request,
        cached,
        split_flag,
        prev_len,
        HEAD_WIDTH,
    )
    partial_out = jnp.dot(attended, output_weight, preferred_element_type=jnp.float32)
    return lax.psum_scatter(
        partial_out.astype(jnp.bfloat16), ("my", "mc"), scatter_dimension=1, tiled=True
    )


def solution(mesh):
    split = Mesh(mesh.devices.reshape(SIDE, SIDE, 4, 2), ("gx", "gz", "my", "mc"))
    groups = ("gx", "gz")
    model = ("my", "mc")
    placed = (
        P(groups, model),
        P(),
        P(None, model),
        P(None, model),
        P(None, model),
        P(model, None),
        P(groups, None, model),
        P(groups, None, model),
        P(),
        P(),
        P(),
        P(),
        P(),
        P(),
        P(groups, None, model),
        P(groups, None, model),
    )
    return jax.shard_map(
        on_device, mesh=split, in_specs=placed, out_specs=P(groups, model), check_vma=False
    )
```

```python
import jax
import jax.numpy as jnp
from jax import lax
from jax.sharding import Mesh, PartitionSpec as P

HEAD_WIDTH = 256
REQS = 4
MOSTLEN = 256


adapter_scale = 2.0


def shifted(value, axis, steps):
    count = lax.axis_size(axis)
    first, last = (max(0, -steps), min(count, count - steps))
    return lax.ppermute(value, axis, [(source, source + steps) for source in range(first, last)])


def rotate(values, position, head_size):
    count = values.shape[0]
    shaped = values.reshape(count, -1, head_size)
    half = head_size // 2
    freq = 10000.0 ** (-jnp.arange(half, dtype=jnp.float32) / half)
    angle = position[:, None, None] * freq[None, None, :]
    cosine = jnp.cos(angle)
    sine = jnp.sin(angle)
    first = shaped[..., :half]
    second = shaped[..., half:]
    turned = jnp.concatenate(
        [first * cosine - second * sine, second * cosine + first * sine], axis=-1
    )
    return turned.reshape(count, -1)


def layout(lengths, cached, split_flag, prev_len, count):
    ends = jnp.cumsum(lengths)
    starts = ends - lengths
    place = jnp.arange(count, dtype=jnp.int32)
    member = ((place[:, None] >= starts[None, :]) & (place[:, None] < ends[None, :])).astype(
        jnp.int32
    )
    request = jnp.sum(member * jnp.arange(lengths.shape[0], dtype=jnp.int32)[None, :], axis=1)
    offset = place - jnp.sum(member * starts[None, :], axis=1)
    extra = jnp.where(request == 0, split_flag * prev_len, 0)
    position = jnp.sum(member * cached[None, :], axis=1) + extra + offset
    return (member, request, position.astype(jnp.float32))


def attend(
    query_vectors,
    keys,
    values,
    prev_keys,
    prev_values,
    cache_keys,
    cache_values,
    request,
    cached,
    split_flag,
    prev_len,
    head_size,
):
    count = query_vectors.shape[0]
    kv_heads = keys.shape[1] // head_size
    ratio = query_vectors.shape[1] // keys.shape[1]
    block = cache_keys.shape[1]
    slots = cache_keys.shape[0] * block
    every_key = jnp.concatenate([cache_keys.reshape(slots, -1), prev_keys, keys], 0).reshape(
        -1, kv_heads, head_size
    )
    every_value = jnp.concatenate(
        [cache_values.reshape(slots, -1), prev_values, values], 0
    ).reshape(-1, kv_heads, head_size)
    owned = jnp.arange(cache_keys.shape[0], dtype=jnp.int32)
    cache_ok = (
        (request[:, None, None] == owned[None, :, None])
        & (jnp.arange(block, dtype=jnp.int32)[None, None, :] < cached[None, :, None])
    ).reshape(count, slots)
    place = jnp.arange(count, dtype=jnp.int32)
    kept = jnp.arange(prev_keys.shape[0], dtype=jnp.int32)
    prev_ok = (
        (split_flag == 1)
        & (request[:, None] == 0)
        & (kept[None, :] >= prev_keys.shape[0] - prev_len)
    )
    own_ok = (request[:, None] == request[None, :]) & (place[None, :] <= place[:, None])
    allowed = jnp.concatenate([cache_ok, prev_ok, own_ok], 1)
    grouped = query_vectors.reshape(count, kv_heads, ratio, head_size)
    scores = jnp.einsum(
        "tkrd,skd->krts", grouped, every_key, preferred_element_type=jnp.float32
    ) * head_size ** (-0.5)
    scores = jnp.where(allowed[None, None], scores, jnp.float32(-1e30))
    top = jnp.max(scores, axis=-1, keepdims=True)
    weights = jnp.exp(scores - top)
    total = jnp.sum(weights, axis=-1)
    numer = jnp.einsum(
        "krts,skd->tkrd",
        weights.astype(jnp.bfloat16),
        every_value,
        preferred_element_type=jnp.float32,
    )
    result = numer / jnp.transpose(total, (2, 0, 1))[..., None]
    return result.reshape(count, -1).astype(jnp.bfloat16)


SIDE = 4


def group_of(first, a_coord, b_coord):
    return b_coord * SIDE + a_coord if first == "gz" else a_coord * SIDE + b_coord


def ring_send(value, axis, step):
    return lax.ppermute(value, axis, [(i, (i + step) % SIDE) for i in range(SIDE)])


def route(local, wanted, first, second):
    coords = {"gx": lax.axis_index("gx"), "gz": lax.axis_index("gz")}
    own_a, own_b = coords[first], coords[second]
    per_owner = local.shape[0]
    slots = wanted.shape[1]
    held = jnp.concatenate([local] + [ring_send(local, first, step) for step in range(1, SIDE)])
    me = group_of(first, own_a, own_b)
    askers = group_of(first, own_a, (own_b + jnp.arange(SIDE)) % SIDE)
    owner = wanted // per_owner
    owner_a = (owner // SIDE, owner % SIDE)[first == "gz"]
    owner_b = (owner // SIDE, owner % SIDE)[second == "gz"]
    source = ((own_a - owner_a[askers]) % SIDE) * per_owner + (wanted % per_owner)[askers]
    outgoing = jnp.take(held, source.reshape(-1), axis=0, mode="clip")
    received = jnp.concatenate(
        [outgoing[:slots]]
        + [
            ring_send(outgoing[step * slots:(step + 1) * slots], second, step)
            for step in range(1, SIDE)
        ]
    )
    pick = ((own_b - owner_b[me]) % SIDE) * slots + jnp.arange(slots)
    return jnp.take(received, pick, axis=0, mode="clip")


def route_with_adapters(blocks, adapters, block_wanted, adapter_wanted, first, second):
    coords = {"gx": lax.axis_index("gx"), "gz": lax.axis_index("gz")}
    own_a, own_b = coords[first], coords[second]
    rows, lanes = blocks.shape[1], blocks.shape[2]
    pieces = adapters.shape[0]
    tile = rows // pieces
    flat = adapters.reshape(pieces, -1)
    padded = jnp.pad(flat, ((0, 0), (0, tile * lanes - flat.shape[1])))
    local = jnp.concatenate([blocks, padded.reshape(1, rows, lanes)])
    per_block = local.shape[0]
    held = jnp.concatenate([local] + [ring_send(local, first, step) for step in range(1, SIDE)])
    held = held.reshape(-1, tile, lanes)
    me = group_of(first, own_a, own_b)
    askers = group_of(first, own_a, (own_b + jnp.arange(SIDE)) % SIDE)

    def owners(wanted, per_owner):
        owner = wanted // per_owner
        owner_a = (owner // SIDE, owner % SIDE)[first == "gz"]
        owner_b = (owner // SIDE, owner % SIDE)[second == "gz"]
        return owner_a, owner_b, wanted % per_owner

    block_a, block_b, block_part = owners(block_wanted, blocks.shape[0])
    adapter_a, adapter_b, adapter_part = owners(adapter_wanted, pieces)
    quarter = jnp.arange(pieces)
    block_items = (
        (((own_a - block_a[askers]) % SIDE) * per_block + block_part[askers]) * pieces
    )[..., None] + quarter
    adapter_items = (
        ((own_a - adapter_a[askers]) % SIDE) * per_block + per_block - 1
    ) * pieces + adapter_part[askers]
    source = jnp.concatenate(
        [block_items.reshape(SIDE, -1), adapter_items.reshape(SIDE, -1)], axis=1
    )
    width = source.shape[1]
    outgoing = jnp.take(held, source.reshape(-1), axis=0, mode="clip")
    received = jnp.concatenate(
        [outgoing[:width]]
        + [
            ring_send(outgoing[step * width:(step + 1) * width], second, step)
            for step in range(1, SIDE)
        ]
    )
    slots = block_wanted.shape[1]
    slot = jnp.arange(slots)
    block_pick = (
        (((own_b - block_b[me]) % SIDE) * width + slot * pieces)[:, None] + quarter
    ).reshape(-1)
    adapter_pick = ((own_b - adapter_b[me]) % SIDE) * width + slots * pieces + slot
    chosen_blocks = jnp.take(received, block_pick, axis=0, mode="clip").reshape(
        slots, rows, lanes
    )
    chosen_adapters = jnp.take(received, adapter_pick, axis=0, mode="clip").reshape(slots, -1)
    chosen_adapters = chosen_adapters[:, : flat.shape[1]].reshape(slots, *adapters.shape[1:])
    return chosen_blocks, chosen_adapters


def on_device(
    stream,
    prenorm_gain,
    query_weight,
    key_weight,
    value_weight,
    output_weight,
    adapter_down_rows,
    adapter_up_query,
    request_adapter,
    adapter_row_index,
    request_token_length,
    continues_previous,
    request_cache_block,
    cached_length,
    cached_rotated_keys,
    cached_value_rows,
):
    count = stream.shape[0]
    group_at = lax.axis_index(("gx", "gz"))
    wanted = adapter_row_index[request_adapter]
    down_width = adapter_down_rows.shape[2]
    adapters = jnp.concatenate([adapter_down_rows, adapter_up_query], axis=2)
    cache_keys, chosen = route_with_adapters(
        cached_rotated_keys, adapters, request_cache_block, wanted, "gz", "gx"
    )
    cache_values = route(cached_value_rows, request_cache_block, "gx", "gz")
    chosen_down = chosen[:, :, :down_width]
    chosen_up = chosen[:, :, down_width:]
    model_count = lax.axis_size(("my", "mc"))
    lanes = 1024
    widened = jnp.pad(chosen_down, ((0, 0), (0, 0), (0, lanes - down_width)))
    gathered = lax.all_gather(widened, ("my", "mc"), axis=2, tiled=True)
    full_down = gathered.reshape(*chosen_down.shape[:2], model_count, lanes)[..., :down_width]
    full_down = full_down.reshape(*chosen_down.shape[:2], model_count * down_width)

    whole = lax.all_gather(stream, ("my", "mc"), axis=1, tiled=True)
    wide = whole.astype(jnp.float32)
    normalized_input = (
        wide * lax.rsqrt(jnp.mean(wide * wide, axis=1, keepdims=True) + 1e-06) * prenorm_gain
    ).astype(jnp.bfloat16)
    before = jnp.maximum(group_at - 1, 0)
    lengths = request_token_length[group_at]
    cached = cached_length[group_at]
    split_flag = continues_previous[group_at]
    prev_len = request_token_length[before, REQS - 1]
    member, request, position = layout(lengths, cached, split_flag, prev_len, count)
    rank_index = adapter_down_rows.shape[1]
    low = jnp.einsum(
        "td,rkd->trk", normalized_input, full_down, preferred_element_type=jnp.float32
    ).reshape(count, REQS * rank_index).astype(jnp.bfloat16)
    own_columns = jnp.repeat(member, rank_index, axis=1).astype(jnp.bfloat16)
    query_update = jnp.dot(
        low * own_columns,
        chosen_up.reshape(REQS * rank_index, -1),
        preferred_element_type=jnp.float32,
    )
    query_vectors = (
        jnp.dot(normalized_input, query_weight, preferred_element_type=jnp.float32)
        + adapter_scale * query_update
    )
    query_vectors = rotate(query_vectors, position, HEAD_WIDTH).astype(jnp.bfloat16)
    keys = rotate(
        jnp.dot(normalized_input, key_weight, preferred_element_type=jnp.float32),
        position,
        HEAD_WIDTH,
    ).astype(jnp.bfloat16)
    values = jnp.dot(normalized_input, value_weight, preferred_element_type=jnp.float32).astype(
        jnp.bfloat16
    )
    tail = count - MOSTLEN
    prev_both = shifted(jnp.concatenate([keys[tail:], values[tail:]], axis=1), ("gx", "gz"), 1)
    prev_keys, prev_values = prev_both[:, : keys.shape[1]], prev_both[:, keys.shape[1]:]
    attended = attend(
        query_vectors,
        keys,
        values,
        prev_keys,
        prev_values,
        cache_keys,
        cache_values,
        request,
        cached,
        split_flag,
        prev_len,
        HEAD_WIDTH,
    )
    partial_out = jnp.dot(attended, output_weight, preferred_element_type=jnp.float32)
    return lax.psum_scatter(
        partial_out.astype(jnp.bfloat16), ("my", "mc"), scatter_dimension=1, tiled=True
    )


def solution(mesh):
    split = Mesh(mesh.devices.reshape(SIDE, SIDE, 4, 2), ("gx", "gz", "my", "mc"))
    groups = ("gx", "gz")
    model = ("my", "mc")
    placed = (
        P(groups, model),
        P(),
        P(None, model),
        P(None, model),
        P(None, model),
        P(model, None),
        P(groups, None, model),
        P(groups, None, model),
        P(),
        P(),
        P(),
        P(),
        P(),
        P(),
        P(groups, None, model),
        P(groups, None, model),
    )
    return jax.shard_map(
        on_device, mesh=split, in_specs=placed, out_specs=P(groups, model), check_vma=False
    )
```

```python
import jax
import jax.numpy as jnp
from jax import lax
from jax.sharding import Mesh, PartitionSpec as P

HEAD_WIDTH = 256
REQS = 4
MOSTLEN = 256


adapter_scale = 2.0


def shifted(value, axis, steps):
    count = lax.axis_size(axis)
    first, last = (max(0, -steps), min(count, count - steps))
    return lax.ppermute(value, axis, [(source, source + steps) for source in range(first, last)])


def rotate(values, position, head_size):
    count = values.shape[0]
    shaped = values.reshape(count, -1, head_size)
    half = head_size // 2
    freq = 10000.0 ** (-jnp.arange(half, dtype=jnp.float32) / half)
    angle = position[:, None, None] * freq[None, None, :]
    cosine = jnp.cos(angle)
    sine = jnp.sin(angle)
    first = shaped[..., :half]
    second = shaped[..., half:]
    turned = jnp.concatenate(
        [first * cosine - second * sine, second * cosine + first * sine], axis=-1
    )
    return turned.reshape(count, -1)


def layout(lengths, cached, split_flag, prev_len, count):
    ends = jnp.cumsum(lengths)
    starts = ends - lengths
    place = jnp.arange(count, dtype=jnp.int32)
    member = ((place[:, None] >= starts[None, :]) & (place[:, None] < ends[None, :])).astype(
        jnp.int32
    )
    request = jnp.sum(member * jnp.arange(lengths.shape[0], dtype=jnp.int32)[None, :], axis=1)
    offset = place - jnp.sum(member * starts[None, :], axis=1)
    extra = jnp.where(request == 0, split_flag * prev_len, 0)
    position = jnp.sum(member * cached[None, :], axis=1) + extra + offset
    return (member, request, position.astype(jnp.float32))


def attend(
    query_vectors,
    keys,
    values,
    prev_keys,
    prev_values,
    cache_keys,
    cache_values,
    request,
    cached,
    split_flag,
    prev_len,
    head_size,
):
    count = query_vectors.shape[0]
    kv_heads = keys.shape[1] // head_size
    ratio = query_vectors.shape[1] // keys.shape[1]
    block = cache_keys.shape[1]
    slots = cache_keys.shape[0] * block
    every_key = jnp.concatenate([cache_keys.reshape(slots, -1), prev_keys, keys], 0).reshape(
        -1, kv_heads, head_size
    )
    every_value = jnp.concatenate(
        [cache_values.reshape(slots, -1), prev_values, values], 0
    ).reshape(-1, kv_heads, head_size)
    owned = jnp.arange(cache_keys.shape[0], dtype=jnp.int32)
    cache_ok = (
        (request[:, None, None] == owned[None, :, None])
        & (jnp.arange(block, dtype=jnp.int32)[None, None, :] < cached[None, :, None])
    ).reshape(count, slots)
    place = jnp.arange(count, dtype=jnp.int32)
    kept = jnp.arange(prev_keys.shape[0], dtype=jnp.int32)
    prev_ok = (
        (split_flag == 1)
        & (request[:, None] == 0)
        & (kept[None, :] >= prev_keys.shape[0] - prev_len)
    )
    own_ok = (request[:, None] == request[None, :]) & (place[None, :] <= place[:, None])
    allowed = jnp.concatenate([cache_ok, prev_ok, own_ok], 1)
    grouped = query_vectors.reshape(count, kv_heads, ratio, head_size)
    scores = jnp.einsum(
        "tkrd,skd->krts", grouped, every_key, preferred_element_type=jnp.float32
    ) * head_size ** (-0.5)
    scores = jnp.where(allowed[None, None], scores, jnp.float32(-1e30))
    top = jnp.max(scores, axis=-1, keepdims=True)
    weights = jnp.exp(scores - top)
    total = jnp.sum(weights, axis=-1)
    numer = jnp.einsum(
        "krts,skd->tkrd",
        weights.astype(jnp.bfloat16),
        every_value,
        preferred_element_type=jnp.float32,
    )
    result = numer / jnp.transpose(total, (2, 0, 1))[..., None]
    return result.reshape(count, -1).astype(jnp.bfloat16)


SIDE = 4


def group_of(first, a_coord, b_coord):
    return b_coord * SIDE + a_coord if first == "gz" else a_coord * SIDE + b_coord


def ring_send(value, axis, step):
    return lax.ppermute(value, axis, [(i, (i + step) % SIDE) for i in range(SIDE)])


def route(local, wanted, first, second):
    coords = {"gx": lax.axis_index("gx"), "gz": lax.axis_index("gz")}
    own_a, own_b = coords[first], coords[second]
    per_owner = local.shape[0]
    slots = wanted.shape[1]
    held = jnp.concatenate([local] + [ring_send(local, first, step) for step in range(1, SIDE)])
    me = group_of(first, own_a, own_b)
    askers = group_of(first, own_a, (own_b + jnp.arange(SIDE)) % SIDE)
    owner = wanted // per_owner
    owner_a = (owner // SIDE, owner % SIDE)[first == "gz"]
    owner_b = (owner // SIDE, owner % SIDE)[second == "gz"]
    table = ((own_a - owner_a) % SIDE) * per_owner + wanted % per_owner
    source = jnp.take(table, askers, axis=0, mode="clip")
    outgoing = jnp.take(held, source.reshape(-1), axis=0, mode="clip")
    received = jnp.concatenate(
        [outgoing[:slots]]
        + [
            ring_send(outgoing[step * slots:(step + 1) * slots], second, step)
            for step in range(1, SIDE)
        ]
    )
    pick = ((own_b - owner_b[me]) % SIDE) * slots + jnp.arange(slots)
    return jnp.take(received, pick, axis=0, mode="clip")


def route_with_adapters(blocks, adapters, block_wanted, adapter_wanted, first, second):
    coords = {"gx": lax.axis_index("gx"), "gz": lax.axis_index("gz")}
    own_a, own_b = coords[first], coords[second]
    rows, lanes = blocks.shape[1], blocks.shape[2]
    pieces = adapters.shape[0]
    tile = rows // pieces
    flat = adapters.reshape(pieces, -1)
    padded = jnp.pad(flat, ((0, 0), (0, tile * lanes - flat.shape[1])))
    local = jnp.concatenate([blocks, padded.reshape(1, rows, lanes)])
    per_block = local.shape[0]
    held = jnp.concatenate([local] + [ring_send(local, first, step) for step in range(1, SIDE)])
    held = held.reshape(-1, tile, lanes)
    me = group_of(first, own_a, own_b)
    askers = group_of(first, own_a, (own_b + jnp.arange(SIDE)) % SIDE)

    def owners(wanted, per_owner):
        owner = wanted // per_owner
        owner_a = (owner // SIDE, owner % SIDE)[first == "gz"]
        owner_b = (owner // SIDE, owner % SIDE)[second == "gz"]
        return owner_a, owner_b, wanted % per_owner

    block_a, block_b, block_part = owners(block_wanted, blocks.shape[0])
    adapter_a, adapter_b, adapter_part = owners(adapter_wanted, pieces)
    quarter = jnp.arange(pieces)
    block_table = (
        (((own_a - block_a) % SIDE) * per_block + block_part) * pieces
    )[..., None] + quarter
    adapter_table = (((own_a - adapter_a) % SIDE) * per_block + per_block - 1) * pieces + adapter_part
    table = jnp.concatenate(
        [block_table.reshape(block_table.shape[0], -1), adapter_table], axis=1
    )
    source = jnp.take(table, askers, axis=0, mode="clip")
    width = source.shape[1]
    outgoing = jnp.take(held, source.reshape(-1), axis=0, mode="clip")
    received = jnp.concatenate(
        [outgoing[:width]]
        + [
            ring_send(outgoing[step * width:(step + 1) * width], second, step)
            for step in range(1, SIDE)
        ]
    )
    slots = block_wanted.shape[1]
    slot = jnp.arange(slots)
    block_pick = (
        (((own_b - block_b[me]) % SIDE) * width + slot * pieces)[:, None] + quarter
    ).reshape(-1)
    adapter_pick = ((own_b - adapter_b[me]) % SIDE) * width + slots * pieces + slot
    chosen_blocks = jnp.take(received, block_pick, axis=0, mode="clip").reshape(
        slots, rows, lanes
    )
    chosen_adapters = jnp.take(received, adapter_pick, axis=0, mode="clip").reshape(slots, -1)
    chosen_adapters = chosen_adapters[:, : flat.shape[1]].reshape(slots, *adapters.shape[1:])
    return chosen_blocks, chosen_adapters


def on_device(
    stream,
    prenorm_gain,
    query_weight,
    key_weight,
    value_weight,
    output_weight,
    adapter_down_rows,
    adapter_up_query,
    request_adapter,
    adapter_row_index,
    request_token_length,
    continues_previous,
    request_cache_block,
    cached_length,
    cached_rotated_keys,
    cached_value_rows,
):
    count = stream.shape[0]
    group_at = lax.axis_index(("gx", "gz"))
    wanted = adapter_row_index[request_adapter]
    down_width = adapter_down_rows.shape[2]
    adapters = jnp.concatenate([adapter_down_rows, adapter_up_query], axis=2)
    cache_keys, chosen = route_with_adapters(
        cached_rotated_keys, adapters, request_cache_block, wanted, "gz", "gx"
    )
    cache_values = route(cached_value_rows, request_cache_block, "gx", "gz")
    chosen_down = chosen[:, :, :down_width]
    chosen_up = chosen[:, :, down_width:]
    model_count = lax.axis_size(("my", "mc"))
    spread = lax.all_to_all(
        jnp.broadcast_to(chosen_down, (model_count, *chosen_down.shape)),
        ("my", "mc"),
        0,
        0,
        tiled=True,
    )
    full_down = jnp.moveaxis(spread, 0, 2).reshape(
        *chosen_down.shape[:2], model_count * down_width
    )

    whole = lax.all_gather(stream, ("my", "mc"), axis=1, tiled=True)
    wide = whole.astype(jnp.float32)
    normalized_input = (
        wide * lax.rsqrt(jnp.mean(wide * wide, axis=1, keepdims=True) + 1e-06) * prenorm_gain
    ).astype(jnp.bfloat16)
    before = jnp.maximum(group_at - 1, 0)
    lengths = request_token_length[group_at]
    cached = cached_length[group_at]
    split_flag = continues_previous[group_at]
    prev_len = request_token_length[before, REQS - 1]
    member, request, position = layout(lengths, cached, split_flag, prev_len, count)
    rank_index = adapter_down_rows.shape[1]
    low = jnp.einsum(
        "td,rkd->trk", normalized_input, full_down, preferred_element_type=jnp.float32
    ).reshape(count, REQS * rank_index).astype(jnp.bfloat16)
    own_columns = jnp.repeat(member, rank_index, axis=1).astype(jnp.bfloat16)
    query_update = jnp.dot(
        low * own_columns,
        chosen_up.reshape(REQS * rank_index, -1),
        preferred_element_type=jnp.float32,
    )
    query_vectors = (
        jnp.dot(normalized_input, query_weight, preferred_element_type=jnp.float32)
        + adapter_scale * query_update
    )
    query_vectors = rotate(query_vectors, position, HEAD_WIDTH).astype(jnp.bfloat16)
    keys = rotate(
        jnp.dot(normalized_input, key_weight, preferred_element_type=jnp.float32),
        position,
        HEAD_WIDTH,
    ).astype(jnp.bfloat16)
    values = jnp.dot(normalized_input, value_weight, preferred_element_type=jnp.float32).astype(
        jnp.bfloat16
    )
    tail = count - MOSTLEN
    prev_both = shifted(jnp.concatenate([keys[tail:], values[tail:]], axis=1), ("gx", "gz"), 1)
    prev_keys, prev_values = prev_both[:, : keys.shape[1]], prev_both[:, keys.shape[1]:]
    attended = attend(
        query_vectors,
        keys,
        values,
        prev_keys,
        prev_values,
        cache_keys,
        cache_values,
        request,
        cached,
        split_flag,
        prev_len,
        HEAD_WIDTH,
    )
    partial_out = jnp.dot(attended, output_weight, preferred_element_type=jnp.float32)
    return lax.psum_scatter(
        partial_out.astype(jnp.bfloat16), ("my", "mc"), scatter_dimension=1, tiled=True
    )


def solution(mesh):
    split = Mesh(mesh.devices.reshape(SIDE, SIDE, 4, 2), ("gx", "gz", "my", "mc"))
    groups = ("gx", "gz")
    model = ("my", "mc")
    placed = (
        P(groups, model),
        P(),
        P(None, model),
        P(None, model),
        P(None, model),
        P(model, None),
        P(groups, None, model),
        P(groups, None, model),
        P(),
        P(),
        P(),
        P(),
        P(),
        P(),
        P(groups, None, model),
        P(groups, None, model),
    )
    return jax.shard_map(
        on_device, mesh=split, in_specs=placed, out_specs=P(groups, model), check_vma=False
    )
```

```python
import jax
import jax.numpy as jnp
from jax import lax
from jax.sharding import Mesh, PartitionSpec as P

HEAD_WIDTH = 256
REQS = 4
MOSTLEN = 256


adapter_scale = 2.0


def shifted(value, axis, steps):
    count = lax.axis_size(axis)
    first, last = (max(0, -steps), min(count, count - steps))
    return lax.ppermute(value, axis, [(source, source + steps) for source in range(first, last)])


def rotate(values, position, head_size):
    count = values.shape[0]
    shaped = values.reshape(count, -1, head_size)
    half = head_size // 2
    freq = 10000.0 ** (-jnp.arange(half, dtype=jnp.float32) / half)
    angle = position[:, None, None] * freq[None, None, :]
    cosine = jnp.cos(angle)
    sine = jnp.sin(angle)
    first = shaped[..., :half]
    second = shaped[..., half:]
    turned = jnp.concatenate(
        [first * cosine - second * sine, second * cosine + first * sine], axis=-1
    )
    return turned.reshape(count, -1)


def layout(lengths, cached, split_flag, prev_len, count):
    ends = jnp.cumsum(lengths)
    starts = ends - lengths
    place = jnp.arange(count, dtype=jnp.int32)
    member = ((place[:, None] >= starts[None, :]) & (place[:, None] < ends[None, :])).astype(
        jnp.int32
    )
    request = jnp.sum(member * jnp.arange(lengths.shape[0], dtype=jnp.int32)[None, :], axis=1)
    offset = place - jnp.sum(member * starts[None, :], axis=1)
    extra = jnp.where(request == 0, split_flag * prev_len, 0)
    position = jnp.sum(member * cached[None, :], axis=1) + extra + offset
    return (member, request, position.astype(jnp.float32))


def attend(
    query_vectors,
    keys,
    values,
    prev_keys,
    prev_values,
    cache_keys,
    cache_values,
    request,
    cached,
    split_flag,
    prev_len,
    head_size,
):
    count = query_vectors.shape[0]
    kv_heads = keys.shape[1] // head_size
    ratio = query_vectors.shape[1] // keys.shape[1]
    block = cache_keys.shape[1]
    slots = cache_keys.shape[0] * block
    every_key = jnp.concatenate([cache_keys.reshape(slots, -1), prev_keys, keys], 0).reshape(
        -1, kv_heads, head_size
    )
    every_value = jnp.concatenate(
        [cache_values.reshape(slots, -1), prev_values, values], 0
    ).reshape(-1, kv_heads, head_size)
    owned = jnp.arange(cache_keys.shape[0], dtype=jnp.int32)
    cache_ok = (
        (request[:, None, None] == owned[None, :, None])
        & (jnp.arange(block, dtype=jnp.int32)[None, None, :] < cached[None, :, None])
    ).reshape(count, slots)
    place = jnp.arange(count, dtype=jnp.int32)
    kept = jnp.arange(prev_keys.shape[0], dtype=jnp.int32)
    prev_ok = (
        (split_flag == 1)
        & (request[:, None] == 0)
        & (kept[None, :] >= prev_keys.shape[0] - prev_len)
    )
    own_ok = (request[:, None] == request[None, :]) & (place[None, :] <= place[:, None])
    allowed = jnp.concatenate([cache_ok, prev_ok, own_ok], 1)
    grouped = query_vectors.reshape(count, kv_heads, ratio, head_size)
    scores = jnp.einsum(
        "tkrd,skd->krts", grouped, every_key, preferred_element_type=jnp.float32
    ) * head_size ** (-0.5)
    scores = jnp.where(allowed[None, None], scores, jnp.float32(-1e30))
    top = jnp.max(scores, axis=-1, keepdims=True)
    weights = jnp.exp(scores - top)
    total = jnp.sum(weights, axis=-1)
    numer = jnp.einsum(
        "krts,skd->tkrd",
        weights.astype(jnp.bfloat16),
        every_value,
        preferred_element_type=jnp.float32,
    )
    result = numer / jnp.transpose(total, (2, 0, 1))[..., None]
    return result.reshape(count, -1).astype(jnp.bfloat16)


SIDE = 4


def group_of(first, a_coord, b_coord):
    return b_coord * SIDE + a_coord if first == "gz" else a_coord * SIDE + b_coord


def ring_send(value, axis, step):
    return lax.ppermute(value, axis, [(i, (i + step) % SIDE) for i in range(SIDE)])


def route(local, wanted, first, second):
    coords = {"gx": lax.axis_index("gx"), "gz": lax.axis_index("gz")}
    own_a, own_b = coords[first], coords[second]
    per_owner = local.shape[0]
    slots = wanted.shape[1]
    spread_out = jnp.broadcast_to(local[None], (SIDE, *local.shape))
    held = lax.all_to_all(spread_out, first, 0, 0, tiled=True).reshape(
        SIDE * per_owner, *local.shape[1:]
    )
    me = group_of(first, own_a, own_b)
    askers = group_of(first, own_a, (own_b + jnp.arange(SIDE)) % SIDE)
    owner = wanted // per_owner
    owner_a = (owner // SIDE, owner % SIDE)[first == "gz"]
    owner_b = (owner // SIDE, owner % SIDE)[second == "gz"]
    table = owner_a * per_owner + wanted % per_owner
    source = jnp.take(table, askers, axis=0, mode="clip")
    outgoing = jnp.take(held, source.reshape(-1), axis=0, mode="clip")
    received = jnp.concatenate(
        [outgoing[:slots]]
        + [
            ring_send(outgoing[step * slots:(step + 1) * slots], second, step)
            for step in range(1, SIDE)
        ]
    )
    pick = ((own_b - owner_b[me]) % SIDE) * slots + jnp.arange(slots)
    return jnp.take(received, pick, axis=0, mode="clip")


def route_with_adapters(blocks, adapters, block_wanted, adapter_wanted, first, second):
    coords = {"gx": lax.axis_index("gx"), "gz": lax.axis_index("gz")}
    own_a, own_b = coords[first], coords[second]
    rows, lanes = blocks.shape[1], blocks.shape[2]
    pieces = adapters.shape[0]
    tile = rows // pieces
    flat = adapters.reshape(pieces, -1)
    padded = jnp.pad(flat, ((0, 0), (0, tile * lanes - flat.shape[1])))
    local = jnp.concatenate([blocks, padded.reshape(1, rows, lanes)])
    per_block = local.shape[0]
    held = jnp.concatenate([local] + [ring_send(local, first, step) for step in range(1, SIDE)])
    held = held.reshape(-1, tile, lanes)
    me = group_of(first, own_a, own_b)
    askers = group_of(first, own_a, (own_b + jnp.arange(SIDE)) % SIDE)

    def owners(wanted, per_owner):
        owner = wanted // per_owner
        owner_a = (owner // SIDE, owner % SIDE)[first == "gz"]
        owner_b = (owner // SIDE, owner % SIDE)[second == "gz"]
        return owner_a, owner_b, wanted % per_owner

    block_a, block_b, block_part = owners(block_wanted, blocks.shape[0])
    adapter_a, adapter_b, adapter_part = owners(adapter_wanted, pieces)
    quarter = jnp.arange(pieces)
    block_table = (
        (((own_a - block_a) % SIDE) * per_block + block_part) * pieces
    )[..., None] + quarter
    adapter_table = (((own_a - adapter_a) % SIDE) * per_block + per_block - 1) * pieces + adapter_part
    table = jnp.concatenate(
        [block_table.reshape(block_table.shape[0], -1), adapter_table], axis=1
    )
    source = jnp.take(table, askers, axis=0, mode="clip")
    width = source.shape[1]
    outgoing = jnp.take(held, source.reshape(-1), axis=0, mode="clip")
    received = jnp.concatenate(
        [outgoing[:width]]
        + [
            ring_send(outgoing[step * width:(step + 1) * width], second, step)
            for step in range(1, SIDE)
        ]
    )
    slots = block_wanted.shape[1]
    slot = jnp.arange(slots)
    block_pick = (
        (((own_b - block_b[me]) % SIDE) * width + slot * pieces)[:, None] + quarter
    ).reshape(-1)
    adapter_pick = ((own_b - adapter_b[me]) % SIDE) * width + slots * pieces + slot
    chosen_blocks = jnp.take(received, block_pick, axis=0, mode="clip").reshape(
        slots, rows, lanes
    )
    chosen_adapters = jnp.take(received, adapter_pick, axis=0, mode="clip").reshape(slots, -1)
    chosen_adapters = chosen_adapters[:, : flat.shape[1]].reshape(slots, *adapters.shape[1:])
    return chosen_blocks, chosen_adapters


def on_device(
    stream,
    prenorm_gain,
    query_weight,
    key_weight,
    value_weight,
    output_weight,
    adapter_down_rows,
    adapter_up_query,
    request_adapter,
    adapter_row_index,
    request_token_length,
    continues_previous,
    request_cache_block,
    cached_length,
    cached_rotated_keys,
    cached_value_rows,
):
    count = stream.shape[0]
    group_at = lax.axis_index(("gx", "gz"))
    wanted = adapter_row_index[request_adapter]
    down_width = adapter_down_rows.shape[2]
    adapters = jnp.concatenate([adapter_down_rows, adapter_up_query], axis=2)
    cache_keys, chosen = route_with_adapters(
        cached_rotated_keys, adapters, request_cache_block, wanted, "gz", "gx"
    )
    cache_values = route(cached_value_rows, request_cache_block, "gx", "gz")
    chosen_down = chosen[:, :, :down_width]
    chosen_up = chosen[:, :, down_width:]
    model_count = lax.axis_size(("my", "mc"))
    spread = lax.all_to_all(
        jnp.broadcast_to(chosen_down, (model_count, *chosen_down.shape)),
        ("my", "mc"),
        0,
        0,
        tiled=True,
    )
    full_down = jnp.moveaxis(spread, 0, 2).reshape(
        *chosen_down.shape[:2], model_count * down_width
    )

    whole = lax.all_gather(stream, ("my", "mc"), axis=1, tiled=True)
    wide = whole.astype(jnp.float32)
    normalized_input = (
        wide * lax.rsqrt(jnp.mean(wide * wide, axis=1, keepdims=True) + 1e-06) * prenorm_gain
    ).astype(jnp.bfloat16)
    before = jnp.maximum(group_at - 1, 0)
    lengths = request_token_length[group_at]
    cached = cached_length[group_at]
    split_flag = continues_previous[group_at]
    prev_len = request_token_length[before, REQS - 1]
    member, request, position = layout(lengths, cached, split_flag, prev_len, count)
    rank_index = adapter_down_rows.shape[1]
    low = jnp.einsum(
        "td,rkd->trk", normalized_input, full_down, preferred_element_type=jnp.float32
    ).reshape(count, REQS * rank_index).astype(jnp.bfloat16)
    own_columns = jnp.repeat(member, rank_index, axis=1).astype(jnp.bfloat16)
    query_update = jnp.dot(
        low * own_columns,
        chosen_up.reshape(REQS * rank_index, -1),
        preferred_element_type=jnp.float32,
    )
    query_vectors = (
        jnp.dot(normalized_input, query_weight, preferred_element_type=jnp.float32)
        + adapter_scale * query_update
    )
    query_vectors = rotate(query_vectors, position, HEAD_WIDTH).astype(jnp.bfloat16)
    keys = rotate(
        jnp.dot(normalized_input, key_weight, preferred_element_type=jnp.float32),
        position,
        HEAD_WIDTH,
    ).astype(jnp.bfloat16)
    values = jnp.dot(normalized_input, value_weight, preferred_element_type=jnp.float32).astype(
        jnp.bfloat16
    )
    tail = count - MOSTLEN
    prev_both = shifted(jnp.concatenate([keys[tail:], values[tail:]], axis=1), ("gx", "gz"), 1)
    prev_keys, prev_values = prev_both[:, : keys.shape[1]], prev_both[:, keys.shape[1]:]
    attended = attend(
        query_vectors,
        keys,
        values,
        prev_keys,
        prev_values,
        cache_keys,
        cache_values,
        request,
        cached,
        split_flag,
        prev_len,
        HEAD_WIDTH,
    )
    partial_out = jnp.dot(attended, output_weight, preferred_element_type=jnp.float32)
    return lax.psum_scatter(
        partial_out.astype(jnp.bfloat16), ("my", "mc"), scatter_dimension=1, tiled=True
    )


def solution(mesh):
    split = Mesh(mesh.devices.reshape(SIDE, SIDE, 4, 2), ("gx", "gz", "my", "mc"))
    groups = ("gx", "gz")
    model = ("my", "mc")
    placed = (
        P(groups, model),
        P(),
        P(None, model),
        P(None, model),
        P(None, model),
        P(model, None),
        P(groups, None, model),
        P(groups, None, model),
        P(),
        P(),
        P(),
        P(),
        P(),
        P(),
        P(groups, None, model),
        P(groups, None, model),
    )
    return jax.shard_map(
        on_device, mesh=split, in_specs=placed, out_specs=P(groups, model), check_vma=False
    )
```

```python
import jax
import jax.numpy as jnp
from jax import lax
from jax.sharding import Mesh, PartitionSpec as P

HEAD_WIDTH = 256
REQS = 4
MOSTLEN = 256


adapter_scale = 2.0


def shifted(value, axis, steps):
    count = lax.axis_size(axis)
    first, last = (max(0, -steps), min(count, count - steps))
    return lax.ppermute(value, axis, [(source, source + steps) for source in range(first, last)])


def rotate(values, position, head_size):
    count = values.shape[0]
    shaped = values.reshape(count, -1, head_size)
    half = head_size // 2
    freq = 10000.0 ** (-jnp.arange(half, dtype=jnp.float32) / half)
    angle = position[:, None, None] * freq[None, None, :]
    cosine = jnp.cos(angle)
    sine = jnp.sin(angle)
    first = shaped[..., :half]
    second = shaped[..., half:]
    turned = jnp.concatenate(
        [first * cosine - second * sine, second * cosine + first * sine], axis=-1
    )
    return turned.reshape(count, -1)


def layout(lengths, cached, split_flag, prev_len, count):
    ends = jnp.cumsum(lengths)
    starts = ends - lengths
    place = jnp.arange(count, dtype=jnp.int32)
    member = ((place[:, None] >= starts[None, :]) & (place[:, None] < ends[None, :])).astype(
        jnp.int32
    )
    request = jnp.sum(member * jnp.arange(lengths.shape[0], dtype=jnp.int32)[None, :], axis=1)
    offset = place - jnp.sum(member * starts[None, :], axis=1)
    extra = jnp.where(request == 0, split_flag * prev_len, 0)
    position = jnp.sum(member * cached[None, :], axis=1) + extra + offset
    return (member, request, position.astype(jnp.float32))


def attend(
    query_vectors,
    keys,
    values,
    prev_keys,
    prev_values,
    cache_keys,
    cache_values,
    request,
    cached,
    split_flag,
    prev_len,
    head_size,
):
    count = query_vectors.shape[0]
    kv_heads = keys.shape[1] // head_size
    ratio = query_vectors.shape[1] // keys.shape[1]
    block = cache_keys.shape[1]
    slots = cache_keys.shape[0] * block
    every_key = jnp.concatenate([cache_keys.reshape(slots, -1), prev_keys, keys], 0).reshape(
        -1, kv_heads, head_size
    )
    every_value = jnp.concatenate(
        [cache_values.reshape(slots, -1), prev_values, values], 0
    ).reshape(-1, kv_heads, head_size)
    owned = jnp.arange(cache_keys.shape[0], dtype=jnp.int32)
    cache_ok = (
        (request[:, None, None] == owned[None, :, None])
        & (jnp.arange(block, dtype=jnp.int32)[None, None, :] < cached[None, :, None])
    ).reshape(count, slots)
    place = jnp.arange(count, dtype=jnp.int32)
    kept = jnp.arange(prev_keys.shape[0], dtype=jnp.int32)
    prev_ok = (
        (split_flag == 1)
        & (request[:, None] == 0)
        & (kept[None, :] >= prev_keys.shape[0] - prev_len)
    )
    own_ok = (request[:, None] == request[None, :]) & (place[None, :] <= place[:, None])
    allowed = jnp.concatenate([cache_ok, prev_ok, own_ok], 1)
    grouped = query_vectors.reshape(count, kv_heads, ratio, head_size)
    scores = jnp.einsum(
        "tkrd,skd->krts", grouped, every_key, preferred_element_type=jnp.float32
    ) * head_size ** (-0.5)
    scores = jnp.where(allowed[None, None], scores, jnp.float32(-1e30))
    top = jnp.max(scores, axis=-1, keepdims=True)
    weights = jnp.exp(scores - top)
    total = jnp.sum(weights, axis=-1)
    numer = jnp.einsum(
        "krts,skd->tkrd",
        weights.astype(jnp.bfloat16),
        every_value,
        preferred_element_type=jnp.float32,
    )
    result = numer / jnp.transpose(total, (2, 0, 1))[..., None]
    return result.reshape(count, -1).astype(jnp.bfloat16)


SIDE = 4


def group_of(first, a_coord, b_coord):
    return b_coord * SIDE + a_coord if first == "gz" else a_coord * SIDE + b_coord


def ring_send(value, axis, step):
    return lax.ppermute(value, axis, [(i, (i + step) % SIDE) for i in range(SIDE)])


def route(local, wanted, first, second):
    coords = {"gx": lax.axis_index("gx"), "gz": lax.axis_index("gz")}
    own_a, own_b = coords[first], coords[second]
    per_owner = local.shape[0]
    slots = wanted.shape[1]
    spread_out = jnp.broadcast_to(local[None], (SIDE, *local.shape))
    held = lax.all_to_all(spread_out, first, 0, 0, tiled=True).reshape(
        SIDE * per_owner, *local.shape[1:]
    )
    me = group_of(first, own_a, own_b)
    askers = group_of(first, own_a, (own_b + jnp.arange(SIDE)) % SIDE)
    owner = wanted // per_owner
    owner_a = (owner // SIDE, owner % SIDE)[first == "gz"]
    owner_b = (owner // SIDE, owner % SIDE)[second == "gz"]
    table = owner_a * per_owner + wanted % per_owner
    source = jnp.take(table, askers, axis=0, mode="clip")
    outgoing = jnp.take(held, source.reshape(-1), axis=0, mode="clip")
    received = jnp.concatenate(
        [outgoing[:slots]]
        + [
            ring_send(outgoing[step * slots:(step + 1) * slots], second, step)
            for step in range(1, SIDE)
        ]
    )
    pick = ((own_b - owner_b[me]) % SIDE) * slots + jnp.arange(slots)
    return jnp.take(received, pick, axis=0, mode="clip")


def route_with_adapters(blocks, adapters, block_wanted, adapter_wanted, first, second):
    coords = {"gx": lax.axis_index("gx"), "gz": lax.axis_index("gz")}
    own_a, own_b = coords[first], coords[second]
    rows, lanes = blocks.shape[1], blocks.shape[2]
    pieces = adapters.shape[0]
    tile = rows // pieces
    flat = adapters.reshape(pieces, -1)
    padded = jnp.pad(flat, ((0, 0), (0, tile * lanes - flat.shape[1])))
    local = jnp.concatenate([blocks, padded.reshape(1, rows, lanes)])
    per_block = local.shape[0]
    held = jnp.concatenate([local] + [ring_send(local, first, step) for step in range(1, SIDE)])
    held = held.reshape(-1, tile, lanes)
    me = group_of(first, own_a, own_b)
    askers = group_of(first, own_a, (own_b + jnp.arange(SIDE)) % SIDE)

    def owners(wanted, per_owner):
        owner = wanted // per_owner
        owner_a = (owner // SIDE, owner % SIDE)[first == "gz"]
        owner_b = (owner // SIDE, owner % SIDE)[second == "gz"]
        return owner_a, owner_b, wanted % per_owner

    block_a, block_b, block_part = owners(block_wanted, blocks.shape[0])
    adapter_a, adapter_b, adapter_part = owners(adapter_wanted, pieces)
    quarter = jnp.arange(pieces)
    block_table = (
        (((own_a - block_a) % SIDE) * per_block + block_part) * pieces
    )[..., None] + quarter
    adapter_table = (((own_a - adapter_a) % SIDE) * per_block + per_block - 1) * pieces + adapter_part
    table = jnp.concatenate(
        [block_table.reshape(block_table.shape[0], -1), adapter_table], axis=1
    )
    source = jnp.take(table, askers, axis=0, mode="clip")
    width = source.shape[1]
    outgoing = jnp.take(held, source.reshape(-1), axis=0, mode="clip")
    near, far, back = (outgoing[step * width:(step + 1) * width] for step in range(1, SIDE))
    half = width // 2
    ahead = ring_send(jnp.concatenate([near, far[:half]]), second, 1)
    behind = ring_send(jnp.concatenate([back, far[half:]]), second, SIDE - 1)
    relayed = jnp.concatenate(
        [ring_send(ahead[width:], second, 1), ring_send(behind[width:], second, SIDE - 1)]
    )
    received = jnp.concatenate([outgoing[:width], ahead[:width], relayed, behind[:width]])
    slots = block_wanted.shape[1]
    slot = jnp.arange(slots)
    block_pick = (
        (((own_b - block_b[me]) % SIDE) * width + slot * pieces)[:, None] + quarter
    ).reshape(-1)
    adapter_pick = ((own_b - adapter_b[me]) % SIDE) * width + slots * pieces + slot
    chosen_blocks = jnp.take(received, block_pick, axis=0, mode="clip").reshape(
        slots, rows, lanes
    )
    chosen_adapters = jnp.take(received, adapter_pick, axis=0, mode="clip").reshape(slots, -1)
    chosen_adapters = chosen_adapters[:, : flat.shape[1]].reshape(slots, *adapters.shape[1:])
    return chosen_blocks, chosen_adapters


def on_device(
    stream,
    prenorm_gain,
    query_weight,
    key_weight,
    value_weight,
    output_weight,
    adapter_down_rows,
    adapter_up_query,
    request_adapter,
    adapter_row_index,
    request_token_length,
    continues_previous,
    request_cache_block,
    cached_length,
    cached_rotated_keys,
    cached_value_rows,
):
    count = stream.shape[0]
    group_at = lax.axis_index(("gx", "gz"))
    wanted = adapter_row_index[request_adapter]
    down_width = adapter_down_rows.shape[2]
    adapters = jnp.concatenate([adapter_down_rows, adapter_up_query], axis=2)
    cache_keys, chosen = route_with_adapters(
        cached_rotated_keys, adapters, request_cache_block, wanted, "gz", "gx"
    )
    cache_values = route(cached_value_rows, request_cache_block, "gx", "gz")
    chosen_down = chosen[:, :, :down_width]
    chosen_up = chosen[:, :, down_width:]
    model_count = lax.axis_size(("my", "mc"))
    spread = lax.all_to_all(
        jnp.broadcast_to(chosen_down, (model_count, *chosen_down.shape)),
        ("my", "mc"),
        0,
        0,
        tiled=True,
    )
    full_down = jnp.moveaxis(spread, 0, 2).reshape(
        *chosen_down.shape[:2], model_count * down_width
    )

    whole = lax.all_gather(stream, ("my", "mc"), axis=1, tiled=True)
    wide = whole.astype(jnp.float32)
    normalized_input = (
        wide * lax.rsqrt(jnp.mean(wide * wide, axis=1, keepdims=True) + 1e-06) * prenorm_gain
    ).astype(jnp.bfloat16)
    before = jnp.maximum(group_at - 1, 0)
    lengths = request_token_length[group_at]
    cached = cached_length[group_at]
    split_flag = continues_previous[group_at]
    prev_len = request_token_length[before, REQS - 1]
    member, request, position = layout(lengths, cached, split_flag, prev_len, count)
    rank_index = adapter_down_rows.shape[1]
    low = jnp.einsum(
        "td,rkd->trk", normalized_input, full_down, preferred_element_type=jnp.float32
    ).reshape(count, REQS * rank_index).astype(jnp.bfloat16)
    own_columns = jnp.repeat(member, rank_index, axis=1).astype(jnp.bfloat16)
    query_update = jnp.dot(
        low * own_columns,
        chosen_up.reshape(REQS * rank_index, -1),
        preferred_element_type=jnp.float32,
    )
    query_vectors = (
        jnp.dot(normalized_input, query_weight, preferred_element_type=jnp.float32)
        + adapter_scale * query_update
    )
    query_vectors = rotate(query_vectors, position, HEAD_WIDTH).astype(jnp.bfloat16)
    keys = rotate(
        jnp.dot(normalized_input, key_weight, preferred_element_type=jnp.float32),
        position,
        HEAD_WIDTH,
    ).astype(jnp.bfloat16)
    values = jnp.dot(normalized_input, value_weight, preferred_element_type=jnp.float32).astype(
        jnp.bfloat16
    )
    tail = count - MOSTLEN
    prev_both = shifted(jnp.concatenate([keys[tail:], values[tail:]], axis=1), ("gx", "gz"), 1)
    prev_keys, prev_values = prev_both[:, : keys.shape[1]], prev_both[:, keys.shape[1]:]
    attended = attend(
        query_vectors,
        keys,
        values,
        prev_keys,
        prev_values,
        cache_keys,
        cache_values,
        request,
        cached,
        split_flag,
        prev_len,
        HEAD_WIDTH,
    )
    partial_out = jnp.dot(attended, output_weight, preferred_element_type=jnp.float32)
    return lax.psum_scatter(
        partial_out.astype(jnp.bfloat16), ("my", "mc"), scatter_dimension=1, tiled=True
    )


def solution(mesh):
    split = Mesh(mesh.devices.reshape(SIDE, SIDE, 4, 2), ("gx", "gz", "my", "mc"))
    groups = ("gx", "gz")
    model = ("my", "mc")
    placed = (
        P(groups, model),
        P(),
        P(None, model),
        P(None, model),
        P(None, model),
        P(model, None),
        P(groups, None, model),
        P(groups, None, model),
        P(),
        P(),
        P(),
        P(),
        P(),
        P(),
        P(groups, None, model),
        P(groups, None, model),
    )
    return jax.shard_map(
        on_device, mesh=split, in_specs=placed, out_specs=P(groups, model), check_vma=False
    )
```

```python
import jax
import jax.numpy as jnp
from jax import lax
from jax.sharding import Mesh, PartitionSpec as P

HEAD_WIDTH = 256
REQS = 4
MOSTLEN = 256


adapter_scale = 2.0


def shifted(value, axis, steps):
    count = lax.axis_size(axis)
    first, last = (max(0, -steps), min(count, count - steps))
    return lax.ppermute(value, axis, [(source, source + steps) for source in range(first, last)])


def rotate(values, position, head_size):
    count = values.shape[0]
    shaped = values.reshape(count, -1, head_size)
    half = head_size // 2
    freq = 10000.0 ** (-jnp.arange(half, dtype=jnp.float32) / half)
    angle = position[:, None, None] * freq[None, None, :]
    cosine = jnp.cos(angle)
    sine = jnp.sin(angle)
    first = shaped[..., :half]
    second = shaped[..., half:]
    turned = jnp.concatenate(
        [first * cosine - second * sine, second * cosine + first * sine], axis=-1
    )
    return turned.reshape(count, -1)


def layout(lengths, cached, split_flag, prev_len, count):
    ends = jnp.cumsum(lengths)
    starts = ends - lengths
    place = jnp.arange(count, dtype=jnp.int32)
    member = ((place[:, None] >= starts[None, :]) & (place[:, None] < ends[None, :])).astype(
        jnp.int32
    )
    request = jnp.sum(member * jnp.arange(lengths.shape[0], dtype=jnp.int32)[None, :], axis=1)
    offset = place - jnp.sum(member * starts[None, :], axis=1)
    extra = jnp.where(request == 0, split_flag * prev_len, 0)
    position = jnp.sum(member * cached[None, :], axis=1) + extra + offset
    return (member, request, position.astype(jnp.float32))


def attend(
    query_vectors,
    keys,
    values,
    prev_keys,
    prev_values,
    cache_keys,
    cache_values,
    request,
    cached,
    split_flag,
    prev_len,
    head_size,
):
    count = query_vectors.shape[0]
    kv_heads = keys.shape[1] // head_size
    ratio = query_vectors.shape[1] // keys.shape[1]
    block = cache_keys.shape[1]
    slots = cache_keys.shape[0] * block
    every_key = jnp.concatenate([cache_keys.reshape(slots, -1), prev_keys, keys], 0).reshape(
        -1, kv_heads, head_size
    )
    every_value = jnp.concatenate(
        [cache_values.reshape(slots, -1), prev_values, values], 0
    ).reshape(-1, kv_heads, head_size)
    owned = jnp.arange(cache_keys.shape[0], dtype=jnp.int32)
    cache_ok = (
        (request[:, None, None] == owned[None, :, None])
        & (jnp.arange(block, dtype=jnp.int32)[None, None, :] < cached[None, :, None])
    ).reshape(count, slots)
    place = jnp.arange(count, dtype=jnp.int32)
    kept = jnp.arange(prev_keys.shape[0], dtype=jnp.int32)
    prev_ok = (
        (split_flag == 1)
        & (request[:, None] == 0)
        & (kept[None, :] >= prev_keys.shape[0] - prev_len)
    )
    own_ok = (request[:, None] == request[None, :]) & (place[None, :] <= place[:, None])
    allowed = jnp.concatenate([cache_ok, prev_ok, own_ok], 1)
    grouped = query_vectors.reshape(count, kv_heads, ratio, head_size)
    scores = jnp.einsum(
        "tkrd,skd->krts", grouped, every_key, preferred_element_type=jnp.float32
    ) * head_size ** (-0.5)
    scores = jnp.where(allowed[None, None], scores, jnp.float32(-1e30))
    top = jnp.max(scores, axis=-1, keepdims=True)
    weights = jnp.exp(scores - top)
    total = jnp.sum(weights, axis=-1)
    numer = jnp.einsum(
        "krts,skd->tkrd",
        weights.astype(jnp.bfloat16),
        every_value,
        preferred_element_type=jnp.float32,
    )
    result = numer / jnp.transpose(total, (2, 0, 1))[..., None]
    return result.reshape(count, -1).astype(jnp.bfloat16)


SIDE = 4


def group_of(first, a_coord, b_coord):
    return b_coord * SIDE + a_coord if first == "gz" else a_coord * SIDE + b_coord


def ring_send(value, axis, step):
    return lax.ppermute(value, axis, [(i, (i + step) % SIDE) for i in range(SIDE)])


def route(local, wanted, first, second):
    coords = {"gx": lax.axis_index("gx"), "gz": lax.axis_index("gz")}
    own_a, own_b = coords[first], coords[second]
    per_owner = local.shape[0]
    slots = wanted.shape[1]
    spread_out = jnp.broadcast_to(local[None], (SIDE, *local.shape))
    held = lax.all_to_all(spread_out, first, 0, 0, tiled=True).reshape(
        SIDE * per_owner, *local.shape[1:]
    )
    me = group_of(first, own_a, own_b)
    askers = group_of(first, own_a, (own_b + jnp.arange(SIDE)) % SIDE)
    owner = wanted // per_owner
    owner_a = (owner // SIDE, owner % SIDE)[first == "gz"]
    owner_b = (owner // SIDE, owner % SIDE)[second == "gz"]
    table = owner_a * per_owner + wanted % per_owner
    source = jnp.take(table, askers, axis=0, mode="clip")
    outgoing = jnp.take(held, source.reshape(-1), axis=0, mode="clip")
    received = jnp.concatenate(
        [outgoing[:slots]]
        + [
            ring_send(outgoing[step * slots:(step + 1) * slots], second, step)
            for step in range(1, SIDE)
        ]
    )
    pick = ((own_b - owner_b[me]) % SIDE) * slots + jnp.arange(slots)
    return jnp.take(received, pick, axis=0, mode="clip")


def route_with_adapters(blocks, adapters, block_wanted, adapter_wanted, first, second):
    coords = {"gx": lax.axis_index("gx"), "gz": lax.axis_index("gz")}
    own_a, own_b = coords[first], coords[second]
    rows, lanes = blocks.shape[1], blocks.shape[2]
    pieces = adapters.shape[0]
    tile = rows // pieces
    flat = adapters.reshape(pieces, -1)
    padded = jnp.pad(flat, ((0, 0), (0, tile * lanes - flat.shape[1])))
    local = jnp.concatenate([blocks, padded.reshape(1, rows, lanes)])
    per_block = local.shape[0]
    held = jnp.concatenate([local] + [ring_send(local, first, step) for step in range(1, SIDE)])
    held = held.reshape(-1, tile, lanes)
    me = group_of(first, own_a, own_b)
    askers = group_of(first, own_a, (own_b + jnp.arange(SIDE)) % SIDE)

    def owners(wanted, per_owner):
        owner = wanted // per_owner
        owner_a = (owner // SIDE, owner % SIDE)[first == "gz"]
        owner_b = (owner // SIDE, owner % SIDE)[second == "gz"]
        return owner_a, owner_b, wanted % per_owner

    block_a, block_b, block_part = owners(block_wanted, blocks.shape[0])
    adapter_a, adapter_b, adapter_part = owners(adapter_wanted, pieces)
    quarter = jnp.arange(pieces)
    block_table = (
        (((own_a - block_a) % SIDE) * per_block + block_part) * pieces
    )[..., None] + quarter
    adapter_table = (((own_a - adapter_a) % SIDE) * per_block + per_block - 1) * pieces + adapter_part
    table = jnp.concatenate(
        [block_table.reshape(block_table.shape[0], -1), adapter_table], axis=1
    )
    source = jnp.take(table, askers, axis=0, mode="clip")
    width = source.shape[1]
    outgoing = jnp.take(held, source.reshape(-1), axis=0, mode="clip")
    lead = slots_items = block_wanted.shape[1] * pieces
    adapter_parts = [outgoing[lead:width]] + [
        ring_send(outgoing[step * width + lead:(step + 1) * width], second, step)
        for step in range(1, SIDE)
    ]
    block_parts = [outgoing[:lead]] + [
        ring_send(outgoing[step * width:step * width + lead], second, step)
        for step in range(1, SIDE)
    ]
    adapter_received = jnp.concatenate(adapter_parts)
    received = jnp.concatenate(block_parts)
    slots = block_wanted.shape[1]
    slot = jnp.arange(slots)
    block_pick = (
        (((own_b - block_b[me]) % SIDE) * slots_items + slot * pieces)[:, None] + quarter
    ).reshape(-1)
    adapter_pick = ((own_b - adapter_b[me]) % SIDE) * slots + slot
    chosen_blocks = jnp.take(received, block_pick, axis=0, mode="clip").reshape(
        slots, rows, lanes
    )
    chosen_adapters = jnp.take(adapter_received, adapter_pick, axis=0, mode="clip").reshape(
        slots, -1
    )
    chosen_adapters = chosen_adapters[:, : flat.shape[1]].reshape(slots, *adapters.shape[1:])
    return chosen_blocks, chosen_adapters


def on_device(
    stream,
    prenorm_gain,
    query_weight,
    key_weight,
    value_weight,
    output_weight,
    adapter_down_rows,
    adapter_up_query,
    request_adapter,
    adapter_row_index,
    request_token_length,
    continues_previous,
    request_cache_block,
    cached_length,
    cached_rotated_keys,
    cached_value_rows,
):
    count = stream.shape[0]
    group_at = lax.axis_index(("gx", "gz"))
    wanted = adapter_row_index[request_adapter]
    down_width = adapter_down_rows.shape[2]
    adapters = jnp.concatenate([adapter_down_rows, adapter_up_query], axis=2)
    cache_keys, chosen = route_with_adapters(
        cached_rotated_keys, adapters, request_cache_block, wanted, "gz", "gx"
    )
    cache_values = route(cached_value_rows, request_cache_block, "gx", "gz")
    chosen_down = chosen[:, :, :down_width]
    chosen_up = chosen[:, :, down_width:]
    model_count = lax.axis_size(("my", "mc"))
    spread = lax.all_to_all(
        jnp.broadcast_to(chosen_down, (model_count, *chosen_down.shape)),
        ("my", "mc"),
        0,
        0,
        tiled=True,
    )
    full_down = jnp.moveaxis(spread, 0, 2).reshape(
        *chosen_down.shape[:2], model_count * down_width
    )

    whole = lax.all_gather(stream, ("my", "mc"), axis=1, tiled=True)
    wide = whole.astype(jnp.float32)
    normalized_input = (
        wide * lax.rsqrt(jnp.mean(wide * wide, axis=1, keepdims=True) + 1e-06) * prenorm_gain
    ).astype(jnp.bfloat16)
    before = jnp.maximum(group_at - 1, 0)
    lengths = request_token_length[group_at]
    cached = cached_length[group_at]
    split_flag = continues_previous[group_at]
    prev_len = request_token_length[before, REQS - 1]
    member, request, position = layout(lengths, cached, split_flag, prev_len, count)
    rank_index = adapter_down_rows.shape[1]
    low = jnp.einsum(
        "td,rkd->trk", normalized_input, full_down, preferred_element_type=jnp.float32
    ).reshape(count, REQS * rank_index).astype(jnp.bfloat16)
    own_columns = jnp.repeat(member, rank_index, axis=1).astype(jnp.bfloat16)
    query_update = jnp.dot(
        low * own_columns,
        chosen_up.reshape(REQS * rank_index, -1),
        preferred_element_type=jnp.float32,
    )
    query_vectors = (
        jnp.dot(normalized_input, query_weight, preferred_element_type=jnp.float32)
        + adapter_scale * query_update
    )
    query_vectors = rotate(query_vectors, position, HEAD_WIDTH).astype(jnp.bfloat16)
    keys = rotate(
        jnp.dot(normalized_input, key_weight, preferred_element_type=jnp.float32),
        position,
        HEAD_WIDTH,
    ).astype(jnp.bfloat16)
    values = jnp.dot(normalized_input, value_weight, preferred_element_type=jnp.float32).astype(
        jnp.bfloat16
    )
    tail = count - MOSTLEN
    prev_both = shifted(jnp.concatenate([keys[tail:], values[tail:]], axis=1), ("gx", "gz"), 1)
    prev_keys, prev_values = prev_both[:, : keys.shape[1]], prev_both[:, keys.shape[1]:]
    attended = attend(
        query_vectors,
        keys,
        values,
        prev_keys,
        prev_values,
        cache_keys,
        cache_values,
        request,
        cached,
        split_flag,
        prev_len,
        HEAD_WIDTH,
    )
    partial_out = jnp.dot(attended, output_weight, preferred_element_type=jnp.float32)
    return lax.psum_scatter(
        partial_out.astype(jnp.bfloat16), ("my", "mc"), scatter_dimension=1, tiled=True
    )


def solution(mesh):
    split = Mesh(mesh.devices.reshape(SIDE, SIDE, 4, 2), ("gx", "gz", "my", "mc"))
    groups = ("gx", "gz")
    model = ("my", "mc")
    placed = (
        P(groups, model),
        P(),
        P(None, model),
        P(None, model),
        P(None, model),
        P(model, None),
        P(groups, None, model),
        P(groups, None, model),
        P(),
        P(),
        P(),
        P(),
        P(),
        P(),
        P(groups, None, model),
        P(groups, None, model),
    )
    return jax.shard_map(
        on_device, mesh=split, in_specs=placed, out_specs=P(groups, model), check_vma=False
    )
```

```python
import jax
import jax.numpy as jnp
from jax import lax
from jax.sharding import Mesh, PartitionSpec as P

HEAD_WIDTH = 256
REQS = 4
MOSTLEN = 256


adapter_scale = 2.0


def shifted(value, axis, steps):
    count = lax.axis_size(axis)
    first, last = (max(0, -steps), min(count, count - steps))
    return lax.ppermute(value, axis, [(source, source + steps) for source in range(first, last)])


def rotate(values, position, head_size):
    count = values.shape[0]
    shaped = values.reshape(count, -1, head_size)
    half = head_size // 2
    freq = 10000.0 ** (-jnp.arange(half, dtype=jnp.float32) / half)
    angle = position[:, None, None] * freq[None, None, :]
    cosine = jnp.cos(angle)
    sine = jnp.sin(angle)
    first = shaped[..., :half]
    second = shaped[..., half:]
    turned = jnp.concatenate(
        [first * cosine - second * sine, second * cosine + first * sine], axis=-1
    )
    return turned.reshape(count, -1)


def layout(lengths, cached, split_flag, prev_len, count):
    ends = jnp.cumsum(lengths)
    starts = ends - lengths
    place = jnp.arange(count, dtype=jnp.int32)
    member = ((place[:, None] >= starts[None, :]) & (place[:, None] < ends[None, :])).astype(
        jnp.int32
    )
    request = jnp.sum(member * jnp.arange(lengths.shape[0], dtype=jnp.int32)[None, :], axis=1)
    offset = place - jnp.sum(member * starts[None, :], axis=1)
    extra = jnp.where(request == 0, split_flag * prev_len, 0)
    position = jnp.sum(member * cached[None, :], axis=1) + extra + offset
    return (member, request, position.astype(jnp.float32))


def attend(
    query_vectors,
    keys,
    values,
    prev_keys,
    prev_values,
    cache_keys,
    cache_values,
    request,
    cached,
    split_flag,
    prev_len,
    head_size,
):
    count = query_vectors.shape[0]
    kv_heads = keys.shape[1] // head_size
    ratio = query_vectors.shape[1] // keys.shape[1]
    block = cache_keys.shape[1]
    slots = cache_keys.shape[0] * block
    every_key = jnp.concatenate([cache_keys.reshape(slots, -1), prev_keys, keys], 0).reshape(
        -1, kv_heads, head_size
    )
    every_value = jnp.concatenate(
        [cache_values.reshape(slots, -1), prev_values, values], 0
    ).reshape(-1, kv_heads, head_size)
    owned = jnp.arange(cache_keys.shape[0], dtype=jnp.int32)
    cache_ok = (
        (request[:, None, None] == owned[None, :, None])
        & (jnp.arange(block, dtype=jnp.int32)[None, None, :] < cached[None, :, None])
    ).reshape(count, slots)
    place = jnp.arange(count, dtype=jnp.int32)
    kept = jnp.arange(prev_keys.shape[0], dtype=jnp.int32)
    prev_ok = (
        (split_flag == 1)
        & (request[:, None] == 0)
        & (kept[None, :] >= prev_keys.shape[0] - prev_len)
    )
    own_ok = (request[:, None] == request[None, :]) & (place[None, :] <= place[:, None])
    allowed = jnp.concatenate([cache_ok, prev_ok, own_ok], 1)
    grouped = query_vectors.reshape(count, kv_heads, ratio, head_size)
    scores = jnp.einsum(
        "tkrd,skd->krts", grouped, every_key, preferred_element_type=jnp.float32
    ) * head_size ** (-0.5)
    scores = jnp.where(allowed[None, None], scores, jnp.float32(-1e30))
    top = jnp.max(scores, axis=-1, keepdims=True)
    weights = jnp.exp(scores - top)
    total = jnp.sum(weights, axis=-1)
    numer = jnp.einsum(
        "krts,skd->tkrd",
        weights.astype(jnp.bfloat16),
        every_value,
        preferred_element_type=jnp.float32,
    )
    result = numer / jnp.transpose(total, (2, 0, 1))[..., None]
    return result.reshape(count, -1).astype(jnp.bfloat16)


SIDE = 4


def group_of(first, a_coord, b_coord):
    return b_coord * SIDE + a_coord if first == "gz" else a_coord * SIDE + b_coord


def ring_send(value, axis, step):
    return lax.ppermute(value, axis, [(i, (i + step) % SIDE) for i in range(SIDE)])


def route(local, wanted, first, second):
    coords = {"gx": lax.axis_index("gx"), "gz": lax.axis_index("gz")}
    own_a, own_b = coords[first], coords[second]
    per_owner = local.shape[0]
    slots = wanted.shape[1]
    spread_out = jnp.broadcast_to(local[None], (SIDE, *local.shape))
    held = lax.all_to_all(spread_out, first, 0, 0, tiled=True).reshape(
        SIDE * per_owner, *local.shape[1:]
    )
    me = group_of(first, own_a, own_b)
    askers = group_of(first, own_a, (own_b + jnp.arange(SIDE)) % SIDE)
    owner = wanted // per_owner
    owner_a = (owner // SIDE, owner % SIDE)[first == "gz"]
    owner_b = (owner // SIDE, owner % SIDE)[second == "gz"]
    table = owner_a * per_owner + wanted % per_owner
    source = jnp.take(table, askers, axis=0, mode="clip")
    outgoing = jnp.take(held, source.reshape(-1), axis=0, mode="clip")
    received = jnp.concatenate(
        [outgoing[:slots]]
        + [
            ring_send(outgoing[step * slots:(step + 1) * slots], second, step)
            for step in range(1, SIDE)
        ]
    )
    pick = ((own_b - owner_b[me]) % SIDE) * slots + jnp.arange(slots)
    return jnp.take(received, pick, axis=0, mode="clip")


def route_with_adapters(blocks, adapters, block_wanted, adapter_wanted, first, second):
    coords = {"gx": lax.axis_index("gx"), "gz": lax.axis_index("gz")}
    own_a, own_b = coords[first], coords[second]
    rows, lanes = blocks.shape[1], blocks.shape[2]
    pieces = adapters.shape[0]
    tile = rows // pieces
    flat = adapters.reshape(pieces, -1)
    padded = jnp.pad(flat, ((0, 0), (0, tile * lanes - flat.shape[1])))
    local = jnp.concatenate([blocks, padded.reshape(1, rows, lanes)])
    per_block = local.shape[0]
    held = jnp.concatenate([local] + [ring_send(local, first, step) for step in range(1, SIDE)])
    held = held.reshape(-1, tile, lanes)
    me = group_of(first, own_a, own_b)
    askers = group_of(first, own_a, (own_b + jnp.arange(SIDE)) % SIDE)

    def owners(wanted, per_owner):
        owner = wanted // per_owner
        owner_a = (owner // SIDE, owner % SIDE)[first == "gz"]
        owner_b = (owner // SIDE, owner % SIDE)[second == "gz"]
        return owner_a, owner_b, wanted % per_owner

    block_a, block_b, block_part = owners(block_wanted, blocks.shape[0])
    adapter_a, adapter_b, adapter_part = owners(adapter_wanted, pieces)
    quarter = jnp.arange(pieces)
    block_table = (
        (((own_a - block_a) % SIDE) * per_block + block_part) * pieces
    )[..., None] + quarter
    adapter_table = (((own_a - adapter_a) % SIDE) * per_block + per_block - 1) * pieces + adapter_part
    table = jnp.concatenate(
        [block_table.reshape(block_table.shape[0], -1), adapter_table], axis=1
    )
    source = jnp.take(table, askers, axis=0, mode="clip")
    width = source.shape[1]
    outgoing = jnp.take(held, source.reshape(-1), axis=0, mode="clip")
    received = jnp.concatenate(
        [outgoing[:width]]
        + [
            ring_send(outgoing[step * width:(step + 1) * width], second, step)
            for step in range(1, SIDE)
        ]
    )
    slots = block_wanted.shape[1]
    slot = jnp.arange(slots)
    block_pick = (
        (((own_b - block_b[me]) % SIDE) * width + slot * pieces)[:, None] + quarter
    ).reshape(-1)
    adapter_pick = ((own_b - adapter_b[me]) % SIDE) * width + slots * pieces + slot
    chosen_blocks = jnp.take(received, block_pick, axis=0, mode="clip").reshape(
        slots, rows, lanes
    )
    chosen_adapters = jnp.take(received, adapter_pick, axis=0, mode="clip").reshape(slots, -1)
    chosen_adapters = chosen_adapters[:, : flat.shape[1]].reshape(slots, *adapters.shape[1:])
    return chosen_blocks, chosen_adapters


def on_device(
    stream,
    prenorm_gain,
    query_weight,
    key_weight,
    value_weight,
    output_weight,
    adapter_down_rows,
    adapter_up_query,
    request_adapter,
    adapter_row_index,
    request_token_length,
    continues_previous,
    request_cache_block,
    cached_length,
    cached_rotated_keys,
    cached_value_rows,
):
    count = stream.shape[0]
    group_at = lax.axis_index(("gx", "gz"))
    wanted = adapter_row_index[request_adapter]
    down_width = adapter_down_rows.shape[2]
    adapters = jnp.concatenate([adapter_down_rows, adapter_up_query], axis=2)
    cache_keys, chosen = route_with_adapters(
        cached_rotated_keys, adapters, request_cache_block, wanted, "gz", "gx"
    )
    cache_values = route(cached_value_rows, request_cache_block, "gx", "gz")
    chosen_down = chosen[:, :, :down_width]
    chosen_up = chosen[:, :, down_width:]
    model_count = lax.axis_size(("my", "mc"))
    spread = lax.all_to_all(
        jnp.broadcast_to(chosen_down, (model_count, *chosen_down.shape)),
        ("my", "mc"),
        0,
        0,
        tiled=True,
    )
    full_down = jnp.moveaxis(spread, 0, 2).reshape(
        *chosen_down.shape[:2], model_count * down_width
    )

    whole = lax.all_gather(stream, ("my", "mc"), axis=1, tiled=True)
    wide = whole.astype(jnp.float32)
    lanes = 128
    partial_squares = jnp.sum(
        (wide * wide).reshape(count, wide.shape[1] // lanes, lanes), axis=2
    )
    partial_squares = lax.optimization_barrier(partial_squares)
    mean_square = jnp.sum(partial_squares, axis=1, keepdims=True) / wide.shape[1]
    normalized_input = (wide * lax.rsqrt(mean_square + 1e-06) * prenorm_gain).astype(jnp.bfloat16)
    before = jnp.maximum(group_at - 1, 0)
    lengths = request_token_length[group_at]
    cached = cached_length[group_at]
    split_flag = continues_previous[group_at]
    prev_len = request_token_length[before, REQS - 1]
    member, request, position = layout(lengths, cached, split_flag, prev_len, count)
    rank_index = adapter_down_rows.shape[1]
    low = jnp.einsum(
        "td,rkd->trk", normalized_input, full_down, preferred_element_type=jnp.float32
    ).reshape(count, REQS * rank_index).astype(jnp.bfloat16)
    own_columns = jnp.repeat(member, rank_index, axis=1).astype(jnp.bfloat16)
    query_update = jnp.dot(
        low * own_columns,
        chosen_up.reshape(REQS * rank_index, -1),
        preferred_element_type=jnp.float32,
    )
    query_vectors = (
        jnp.dot(normalized_input, query_weight, preferred_element_type=jnp.float32)
        + adapter_scale * query_update
    )
    query_vectors = rotate(query_vectors, position, HEAD_WIDTH).astype(jnp.bfloat16)
    keys = rotate(
        jnp.dot(normalized_input, key_weight, preferred_element_type=jnp.float32),
        position,
        HEAD_WIDTH,
    ).astype(jnp.bfloat16)
    values = jnp.dot(normalized_input, value_weight, preferred_element_type=jnp.float32).astype(
        jnp.bfloat16
    )
    tail = count - MOSTLEN
    prev_both = shifted(jnp.concatenate([keys[tail:], values[tail:]], axis=1), ("gx", "gz"), 1)
    prev_keys, prev_values = prev_both[:, : keys.shape[1]], prev_both[:, keys.shape[1]:]
    attended = attend(
        query_vectors,
        keys,
        values,
        prev_keys,
        prev_values,
        cache_keys,
        cache_values,
        request,
        cached,
        split_flag,
        prev_len,
        HEAD_WIDTH,
    )
    partial_out = jnp.dot(attended, output_weight, preferred_element_type=jnp.float32)
    return lax.psum_scatter(
        partial_out.astype(jnp.bfloat16), ("my", "mc"), scatter_dimension=1, tiled=True
    )


def solution(mesh):
    split = Mesh(mesh.devices.reshape(SIDE, SIDE, 4, 2), ("gx", "gz", "my", "mc"))
    groups = ("gx", "gz")
    model = ("my", "mc")
    placed = (
        P(groups, model),
        P(),
        P(None, model),
        P(None, model),
        P(None, model),
        P(model, None),
        P(groups, None, model),
        P(groups, None, model),
        P(),
        P(),
        P(),
        P(),
        P(),
        P(),
        P(groups, None, model),
        P(groups, None, model),
    )
    return jax.shard_map(
        on_device, mesh=split, in_specs=placed, out_specs=P(groups, model), check_vma=False
    )
```

```python
import jax
import jax.numpy as jnp
from jax import lax
from jax.sharding import Mesh, PartitionSpec as P

HEAD_WIDTH = 256
REQS = 4
MOSTLEN = 256


adapter_scale = 2.0


def shifted(value, axis, steps):
    count = lax.axis_size(axis)
    first, last = (max(0, -steps), min(count, count - steps))
    return lax.ppermute(value, axis, [(source, source + steps) for source in range(first, last)])


def rotate(values, position, head_size):
    count = values.shape[0]
    shaped = values.reshape(count, -1, head_size)
    half = head_size // 2
    freq = 10000.0 ** (-jnp.arange(half, dtype=jnp.float32) / half)
    angle = position[:, None, None] * freq[None, None, :]
    cosine = jnp.cos(angle)
    sine = jnp.sin(angle)
    first = shaped[..., :half]
    second = shaped[..., half:]
    turned = jnp.concatenate(
        [first * cosine - second * sine, second * cosine + first * sine], axis=-1
    )
    return turned.reshape(count, -1)


def layout(lengths, cached, split_flag, prev_len, count):
    ends = jnp.cumsum(lengths)
    starts = ends - lengths
    place = jnp.arange(count, dtype=jnp.int32)
    member = ((place[:, None] >= starts[None, :]) & (place[:, None] < ends[None, :])).astype(
        jnp.int32
    )
    request = jnp.sum(member * jnp.arange(lengths.shape[0], dtype=jnp.int32)[None, :], axis=1)
    offset = place - jnp.sum(member * starts[None, :], axis=1)
    extra = jnp.where(request == 0, split_flag * prev_len, 0)
    position = jnp.sum(member * cached[None, :], axis=1) + extra + offset
    return (member, request, position.astype(jnp.float32))


def attend(
    query_vectors,
    keys,
    values,
    prev_keys,
    prev_values,
    cache_keys,
    cache_values,
    request,
    cached,
    split_flag,
    prev_len,
    head_size,
):
    count = query_vectors.shape[0]
    kv_heads = keys.shape[1] // head_size
    ratio = query_vectors.shape[1] // keys.shape[1]
    block = cache_keys.shape[1]
    slots = cache_keys.shape[0] * block
    every_key = jnp.concatenate([cache_keys.reshape(slots, -1), prev_keys, keys], 0).reshape(
        -1, kv_heads, head_size
    )
    every_value = jnp.concatenate(
        [cache_values.reshape(slots, -1), prev_values, values], 0
    ).reshape(-1, kv_heads, head_size)
    owned = jnp.arange(cache_keys.shape[0], dtype=jnp.int32)
    cache_ok = (
        (request[:, None, None] == owned[None, :, None])
        & (jnp.arange(block, dtype=jnp.int32)[None, None, :] < cached[None, :, None])
    ).reshape(count, slots)
    place = jnp.arange(count, dtype=jnp.int32)
    kept = jnp.arange(prev_keys.shape[0], dtype=jnp.int32)
    prev_ok = (
        (split_flag == 1)
        & (request[:, None] == 0)
        & (kept[None, :] >= prev_keys.shape[0] - prev_len)
    )
    own_ok = (request[:, None] == request[None, :]) & (place[None, :] <= place[:, None])
    allowed = jnp.concatenate([cache_ok, prev_ok, own_ok], 1)
    grouped = query_vectors.reshape(count, kv_heads, ratio, head_size)
    scores = jnp.einsum(
        "tkrd,skd->krts", grouped, every_key, preferred_element_type=jnp.float32
    ) * head_size ** (-0.5)
    scores = jnp.where(allowed[None, None], scores, jnp.float32(-1e30))
    top = jnp.max(scores, axis=-1, keepdims=True)
    weights = jnp.exp(scores - top)
    total = jnp.sum(weights, axis=-1)
    numer = jnp.einsum(
        "krts,skd->tkrd",
        weights.astype(jnp.bfloat16),
        every_value,
        preferred_element_type=jnp.float32,
    )
    result = numer / jnp.transpose(total, (2, 0, 1))[..., None]
    return result.reshape(count, -1).astype(jnp.bfloat16)


SIDE = 4


def group_of(first, a_coord, b_coord):
    return b_coord * SIDE + a_coord if first == "gz" else a_coord * SIDE + b_coord


def ring_send(value, axis, step):
    return lax.ppermute(value, axis, [(i, (i + step) % SIDE) for i in range(SIDE)])


def route(local, wanted, first, second):
    coords = {"gx": lax.axis_index("gx"), "gz": lax.axis_index("gz")}
    own_a, own_b = coords[first], coords[second]
    per_owner = local.shape[0]
    slots = wanted.shape[1]
    spread_out = jnp.broadcast_to(local[None], (SIDE, *local.shape))
    held = lax.all_to_all(spread_out, first, 0, 0, tiled=True).reshape(
        SIDE * per_owner, *local.shape[1:]
    )
    me = group_of(first, own_a, own_b)
    askers = group_of(first, own_a, (own_b + jnp.arange(SIDE)) % SIDE)
    owner = wanted // per_owner
    owner_a = (owner // SIDE, owner % SIDE)[first == "gz"]
    owner_b = (owner // SIDE, owner % SIDE)[second == "gz"]
    table = owner_a * per_owner + wanted % per_owner
    source = table.at[askers].get(mode="promise_in_bounds")
    outgoing = held.at[source.reshape(-1)].get(mode="promise_in_bounds")
    received = jnp.concatenate(
        [outgoing[:slots]]
        + [
            ring_send(outgoing[step * slots:(step + 1) * slots], second, step)
            for step in range(1, SIDE)
        ]
    )
    pick = ((own_b - owner_b[me]) % SIDE) * slots + jnp.arange(slots)
    return received.at[pick].get(mode="promise_in_bounds")


def route_with_adapters(blocks, adapters, block_wanted, adapter_wanted, first, second):
    coords = {"gx": lax.axis_index("gx"), "gz": lax.axis_index("gz")}
    own_a, own_b = coords[first], coords[second]
    rows, lanes = blocks.shape[1], blocks.shape[2]
    pieces = adapters.shape[0]
    tile = rows // pieces
    flat = adapters.reshape(pieces, -1)
    padded = jnp.pad(flat, ((0, 0), (0, tile * lanes - flat.shape[1])))
    local = jnp.concatenate([blocks, padded.reshape(1, rows, lanes)])
    per_block = local.shape[0]
    held = jnp.concatenate([local] + [ring_send(local, first, step) for step in range(1, SIDE)])
    held = held.reshape(-1, tile, lanes)
    me = group_of(first, own_a, own_b)
    askers = group_of(first, own_a, (own_b + jnp.arange(SIDE)) % SIDE)

    def owners(wanted, per_owner):
        owner = wanted // per_owner
        owner_a = (owner // SIDE, owner % SIDE)[first == "gz"]
        owner_b = (owner // SIDE, owner % SIDE)[second == "gz"]
        return owner_a, owner_b, wanted % per_owner

    block_a, block_b, block_part = owners(block_wanted, blocks.shape[0])
    adapter_a, adapter_b, adapter_part = owners(adapter_wanted, pieces)
    quarter = jnp.arange(pieces)
    block_table = (
        (((own_a - block_a) % SIDE) * per_block + block_part) * pieces
    )[..., None] + quarter
    adapter_table = (((own_a - adapter_a) % SIDE) * per_block + per_block - 1) * pieces + adapter_part
    table = jnp.concatenate(
        [block_table.reshape(block_table.shape[0], -1), adapter_table], axis=1
    )
    source = table.at[askers].get(mode="promise_in_bounds")
    width = source.shape[1]
    outgoing = held.at[source.reshape(-1)].get(mode="promise_in_bounds")
    received = jnp.concatenate(
        [outgoing[:width]]
        + [
            ring_send(outgoing[step * width:(step + 1) * width], second, step)
            for step in range(1, SIDE)
        ]
    )
    slots = block_wanted.shape[1]
    slot = jnp.arange(slots)
    block_pick = (
        (((own_b - block_b[me]) % SIDE) * width + slot * pieces)[:, None] + quarter
    ).reshape(-1)
    adapter_pick = ((own_b - adapter_b[me]) % SIDE) * width + slots * pieces + slot
    chosen_blocks = received.at[block_pick].get(mode="promise_in_bounds").reshape(
        slots, rows, lanes
    )
    chosen_adapters = received.at[adapter_pick].get(mode="promise_in_bounds").reshape(slots, -1)
    chosen_adapters = chosen_adapters[:, : flat.shape[1]].reshape(slots, *adapters.shape[1:])
    return chosen_blocks, chosen_adapters


def on_device(
    stream,
    prenorm_gain,
    query_weight,
    key_weight,
    value_weight,
    output_weight,
    adapter_down_rows,
    adapter_up_query,
    request_adapter,
    adapter_row_index,
    request_token_length,
    continues_previous,
    request_cache_block,
    cached_length,
    cached_rotated_keys,
    cached_value_rows,
):
    count = stream.shape[0]
    group_at = lax.axis_index(("gx", "gz"))
    wanted = adapter_row_index[request_adapter]
    down_width = adapter_down_rows.shape[2]
    adapters = jnp.concatenate([adapter_down_rows, adapter_up_query], axis=2)
    cache_keys, chosen = route_with_adapters(
        cached_rotated_keys, adapters, request_cache_block, wanted, "gz", "gx"
    )
    cache_values = route(cached_value_rows, request_cache_block, "gx", "gz")
    chosen_down = chosen[:, :, :down_width]
    chosen_up = chosen[:, :, down_width:]
    model_count = lax.axis_size(("my", "mc"))
    spread = lax.all_to_all(
        jnp.broadcast_to(chosen_down, (model_count, *chosen_down.shape)),
        ("my", "mc"),
        0,
        0,
        tiled=True,
    )
    full_down = jnp.moveaxis(spread, 0, 2).reshape(
        *chosen_down.shape[:2], model_count * down_width
    )

    whole = lax.all_gather(stream, ("my", "mc"), axis=1, tiled=True)
    wide = whole.astype(jnp.float32)
    normalized_input = (
        wide * lax.rsqrt(jnp.mean(wide * wide, axis=1, keepdims=True) + 1e-06) * prenorm_gain
    ).astype(jnp.bfloat16)
    before = jnp.maximum(group_at - 1, 0)
    lengths = request_token_length[group_at]
    cached = cached_length[group_at]
    split_flag = continues_previous[group_at]
    prev_len = request_token_length[before, REQS - 1]
    member, request, position = layout(lengths, cached, split_flag, prev_len, count)
    rank_index = adapter_down_rows.shape[1]
    low = jnp.einsum(
        "td,rkd->trk", normalized_input, full_down, preferred_element_type=jnp.float32
    ).reshape(count, REQS * rank_index).astype(jnp.bfloat16)
    own_columns = jnp.repeat(member, rank_index, axis=1).astype(jnp.bfloat16)
    query_update = jnp.dot(
        low * own_columns,
        chosen_up.reshape(REQS * rank_index, -1),
        preferred_element_type=jnp.float32,
    )
    query_vectors = (
        jnp.dot(normalized_input, query_weight, preferred_element_type=jnp.float32)
        + adapter_scale * query_update
    )
    query_vectors = rotate(query_vectors, position, HEAD_WIDTH).astype(jnp.bfloat16)
    keys = rotate(
        jnp.dot(normalized_input, key_weight, preferred_element_type=jnp.float32),
        position,
        HEAD_WIDTH,
    ).astype(jnp.bfloat16)
    values = jnp.dot(normalized_input, value_weight, preferred_element_type=jnp.float32).astype(
        jnp.bfloat16
    )
    tail = count - MOSTLEN
    prev_both = shifted(jnp.concatenate([keys[tail:], values[tail:]], axis=1), ("gx", "gz"), 1)
    prev_keys, prev_values = prev_both[:, : keys.shape[1]], prev_both[:, keys.shape[1]:]
    attended = attend(
        query_vectors,
        keys,
        values,
        prev_keys,
        prev_values,
        cache_keys,
        cache_values,
        request,
        cached,
        split_flag,
        prev_len,
        HEAD_WIDTH,
    )
    partial_out = jnp.dot(attended, output_weight, preferred_element_type=jnp.float32)
    return lax.psum_scatter(
        partial_out.astype(jnp.bfloat16), ("my", "mc"), scatter_dimension=1, tiled=True
    )


def solution(mesh):
    split = Mesh(mesh.devices.reshape(SIDE, SIDE, 4, 2), ("gx", "gz", "my", "mc"))
    groups = ("gx", "gz")
    model = ("my", "mc")
    placed = (
        P(groups, model),
        P(),
        P(None, model),
        P(None, model),
        P(None, model),
        P(model, None),
        P(groups, None, model),
        P(groups, None, model),
        P(),
        P(),
        P(),
        P(),
        P(),
        P(),
        P(groups, None, model),
        P(groups, None, model),
    )
    return jax.shard_map(
        on_device, mesh=split, in_specs=placed, out_specs=P(groups, model), check_vma=False
    )
```
